32 devices in a mesh: seq: 16 (over z, y, core), heads: 2 (over x).
Axes of the slice: x: 2, y: 2, z: 4, core: 2. Of those that a mesh axis runs over, the one named last changes fastest.
Arguments:
- residual_in: bfloat16 [2048, 3072], P('seq', 'heads'), may hold values from -24 to 24
- self_queries: bfloat16 [2048, 3072], P('seq', 'heads'), may hold values from -170 to 170
- self_keys_values: bfloat16 [2048, 2048], P('seq', 'heads'), may hold values from -5 to 5
- self_out_weight: bfloat16 [3072, 3072], P('seq', 'heads'), may hold values from -0.109375 to 0.109375
- gain_query: float32 [3072], replicated, may hold values from 0.1 to 1.9
- gain_keyvalue: float32 [3072], replicated, may hold values from 0.1 to 1.9
- cross_weight: bfloat16 [3072, 5120], P(None, 'heads')
Outputs:
- hidden: bfloat16 [2048, 3072], P('seq', 'heads')
- cross_attention: bfloat16 [2048, 3072], P('seq', 'heads')
The draws below stay inside these ranges and needn't reach their ends.
All inputs are finite; a program needn't handle non-finite values.
Results may differ from the reference program's by a relative error of at most 0.02.
Values may be sent and summed in bfloat16 or wider, within the bound.
No kernel may reach another device: no remote copies, remote signals or barrier semaphores. Data moves between devices by JAX's collectives and lax.ppermute only.
A program may use at most 128 MiB of HBM per device.

```python
import math
import jax
import jax.numpy as jnp
from jax import lax

D = 3072
HD = 128
KVH = 8
QPK = 3
WINDOW = 2048
TOK_DEV = 128
TOKENS = 2048
QH = 24


def self_key_table(key):
    table = jnp.clip(jax.random.normal(jax.random.fold_in(key, 11), (TOKENS, KVH, HD), jnp.float32), -4.0, 4.0)
    return table


def draw_self_keys_values(key, part):
    keys_part = self_key_table(key)
    values_part = jnp.clip(jax.random.normal(jax.random.fold_in(key, 13), (TOKENS, KVH, HD), jnp.float32), -4.0, 4.0)
    stacked = jnp.stack([keys_part, values_part], axis=2)
    return stacked.reshape(TOKENS, KVH * 2 * HD).astype(jnp.bfloat16)


def draw_self_queries(key, part):
    base = jnp.clip(jax.random.normal(jax.random.fold_in(key, 21), (TOKENS, KVH, QPK, HD), jnp.float32), -4.0, 4.0)
    return base.reshape(TOKENS, KVH * QPK * HD).astype(jnp.bfloat16)


def draw_residual_in(key, part):
    values = jnp.clip(jax.random.normal(jax.random.fold_in(key, 31), (TOKENS, D), jnp.float32), -4.0, 4.0)
    row_scale = jnp.exp(jax.random.uniform(jax.random.fold_in(key, 32), (TOKENS,), jnp.float32, math.log(0.3), math.log(3.0)))
    col_scale = jnp.exp(jax.random.uniform(jax.random.fold_in(key, 33), (D,), jnp.float32, math.log(0.5), math.log(2.0)))
    return (values * row_scale[:, None] * col_scale[None, :]).astype(jnp.bfloat16)


def draw_cross_weight(key, part):
    base = jnp.clip(jax.random.normal(jax.random.fold_in(key, 41), (D, KVH, QPK + 2, HD), jnp.float32), -4.0, 4.0)
    return (base / math.sqrt(D)).reshape(D, KVH * (QPK + 2) * HD).astype(jnp.bfloat16)


def block_scale(key, dims, cuts, least, largest):
    level = 1.0
    for position, blocks in cuts:
        heights = jax.random.uniform(jax.random.fold_in(jax.random.fold_in(key, 6), position), (blocks,), jnp.float32, least / len(cuts), largest / len(cuts))
        level = level * jnp.repeat(jnp.exp(heights), dims[position] // blocks).reshape((-1,) + (1,) * (len(dims) - 1 - position))
    return level


def scatter_about(stream_key, dims, width, limit, split=(), held_as=jnp.bfloat16):
    entries = jax.random.normal(stream_key, dims, jnp.float32) * width
    if len(split) > 0:
        entries = block_scale(stream_key, dims, split, -0.22, 0.18) * entries
    return jnp.clip(entries, min=-limit, max=limit).astype(held_as)


def setup_inputs(seed: int = 0) -> dict:
    key_list = jax.random.split(jax.random.key(seed), 8)
    residual_in = draw_residual_in(jax.random.fold_in(key_list[7], 71), 0)
    self_queries = draw_self_queries(jax.random.fold_in(key_list[7], 71), 0)
    self_keys_values = draw_self_keys_values(jax.random.fold_in(key_list[7], 71), 0)
    self_out_weight = scatter_about(key_list[3], (QH * HD, D), (QH * HD) ** -0.5, 0.109375, ((0, 16), (1, 2)))
    gain_query = jnp.clip(1.0 + 0.18 * jax.random.normal(key_list[4], (D,), jnp.float32), 0.1, 1.9)
    gain_keyvalue = jnp.clip(1.0 + 0.18 * jax.random.normal(key_list[5], (D,), jnp.float32), 0.1, 1.9)
    cross_weight = draw_cross_weight(jax.random.fold_in(key_list[7], 71), 0)
    return dict(residual_in=residual_in, self_queries=self_queries, self_keys_values=self_keys_values, self_out_weight=self_out_weight, gain_query=gain_query, gain_keyvalue=gain_keyvalue, cross_weight=cross_weight)


def softmax_rows(scores, allowed):
    masked = jnp.where(allowed, scores, -jnp.inf)
    row_top = lax.optimization_barrier(jnp.max(masked, axis=-1, keepdims=True))
    weights = jnp.where(allowed, jnp.exp(masked - row_top), 0.0)
    totals = lax.optimization_barrier(jnp.sum(weights, axis=-1))
    rounded = lax.optimization_barrier(weights.astype(jnp.bfloat16)).astype(jnp.float32)
    return (rounded, totals, weights)

def reference(residual_in, self_queries, self_keys_values, self_out_weight, gain_query, gain_keyvalue, cross_weight):
    score_scale = 1.0 / math.sqrt(HD)
    queries = self_queries.astype(jnp.float32).reshape(TOKENS, KVH, QPK, HD)
    paired = self_keys_values.astype(jnp.float32).reshape(TOKENS, KVH, 2, HD)
    padded = jnp.concatenate([jnp.zeros((WINDOW, KVH, 2, HD), jnp.float32), paired], axis=0)

    def self_block(block_index):
        first_row = (block_index * TOK_DEV).astype(jnp.int32)
        block_q = lax.dynamic_slice_in_dim(queries, first_row, TOK_DEV, 0)
        nearby = lax.dynamic_slice_in_dim(padded, first_row, WINDOW + TOK_DEV, 0)
        scores = jnp.einsum('tgqd,sgd->gqts', block_q, nearby[:, :, 0]) * score_scale
        query_pos = first_row + jnp.arange(TOK_DEV, dtype=jnp.int32)
        key_pos = first_row - WINDOW + jnp.arange(WINDOW + TOK_DEV, dtype=jnp.int32)
        allowed = (key_pos[None, :] <= query_pos[:, None]) & (key_pos[None, :] > query_pos[:, None] - WINDOW) & (key_pos[None, :] >= 0)
        rounded, totals, unused = softmax_rows(scores, allowed)
        weighted = jnp.einsum('gqts,sgd->tgqd', rounded, nearby[:, :, 1])
        return (weighted / jnp.transpose(totals, (2, 0, 1))[..., None]).astype(jnp.bfloat16)
    attended = lax.map(self_block, jnp.arange(TOKENS // TOK_DEV, dtype=jnp.int32)).reshape(TOKENS, KVH * QPK * HD)
    hidden = (residual_in.astype(jnp.float32) + jnp.dot(attended, self_out_weight, preferred_element_type=jnp.float32)).astype(jnp.bfloat16)
    widened = hidden.astype(jnp.float32)
    inverse = lax.rsqrt(lax.optimization_barrier(jnp.mean(widened * widened, axis=-1, keepdims=True)) + 1e-06)
    normed_q = (widened * inverse * gain_query).astype(jnp.bfloat16)
    normed_kv = (widened * inverse * gain_keyvalue).astype(jnp.bfloat16)
    col_layout = cross_weight.reshape(D, KVH, QPK + 2, HD)
    query_cols = col_layout[:, :, :QPK].reshape(D, KVH * QPK * HD)
    pair_cols = col_layout[:, :, QPK:].reshape(D, KVH * 2 * HD)
    cross_q = jnp.dot(normed_q, query_cols, preferred_element_type=jnp.float32)
    shared = jnp.dot(normed_kv, pair_cols, preferred_element_type=jnp.float32)
    cross_wide = cross_q.reshape(TOKENS, KVH, QPK, HD)
    shared_wide = shared.reshape(TOKENS, KVH, 2, HD)
    all_keys = jnp.arange(TOKENS, dtype=jnp.int32)

    def cross_block(block_index):
        first_row = (block_index * TOK_DEV).astype(jnp.int32)
        block_q = lax.dynamic_slice_in_dim(cross_wide, first_row, TOK_DEV, 0)
        scores = jnp.einsum('tgqd,sgd->gqts', block_q, shared_wide[:, :, 0], precision=lax.Precision.HIGHEST) * score_scale
        query_pos = first_row + jnp.arange(TOK_DEV, dtype=jnp.int32)
        allowed = all_keys[None, :] <= query_pos[:, None]
        unused, totals, weights = softmax_rows(scores, allowed)
        weighted = jnp.einsum('gqts,sgd->tgqd', weights, shared_wide[:, :, 1], precision=lax.Precision.HIGHEST)
        return (weighted / jnp.transpose(totals, (2, 0, 1))[..., None]).astype(jnp.bfloat16)
    cross_attention = lax.map(cross_block, jnp.arange(TOKENS // TOK_DEV, dtype=jnp.int32)).reshape(TOKENS, KVH * QPK * HD)
    return (hidden, cross_attention)
```

```python
import functools
import math

import jax
import jax.numpy as jnp
from jax import lax
from jax.experimental import pallas as pl
from jax.experimental.pallas import tpu as pltpu
from jax.sharding import PartitionSpec as P

HD = 128
QPK = 3
WINDOW = 2048


def _split(x):
    high = x.astype(jnp.bfloat16)
    low = (x - high.astype(jnp.float32)).astype(jnp.bfloat16)
    return high, low


def _attend_kernel(pos_ref, q_ref, kv_ref, o_ref, *, window, exact):
    rows = q_ref.shape[0]
    keys = kv_ref.shape[0]
    first = pos_ref[0]
    query_pos = first + lax.broadcasted_iota(jnp.int32, (rows, keys), 0)
    key_pos = lax.broadcasted_iota(jnp.int32, (rows, keys), 1)
    allowed = key_pos <= query_pos
    if window is not None:
        allowed = allowed & (key_pos > query_pos - window)
    key = kv_ref[:, :HD]
    value = kv_ref[:, HD:]
    score_scale = 1.0 / math.sqrt(HD)
    contract = (((1,), (1,)), ((), ()))
    for head in range(q_ref.shape[1] // HD):
        query = q_ref[:, head * HD:(head + 1) * HD]
        if exact:
            q_hi, q_lo = _split(query.astype(jnp.float32))
            scores = lax.dot_general(q_hi, key, contract, preferred_element_type=jnp.float32)
            scores = scores + lax.dot_general(q_lo, key, contract, preferred_element_type=jnp.float32)
        else:
            scores = lax.dot_general(query, key, contract, preferred_element_type=jnp.float32)
        scores = scores * score_scale
        masked = jnp.where(allowed, scores, -jnp.inf)
        row_top = jnp.max(masked, axis=-1, keepdims=True)
        weights = jnp.where(allowed, jnp.exp(masked - row_top), 0.0)
        totals = jnp.sum(weights, axis=-1, keepdims=True)
        if exact:
            w_hi, w_lo = _split(weights)
            acc = jnp.dot(w_hi, value, preferred_element_type=jnp.float32)
            acc = acc + jnp.dot(w_lo, value, preferred_element_type=jnp.float32)
        else:
            acc = jnp.dot(weights.astype(jnp.bfloat16), value, preferred_element_type=jnp.float32)
        o_ref[:, head * HD:(head + 1) * HD] = (acc / totals).astype(o_ref.dtype)


def attend(first_pos, queries, pairs, window, exact):
    rows, qcols = queries.shape
    keys, kvcols = pairs.shape
    groups = kvcols // (2 * HD)
    qblock = qcols // groups
    kernel = functools.partial(_attend_kernel, window=window, exact=exact)
    return pl.pallas_call(
        kernel,
        out_shape=jax.ShapeDtypeStruct((rows, qcols), jnp.bfloat16),
        grid_spec=pltpu.PrefetchScalarGridSpec(
            num_scalar_prefetch=1,
            grid=(groups,),
            in_specs=[
                pl.BlockSpec((rows, qblock), lambda g, pos: (0, g)),
                pl.BlockSpec((keys, 2 * HD), lambda g, pos: (0, g)),
            ],
            out_specs=pl.BlockSpec((rows, qblock), lambda g, pos: (0, g)),
        ),
    )(first_pos, queries, pairs)


def make_body(heads_count):
    def gather_heads(x):
        if heads_count == 2:
            other = lax.ppermute(x, "heads", [(0, 1), (1, 0)])
            first = lax.axis_index("heads") == 0
            low = jnp.where(first, x, other)
            high = jnp.where(first, other, x)
            return jnp.concatenate([low, high], axis=1)
        return lax.all_gather(x, "heads", axis=1, tiled=True)

    def body(
        residual_in,
        self_queries,
        self_keys_values,
        self_out_weight,
        gain_query,
        gain_keyvalue,
        cross_weight,
    ):
        tok_rows = residual_in.shape[0]
        groups = self_keys_values.shape[1] // (2 * HD)
        seq_place = lax.axis_index("seq")
        first_pos = (seq_place * tok_rows).astype(jnp.int32).reshape(1)

        key_window = lax.all_gather(self_keys_values, "seq", axis=0, tiled=True)
        attended = attend(first_pos, self_queries, key_window, WINDOW, False)

        out_weight = lax.all_gather(self_out_weight, "seq", axis=0, tiled=True)
        projected = jnp.dot(
            gather_heads(attended), out_weight, preferred_element_type=jnp.float32
        )
        hidden = (residual_in.astype(jnp.float32) + projected).astype(jnp.bfloat16)
        full_rows = gather_heads(hidden)
        widened = full_rows.astype(jnp.float32)
        inverse = lax.rsqrt(jnp.mean(widened * widened, axis=-1, keepdims=True) + 1e-06)
        normed_q = (widened * inverse * gain_query).astype(jnp.bfloat16)
        normed_kv = (widened * inverse * gain_keyvalue).astype(jnp.bfloat16)
        both = jnp.dot(
            jnp.concatenate([normed_q, normed_kv], axis=0),
            cross_weight,
            preferred_element_type=jnp.float32,
        ).reshape(2 * tok_rows, groups, QPK + 2, HD)
        cross_q = both[:tok_rows, :, :QPK].reshape(tok_rows, groups * QPK * HD)
        shared = both[tok_rows:, :, QPK:].reshape(tok_rows, groups * 2 * HD)
        shared_all = lax.all_gather(shared.astype(jnp.bfloat16), "seq", axis=0, tiled=True)
        cross_attention = attend(first_pos, cross_q, shared_all, None, True)
        return (hidden, cross_attention)

    return body


def solution(mesh):
    return jax.shard_map(
        make_body(mesh.shape["heads"]),
        mesh=mesh,
        in_specs=(
            P("seq", "heads"),
            P("seq", "heads"),
            P("seq", "heads"),
            P("seq", "heads"),
            P(),
            P(),
            P(None, "heads"),
        ),
        out_specs=(P("seq", "heads"), P("seq", "heads")),
        check_vma=False,
    )
```

```python
import functools
import math

import jax
import jax.numpy as jnp
from jax import lax
from jax.experimental import pallas as pl
from jax.experimental.pallas import tpu as pltpu
from jax.sharding import Mesh, PartitionSpec as P

HD = 128
QPK = 3
WINDOW = 2048


def _split(x):
    high = x.astype(jnp.bfloat16)
    low = (x - high.astype(jnp.float32)).astype(jnp.bfloat16)
    return high, low


def _attend_kernel(pos_ref, q_ref, *refs, window, exact, block_rows, cores):
    kv_refs = refs[:-1]
    o_ref = refs[-1]
    rows = q_ref.shape[0]
    first = pos_ref[0]
    masks = []
    for part, kv_ref in enumerate(kv_refs):
        keys = kv_ref.shape[0]
        query_pos = first + lax.broadcasted_iota(jnp.int32, (rows, keys), 0)
        index = lax.broadcasted_iota(jnp.int32, (rows, keys), 1)
        key_pos = ((index // block_rows) * cores + pos_ref[1 + part]) * block_rows + index % block_rows
        allowed = key_pos <= query_pos
        if window is not None:
            allowed = allowed & (key_pos > query_pos - window)
        masks.append(allowed)
    score_scale = 1.0 / math.sqrt(HD)
    contract = (((1,), (1,)), ((), ()))
    for head in range(q_ref.shape[1] // HD):
        query = q_ref[:, head * HD:(head + 1) * HD]
        if exact:
            q_hi, q_lo = _split(query.astype(jnp.float32))
        parts = []
        for kv_ref, allowed in zip(kv_refs, masks):
            key = kv_ref[:, :HD]
            if exact:
                scores = lax.dot_general(q_hi, key, contract, preferred_element_type=jnp.float32)
                scores = scores + lax.dot_general(q_lo, key, contract, preferred_element_type=jnp.float32)
            else:
                scores = lax.dot_general(query, key, contract, preferred_element_type=jnp.float32)
            parts.append(jnp.where(allowed, scores * score_scale, -jnp.inf))
        row_top = functools.reduce(
            jnp.maximum, [jnp.max(m, axis=-1, keepdims=True) for m in parts]
        )
        totals = 0.0
        acc = 0.0
        for kv_ref, allowed, masked in zip(kv_refs, masks, parts):
            value = kv_ref[:, HD:]
            weights = jnp.where(allowed, jnp.exp(masked - row_top), 0.0)
            totals = totals + jnp.sum(weights, axis=-1, keepdims=True)
            if exact:
                w_hi, w_lo = _split(weights)
                acc = acc + jnp.dot(w_hi, value, preferred_element_type=jnp.float32)
                acc = acc + jnp.dot(w_lo, value, preferred_element_type=jnp.float32)
            else:
                acc = acc + jnp.dot(weights.astype(jnp.bfloat16), value, preferred_element_type=jnp.float32)
        o_ref[:, head * HD:(head + 1) * HD] = (acc / totals).astype(o_ref.dtype)


def attend(places, queries, parts, window, exact, cores):
    rows, qcols = queries.shape
    groups = parts[0].shape[1] // (2 * HD)
    qblock = qcols // groups
    kernel = functools.partial(
        _attend_kernel, window=window, exact=exact, block_rows=rows, cores=cores
    )
    return pl.pallas_call(
        kernel,
        out_shape=jax.ShapeDtypeStruct((rows, qcols), jnp.bfloat16),
        grid_spec=pltpu.PrefetchScalarGridSpec(
            num_scalar_prefetch=1,
            grid=(groups,),
            in_specs=[pl.BlockSpec((rows, qblock), lambda g, pos: (0, g))]
            + [pl.BlockSpec((p.shape[0], 2 * HD), lambda g, pos: (0, g)) for p in parts],
            out_specs=pl.BlockSpec((rows, qblock), lambda g, pos: (0, g)),
        ),
    )(places, queries, *parts)


def make_body(heads_count):
    def gather_heads(x):
        if heads_count == 2:
            other = lax.ppermute(x, "heads", [(0, 1), (1, 0)])
            first = lax.axis_index("heads") == 0
            low = jnp.where(first, x, other)
            high = jnp.where(first, other, x)
            return jnp.concatenate([low, high], axis=1)
        return lax.all_gather(x, "heads", axis=1, tiled=True)

    def gather_seq(x):
        own = lax.all_gather(x, "chip", axis=0, tiled=True)
        other = lax.ppermute(own, "core", [(0, 1), (1, 0)])
        return own, other

    def body(
        residual_in,
        self_queries,
        self_keys_values,
        self_out_weight,
        gain_query,
        gain_keyvalue,
        cross_weight,
    ):
        tok_rows = residual_in.shape[0]
        groups = self_keys_values.shape[1] // (2 * HD)
        core = lax.axis_index("core")
        seq_place = lax.axis_index("chip") * 2 + core
        places = jnp.stack([seq_place * tok_rows, core, 1 - core]).astype(jnp.int32)

        key_parts = gather_seq(self_keys_values)
        attended = attend(places, self_queries, key_parts, WINDOW, False, 2)

        weight_own, weight_other = gather_seq(self_out_weight)
        att_full = gather_heads(attended)
        chips = weight_own.shape[0] // self_out_weight.shape[0]
        att_split = att_full.reshape(tok_rows, chips, 2, self_out_weight.shape[0])
        att_own = jnp.where(core == 0, att_split[:, :, 0], att_split[:, :, 1])
        att_other = jnp.where(core == 0, att_split[:, :, 1], att_split[:, :, 0])
        projected = jnp.dot(
            att_own.reshape(tok_rows, -1), weight_own, preferred_element_type=jnp.float32
        ) + jnp.dot(
            att_other.reshape(tok_rows, -1), weight_other, preferred_element_type=jnp.float32
        )
        hidden = (residual_in.astype(jnp.float32) + projected).astype(jnp.bfloat16)
        full_rows = gather_heads(hidden)
        widened = full_rows.astype(jnp.float32)
        inverse = lax.rsqrt(jnp.mean(widened * widened, axis=-1, keepdims=True) + 1e-06)
        normed_q = (widened * inverse * gain_query).astype(jnp.bfloat16)
        normed_kv = (widened * inverse * gain_keyvalue).astype(jnp.bfloat16)
        both = jnp.dot(
            jnp.concatenate([normed_q, normed_kv], axis=0),
            cross_weight,
            preferred_element_type=jnp.float32,
        ).reshape(2 * tok_rows, groups, QPK + 2, HD)
        cross_q = both[:tok_rows, :, :QPK].reshape(tok_rows, groups * QPK * HD)
        shared = both[tok_rows:, :, QPK:].reshape(tok_rows, groups * 2 * HD)
        shared_parts = gather_seq(shared.astype(jnp.bfloat16))
        cross_attention = attend(places, cross_q, shared_parts, None, True, 2)
        return (hidden, cross_attention)

    return body


def solution(mesh):
    seq_count = mesh.shape["seq"]
    heads_count = mesh.shape["heads"]
    split = Mesh(
        mesh.devices.reshape(seq_count // 2, 2, heads_count), ("chip", "core", "heads")
    )
    rows = P(("chip", "core"), "heads")
    return jax.shard_map(
        make_body(heads_count),
        mesh=split,
        in_specs=(rows, rows, rows, rows, P(), P(), P(None, "heads")),
        out_specs=(rows, rows),
        check_vma=False,
    )
```

```python
import functools
import math

import jax
import jax.numpy as jnp
from jax import lax
from jax.experimental import pallas as pl
from jax.experimental.pallas import tpu as pltpu
from jax.sharding import PartitionSpec as P

HD = 128
QPK = 3
WINDOW = 2048


def _split(x):
    high = x.astype(jnp.bfloat16)
    low = (x - high.astype(jnp.float32)).astype(jnp.bfloat16)
    return high, low


def _attend_kernel(pos_ref, q_ref, kv_ref, o_ref, *, window, exact):
    rows = q_ref.shape[0]
    keys = kv_ref.shape[0]
    first = pos_ref[0]
    query_pos = first + lax.broadcasted_iota(jnp.int32, (rows, keys), 0)
    key_pos = lax.broadcasted_iota(jnp.int32, (rows, keys), 1)
    allowed = key_pos <= query_pos
    if window is not None:
        allowed = allowed & (key_pos > query_pos - window)
    key = kv_ref[:, :HD]
    value = kv_ref[:, HD:]
    score_scale = 1.0 / math.sqrt(HD)
    contract = (((1,), (1,)), ((), ()))
    for head in range(q_ref.shape[1] // HD):
        query = q_ref[:, head * HD:(head + 1) * HD]
        if exact:
            q_hi, q_lo = _split(query.astype(jnp.float32))
            scores = lax.dot_general(q_hi, key, contract, preferred_element_type=jnp.float32)
            scores = scores + lax.dot_general(q_lo, key, contract, preferred_element_type=jnp.float32)
        else:
            scores = lax.dot_general(query, key, contract, preferred_element_type=jnp.float32)
        scores = scores * score_scale
        masked = jnp.where(allowed, scores, -jnp.inf)
        row_top = jnp.max(masked, axis=-1, keepdims=True)
        weights = jnp.where(allowed, jnp.exp(masked - row_top), 0.0)
        totals = jnp.sum(weights, axis=-1, keepdims=True)
        if exact:
            w_hi, w_lo = _split(weights)
            acc = jnp.dot(w_hi, value, preferred_element_type=jnp.float32)
            acc = acc + jnp.dot(w_lo, value, preferred_element_type=jnp.float32)
        else:
            acc = jnp.dot(weights.astype(jnp.bfloat16), value, preferred_element_type=jnp.float32)
        o_ref[:, head * HD:(head + 1) * HD] = (acc / totals).astype(o_ref.dtype)


def attend(first_pos, queries, pairs, window, exact):
    rows, qcols = queries.shape
    keys, kvcols = pairs.shape
    groups = kvcols // (2 * HD)
    qblock = qcols // groups
    kernel = functools.partial(_attend_kernel, window=window, exact=exact)
    return pl.pallas_call(
        kernel,
        out_shape=jax.ShapeDtypeStruct((rows, qcols), jnp.bfloat16),
        grid_spec=pltpu.PrefetchScalarGridSpec(
            num_scalar_prefetch=1,
            grid=(groups,),
            in_specs=[
                pl.BlockSpec((rows, qblock), lambda g, pos: (0, g)),
                pl.BlockSpec((keys, 2 * HD), lambda g, pos: (0, g)),
            ],
            out_specs=pl.BlockSpec((rows, qblock), lambda g, pos: (0, g)),
        ),
    )(first_pos, queries, pairs)


def make_body(heads_count):
    def gather_heads(x):
        if heads_count == 2:
            other = lax.ppermute(x, "heads", [(0, 1), (1, 0)])
            first = lax.axis_index("heads") == 0
            low = jnp.where(first, x, other)
            high = jnp.where(first, other, x)
            return jnp.concatenate([low, high], axis=1)
        return lax.all_gather(x, "heads", axis=1, tiled=True)

    def body(
        residual_in,
        self_queries,
        self_keys_values,
        self_out_weight,
        gain_query,
        gain_keyvalue,
        cross_weight,
    ):
        tok_rows = residual_in.shape[0]
        groups = self_keys_values.shape[1] // (2 * HD)
        seq_place = lax.axis_index("seq")
        first_pos = (seq_place * tok_rows).astype(jnp.int32).reshape(1)

        kv_size = self_keys_values.size
        packed = jnp.concatenate([self_keys_values.reshape(-1), self_out_weight.reshape(-1)])
        gathered = lax.all_gather(packed[None], "seq", axis=0, tiled=True)
        col_layout = cross_weight.reshape(cross_weight.shape[0], groups, QPK + 2, HD)
        weight_kv = col_layout[:, :, QPK:].reshape(cross_weight.shape[0], groups * 2 * HD)
        weight_q = col_layout[:, :, :QPK].reshape(cross_weight.shape[0], groups * QPK * HD)
        gathered, weight_kv, weight_q = lax.optimization_barrier((gathered, weight_kv, weight_q))
        seq_count = gathered.shape[0]
        key_window = gathered[:, :kv_size].reshape(seq_count * tok_rows, -1)
        out_weight = gathered[:, kv_size:].reshape(
            seq_count * self_out_weight.shape[0], self_out_weight.shape[1]
        )
        attended = attend(first_pos, self_queries, key_window, WINDOW, False)

        projected = jnp.dot(
            gather_heads(attended), out_weight, preferred_element_type=jnp.float32
        )
        hidden = (residual_in.astype(jnp.float32) + projected).astype(jnp.bfloat16)
        full_rows = gather_heads(hidden)
        widened = full_rows.astype(jnp.float32)
        inverse = lax.rsqrt(jnp.mean(widened * widened, axis=-1, keepdims=True) + 1e-06)
        normed_q = (widened * inverse * gain_query).astype(jnp.bfloat16)
        normed_kv = (widened * inverse * gain_keyvalue).astype(jnp.bfloat16)
        shared = jnp.dot(normed_kv, weight_kv, preferred_element_type=jnp.float32)
        shared_all = lax.all_gather(shared.astype(jnp.bfloat16), "seq", axis=0, tiled=True)
        cross_q = jnp.dot(normed_q, weight_q, preferred_element_type=jnp.float32)
        cross_attention = attend(first_pos, cross_q, shared_all, None, True)
        return (hidden, cross_attention)

    return body


def solution(mesh):
    return jax.shard_map(
        make_body(mesh.shape["heads"]),
        mesh=mesh,
        in_specs=(
            P("seq", "heads"),
            P("seq", "heads"),
            P("seq", "heads"),
            P("seq", "heads"),
            P(),
            P(),
            P(None, "heads"),
        ),
        out_specs=(P("seq", "heads"), P("seq", "heads")),
        check_vma=False,
    )
```

```python
import functools
import math

import jax
import jax.numpy as jnp
from jax import lax
from jax.experimental import pallas as pl
from jax.experimental.pallas import tpu as pltpu
from jax.sharding import PartitionSpec as P

HD = 128
QPK = 3
WINDOW = 2048


def _split(x):
    high = x.astype(jnp.bfloat16)
    low = (x - high.astype(jnp.float32)).astype(jnp.bfloat16)
    return high, low


def _attend_kernel(pos_ref, q_ref, kv_ref, o_ref, *, window, exact):
    rows = q_ref.shape[0]
    keys = kv_ref.shape[0] * (kv_ref.shape[1] // 2 if len(kv_ref.shape) == 3 else 1)
    first = pos_ref[0]
    query_pos = first + lax.broadcasted_iota(jnp.int32, (rows, keys), 0)
    key_pos = lax.broadcasted_iota(jnp.int32, (rows, keys), 1)
    allowed = key_pos <= query_pos
    if window is not None:
        allowed = allowed & (key_pos > query_pos - window)
    if len(kv_ref.shape) == 3:
        half = kv_ref.shape[1] // 2
        key = kv_ref[:, :half, :].reshape(-1, HD)
        value = kv_ref[:, half:, :].reshape(-1, HD)
    else:
        key = kv_ref[:, :HD]
        value = kv_ref[:, HD:]
    score_scale = 1.0 / math.sqrt(HD)
    contract = (((1,), (1,)), ((), ()))
    for head in range(q_ref.shape[1] // HD):
        query = q_ref[:, head * HD:(head + 1) * HD]
        if exact:
            q_hi, q_lo = _split(query.astype(jnp.float32))
            scores = lax.dot_general(q_hi, key, contract, preferred_element_type=jnp.float32)
            scores = scores + lax.dot_general(q_lo, key, contract, preferred_element_type=jnp.float32)
        else:
            scores = lax.dot_general(query, key, contract, preferred_element_type=jnp.float32)
        scores = scores * score_scale
        masked = jnp.where(allowed, scores, -jnp.inf)
        row_top = jnp.max(masked, axis=-1, keepdims=True)
        weights = jnp.where(allowed, jnp.exp(masked - row_top), 0.0)
        totals = jnp.sum(weights, axis=-1, keepdims=True)
        if exact:
            w_hi, w_lo = _split(weights)
            acc = jnp.dot(w_hi, value, preferred_element_type=jnp.float32)
            acc = acc + jnp.dot(w_lo, value, preferred_element_type=jnp.float32)
        else:
            acc = jnp.dot(weights.astype(jnp.bfloat16), value, preferred_element_type=jnp.float32)
        o_ref[:, head * HD:(head + 1) * HD] = (acc / totals).astype(o_ref.dtype)


def attend(first_pos, queries, pairs, window, exact, groups=None, offset=0):
    rows, qcols = queries.shape
    if groups is None:
        groups = pairs.shape[1] // (2 * HD)
        kv_spec = pl.BlockSpec((pairs.shape[0], 2 * HD), lambda g, pos: (0, g))
    else:
        kv_spec = pl.BlockSpec((pairs.shape[0], 2 * rows, HD), lambda g, pos: (0, offset + g, 0))
    qblock = qcols // groups
    kernel = functools.partial(_attend_kernel, window=window, exact=exact)
    return pl.pallas_call(
        kernel,
        out_shape=jax.ShapeDtypeStruct((rows, qcols), jnp.bfloat16),
        grid_spec=pltpu.PrefetchScalarGridSpec(
            num_scalar_prefetch=1,
            grid=(groups,),
            in_specs=[
                pl.BlockSpec((rows, qblock), lambda g, pos: (0, g)),
                kv_spec,
            ],
            out_specs=pl.BlockSpec((rows, qblock), lambda g, pos: (0, g)),
        ),
    )(first_pos, queries, pairs)


def _project_kernel(att_ref, w_ref, res_ref, o_ref):
    weight = w_ref[...].reshape(-1, w_ref.shape[-1])
    acc = jnp.dot(att_ref[...], weight, preferred_element_type=jnp.float32)
    o_ref[...] = (res_ref[...].astype(jnp.float32) + acc).astype(o_ref.dtype)


def project(attended, slab, residual, weight_rows):
    rows, width = residual.shape
    return pl.pallas_call(
        _project_kernel,
        out_shape=jax.ShapeDtypeStruct((rows, width), jnp.bfloat16),
        grid=(width // HD,),
        in_specs=[
            pl.BlockSpec(attended.shape, lambda c: (0, 0)),
            pl.BlockSpec((slab.shape[0], weight_rows, HD), lambda c: (0, c, 0)),
            pl.BlockSpec((rows, HD), lambda c: (0, c)),
        ],
        out_specs=pl.BlockSpec((rows, HD), lambda c: (0, c)),
    )(attended, slab, residual)


def to_slab(x):
    rows, cols = x.shape
    return x.reshape(rows, cols // HD, HD).transpose(1, 0, 2).reshape(-1, HD)


def make_body(heads_count):
    def gather_heads(x):
        if heads_count == 2:
            other = lax.ppermute(x, "heads", [(0, 1), (1, 0)])
            first = lax.axis_index("heads") == 0
            low = jnp.where(first, x, other)
            high = jnp.where(first, other, x)
            return jnp.concatenate([low, high], axis=1)
        return lax.all_gather(x, "heads", axis=1, tiled=True)

    def body(
        residual_in,
        self_queries,
        self_keys_values,
        self_out_weight,
        gain_query,
        gain_keyvalue,
        cross_weight,
    ):
        tok_rows = residual_in.shape[0]
        groups = self_keys_values.shape[1] // (2 * HD)
        seq_place = lax.axis_index("seq")
        first_pos = (seq_place * tok_rows).astype(jnp.int32).reshape(1)

        weight_rows = self_out_weight.shape[0]
        weight_part = to_slab(self_out_weight)
        pad = (-weight_part.shape[0]) % (2 * tok_rows)
        weight_part = jnp.pad(weight_part, ((0, pad), (0, 0)))
        offset = weight_part.shape[0] // (2 * tok_rows)
        packed = jnp.concatenate([weight_part, to_slab(self_keys_values)], axis=0)
        slab = lax.all_gather(packed[None], "seq", axis=0, tiled=True)
        attended = attend(first_pos, self_queries, slab, WINDOW, False, groups, offset)
        hidden = project(gather_heads(attended), slab, residual_in, weight_rows)
        full_rows = gather_heads(hidden)
        widened = full_rows.astype(jnp.float32)
        inverse = lax.rsqrt(jnp.mean(widened * widened, axis=-1, keepdims=True) + 1e-06)
        normed_q = (widened * inverse * gain_query).astype(jnp.bfloat16)
        normed_kv = (widened * inverse * gain_keyvalue).astype(jnp.bfloat16)
        both = jnp.dot(
            jnp.concatenate([normed_q, normed_kv], axis=0),
            cross_weight,
            preferred_element_type=jnp.float32,
        ).reshape(2 * tok_rows, groups, QPK + 2, HD)
        cross_q = both[:tok_rows, :, :QPK].reshape(tok_rows, groups * QPK * HD)
        shared = both[tok_rows:, :, QPK:].reshape(tok_rows, groups * 2 * HD)
        shared_all = lax.all_gather(shared.astype(jnp.bfloat16), "seq", axis=0, tiled=True)
        cross_attention = attend(first_pos, cross_q, shared_all, None, True)
        return (hidden, cross_attention)

    return body


def solution(mesh):
    return jax.shard_map(
        make_body(mesh.shape["heads"]),
        mesh=mesh,
        in_specs=(
            P("seq", "heads"),
            P("seq", "heads"),
            P("seq", "heads"),
            P("seq", "heads"),
            P(),
            P(),
            P(None, "heads"),
        ),
        out_specs=(P("seq", "heads"), P("seq", "heads")),
        check_vma=False,
    )
```

```python
import functools
import math

import jax
import jax.numpy as jnp
from jax import lax
from jax.experimental import pallas as pl
from jax.experimental.pallas import tpu as pltpu
from jax.sharding import PartitionSpec as P

HD = 128
QPK = 3
WINDOW = 2048


def _split(x):
    high = x.astype(jnp.bfloat16)
    low = (x - high.astype(jnp.float32)).astype(jnp.bfloat16)
    return high, low


def _attend_kernel(pos_ref, q_ref, kv_ref, o_ref, *, window, exact):
    rows = q_ref.shape[0]
    keys = kv_ref.shape[0] * (kv_ref.shape[1] // 2 if len(kv_ref.shape) == 3 else 1)
    first = pos_ref[0]
    query_pos = first + lax.broadcasted_iota(jnp.int32, (rows, keys), 0)
    key_pos = lax.broadcasted_iota(jnp.int32, (rows, keys), 1)
    allowed = key_pos <= query_pos
    if window is not None:
        allowed = allowed & (key_pos > query_pos - window)
    if len(kv_ref.shape) == 3:
        half = kv_ref.shape[1] // 2
        key = kv_ref[:, :half, :].reshape(-1, HD)
        value = kv_ref[:, half:, :].reshape(-1, HD)
    else:
        key = kv_ref[:, :HD]
        value = kv_ref[:, HD:]
    score_scale = 1.0 / math.sqrt(HD)
    contract = (((1,), (1,)), ((), ()))
    for head in range(q_ref.shape[1] // HD):
        query = q_ref[:, head * HD:(head + 1) * HD]
        if exact:
            q_hi, q_lo = _split(query.astype(jnp.float32))
            scores = lax.dot_general(q_hi, key, contract, preferred_element_type=jnp.float32)
            scores = scores + lax.dot_general(q_lo, key, contract, preferred_element_type=jnp.float32)
        else:
            scores = lax.dot_general(query, key, contract, preferred_element_type=jnp.float32)
        scores = scores * score_scale
        masked = jnp.where(allowed, scores, -jnp.inf)
        row_top = jnp.max(masked, axis=-1, keepdims=True)
        weights = jnp.where(allowed, jnp.exp(masked - row_top), 0.0)
        totals = jnp.sum(weights, axis=-1, keepdims=True)
        if exact:
            w_hi, w_lo = _split(weights)
            acc = jnp.dot(w_hi, value, preferred_element_type=jnp.float32)
            acc = acc + jnp.dot(w_lo, value, preferred_element_type=jnp.float32)
        else:
            acc = jnp.dot(weights.astype(jnp.bfloat16), value, preferred_element_type=jnp.float32)
        o_ref[:, head * HD:(head + 1) * HD] = (acc / totals).astype(o_ref.dtype)


def attend(first_pos, queries, pairs, window, exact, groups=None, offset=0):
    rows, qcols = queries.shape
    if groups is None:
        groups = pairs.shape[1] // (2 * HD)
        kv_spec = pl.BlockSpec((pairs.shape[0], 2 * HD), lambda g, pos: (0, g))
    else:
        kv_spec = pl.BlockSpec((pairs.shape[0], 2 * rows, HD), lambda g, pos: (0, offset + g, 0))
    qblock = qcols // groups
    kernel = functools.partial(_attend_kernel, window=window, exact=exact)
    return pl.pallas_call(
        kernel,
        out_shape=jax.ShapeDtypeStruct((rows, qcols), jnp.bfloat16),
        grid_spec=pltpu.PrefetchScalarGridSpec(
            num_scalar_prefetch=1,
            grid=(groups,),
            in_specs=[
                pl.BlockSpec((rows, qblock), lambda g, pos: (0, g)),
                kv_spec,
            ],
            out_specs=pl.BlockSpec((rows, qblock), lambda g, pos: (0, g)),
        ),
    )(first_pos, queries, pairs)


def _project_kernel(att_ref, w_ref, res_ref, o_ref, *, weight_rows):
    for part in range(o_ref.shape[1] // HD):
        weight = w_ref[:, part * weight_rows:(part + 1) * weight_rows, :].reshape(-1, HD)
        acc = jnp.dot(att_ref[...], weight, preferred_element_type=jnp.float32)
        cols = slice(part * HD, (part + 1) * HD)
        o_ref[:, cols] = (res_ref[:, cols].astype(jnp.float32) + acc).astype(o_ref.dtype)


def project(attended, slab, residual, weight_rows):
    rows, width = residual.shape
    blocks = width // HD
    per_step = next(n for n in (4, 3, 2, 1) if blocks % n == 0)
    return pl.pallas_call(
        functools.partial(_project_kernel, weight_rows=weight_rows),
        out_shape=jax.ShapeDtypeStruct((rows, width), jnp.bfloat16),
        grid=(blocks // per_step,),
        in_specs=[
            pl.BlockSpec(attended.shape, lambda c: (0, 0)),
            pl.BlockSpec((slab.shape[0], per_step * weight_rows, HD), lambda c: (0, c, 0)),
            pl.BlockSpec((rows, per_step * HD), lambda c: (0, c)),
        ],
        out_specs=pl.BlockSpec((rows, per_step * HD), lambda c: (0, c)),
    )(attended, slab, residual)


def to_slab(x):
    rows, cols = x.shape
    return x.reshape(rows, cols // HD, HD).transpose(1, 0, 2).reshape(-1, HD)


def make_body(heads_count):
    def gather_heads(x):
        if heads_count == 2:
            other = lax.ppermute(x, "heads", [(0, 1), (1, 0)])
            first = lax.axis_index("heads") == 0
            low = jnp.where(first, x, other)
            high = jnp.where(first, other, x)
            return jnp.concatenate([low, high], axis=1)
        return lax.all_gather(x, "heads", axis=1, tiled=True)

    def body(
        residual_in,
        self_queries,
        self_keys_values,
        self_out_weight,
        gain_query,
        gain_keyvalue,
        cross_weight,
    ):
        tok_rows = residual_in.shape[0]
        groups = self_keys_values.shape[1] // (2 * HD)
        seq_place = lax.axis_index("seq")
        first_pos = (seq_place * tok_rows).astype(jnp.int32).reshape(1)

        weight_rows = self_out_weight.shape[0]
        weight_part = to_slab(self_out_weight)
        pad = (-weight_part.shape[0]) % (2 * tok_rows)
        weight_part = jnp.pad(weight_part, ((0, pad), (0, 0)))
        offset = weight_part.shape[0] // (2 * tok_rows)
        packed = jnp.concatenate([weight_part, to_slab(self_keys_values)], axis=0)
        slab = lax.all_gather(packed[None], "seq", axis=0, tiled=True)
        col_layout = cross_weight.reshape(cross_weight.shape[0], groups, QPK + 2, HD)
        weight_kv = col_layout[:, :, QPK:].reshape(cross_weight.shape[0], groups * 2 * HD)
        weight_q = col_layout[:, :, :QPK].reshape(cross_weight.shape[0], groups * QPK * HD)
        slab, weight_kv, weight_q = lax.optimization_barrier((slab, weight_kv, weight_q))
        attended = attend(first_pos, self_queries, slab, WINDOW, False, groups, offset)
        hidden = project(gather_heads(attended), slab, residual_in, weight_rows)
        full_rows = gather_heads(hidden)
        widened = full_rows.astype(jnp.float32)
        inverse = lax.rsqrt(jnp.mean(widened * widened, axis=-1, keepdims=True) + 1e-06)
        normed_q = (widened * inverse * gain_query).astype(jnp.bfloat16)
        normed_kv = (widened * inverse * gain_keyvalue).astype(jnp.bfloat16)
        shared = jnp.dot(normed_kv, weight_kv, preferred_element_type=jnp.float32)
        shared_all = lax.all_gather(shared.astype(jnp.bfloat16), "seq", axis=0, tiled=True)
        cross_q = jnp.dot(normed_q, weight_q, preferred_element_type=jnp.float32)
        cross_attention = attend(first_pos, cross_q, shared_all, None, True)
        return (hidden, cross_attention)

    return body


def solution(mesh):
    return jax.shard_map(
        make_body(mesh.shape["heads"]),
        mesh=mesh,
        in_specs=(
            P("seq", "heads"),
            P("seq", "heads"),
            P("seq", "heads"),
            P("seq", "heads"),
            P(),
            P(),
            P(None, "heads"),
        ),
        out_specs=(P("seq", "heads"), P("seq", "heads")),
        check_vma=False,
    )
```

```python
import functools
import math

import jax
import jax.numpy as jnp
from jax import lax
from jax.experimental import pallas as pl
from jax.experimental.pallas import tpu as pltpu
from jax.sharding import PartitionSpec as P

HD = 128
QPK = 3
WINDOW = 2048


def _split(x):
    high = x.astype(jnp.bfloat16)
    low = (x - high.astype(jnp.float32)).astype(jnp.bfloat16)
    return high, low


def _attend_kernel(pos_ref, q_ref, kv_ref, o_ref, *, window, exact):
    rows = q_ref.shape[0]
    keys = kv_ref.shape[0] * (kv_ref.shape[1] // 2 if len(kv_ref.shape) == 3 else 1)
    first = pos_ref[0]
    query_pos = first + lax.broadcasted_iota(jnp.int32, (rows, keys), 0)
    key_pos = lax.broadcasted_iota(jnp.int32, (rows, keys), 1)
    allowed = key_pos <= query_pos
    if window is not None:
        allowed = allowed & (key_pos > query_pos - window)
    if len(kv_ref.shape) == 3:
        half = kv_ref.shape[1] // 2
        key = kv_ref[:, :half, :].reshape(-1, HD)
        value = kv_ref[:, half:, :].reshape(-1, HD)
    else:
        key = kv_ref[:, :HD]
        value = kv_ref[:, HD:]
    score_scale = 1.0 / math.sqrt(HD)
    contract = (((1,), (1,)), ((), ()))
    for head in range(q_ref.shape[1] // HD):
        query = q_ref[:, head * HD:(head + 1) * HD]
        if exact:
            q_hi, q_lo = _split(query.astype(jnp.float32))
            scores = lax.dot_general(q_hi, key, contract, preferred_element_type=jnp.float32)
            scores = scores + lax.dot_general(q_lo, key, contract, preferred_element_type=jnp.float32)
        else:
            scores = lax.dot_general(query, key, contract, preferred_element_type=jnp.float32)
        scores = scores * score_scale
        masked = jnp.where(allowed, scores, -jnp.inf)
        row_top = jnp.max(masked, axis=-1, keepdims=True)
        weights = jnp.where(allowed, jnp.exp(masked - row_top), 0.0)
        totals = jnp.sum(weights, axis=-1, keepdims=True)
        if exact:
            w_hi, w_lo = _split(weights)
            acc = jnp.dot(w_hi, value, preferred_element_type=jnp.float32)
            acc = acc + jnp.dot(w_lo, value, preferred_element_type=jnp.float32)
        else:
            acc = jnp.dot(weights.astype(jnp.bfloat16), value, preferred_element_type=jnp.float32)
        o_ref[:, head * HD:(head + 1) * HD] = (acc / totals).astype(o_ref.dtype)


def attend(first_pos, queries, pairs, window, exact, groups=None, offset=0):
    rows, qcols = queries.shape
    if groups is None:
        groups = pairs.shape[1] // (2 * HD)
        kv_spec = pl.BlockSpec((pairs.shape[0], 2 * HD), lambda g, pos: (0, g))
    else:
        kv_spec = pl.BlockSpec((pairs.shape[0], 2 * rows, HD), lambda g, pos: (0, offset + g, 0))
    qblock = qcols // groups
    kernel = functools.partial(_attend_kernel, window=window, exact=exact)
    return pl.pallas_call(
        kernel,
        out_shape=jax.ShapeDtypeStruct((rows, qcols), jnp.bfloat16),
        grid_spec=pltpu.PrefetchScalarGridSpec(
            num_scalar_prefetch=1,
            grid=(groups,),
            in_specs=[
                pl.BlockSpec((rows, qblock), lambda g, pos: (0, g)),
                kv_spec,
            ],
            out_specs=pl.BlockSpec((rows, qblock), lambda g, pos: (0, g)),
        ),
    )(first_pos, queries, pairs)


def _project_kernel(att_ref, w_ref, res_ref, o_ref, *, weight_rows):
    for part in range(o_ref.shape[1] // HD):
        weight = w_ref[:, part * weight_rows:(part + 1) * weight_rows, :].reshape(-1, HD)
        acc = jnp.dot(att_ref[...], weight, preferred_element_type=jnp.float32)
        cols = slice(part * HD, (part + 1) * HD)
        o_ref[:, cols] = (res_ref[:, cols].astype(jnp.float32) + acc).astype(o_ref.dtype)


def project(attended, slab, residual, weight_rows):
    rows, width = residual.shape
    blocks = width // HD
    per_step = next(n for n in (4, 3, 2, 1) if blocks % n == 0)
    return pl.pallas_call(
        functools.partial(_project_kernel, weight_rows=weight_rows),
        out_shape=jax.ShapeDtypeStruct((rows, width), jnp.bfloat16),
        grid=(blocks // per_step,),
        in_specs=[
            pl.BlockSpec(attended.shape, lambda c: (0, 0)),
            pl.BlockSpec((slab.shape[0], per_step * weight_rows, HD), lambda c: (0, c, 0)),
            pl.BlockSpec((rows, per_step * HD), lambda c: (0, c)),
        ],
        out_specs=pl.BlockSpec((rows, per_step * HD), lambda c: (0, c)),
    )(attended, slab, residual)


def _half_kernel(sel_ref, att_ref, w_ref, *refs, weight_rows):
    o_ref = refs[-1]
    for part in range(o_ref.shape[1] // HD):
        weight = w_ref[:, part * weight_rows:(part + 1) * weight_rows, :].reshape(-1, HD)
        acc = jnp.dot(att_ref[...], weight, preferred_element_type=jnp.float32)
        cols = slice(part * HD, (part + 1) * HD)
        for base_ref in refs[:-1]:
            acc = acc + base_ref[:, cols].astype(jnp.float32)
        o_ref[:, cols] = acc.astype(o_ref.dtype)


def project_half(which, attended, slab, bases, weight_rows, out_dtype, width):
    rows = attended.shape[0]
    blocks = width // HD
    per_step = next(n for n in (4, 3, 2, 1) if blocks % n == 0)
    devices = attended.shape[1] // weight_rows
    return pl.pallas_call(
        functools.partial(_half_kernel, weight_rows=weight_rows),
        out_shape=jax.ShapeDtypeStruct((rows, width), out_dtype),
        grid_spec=pltpu.PrefetchScalarGridSpec(
            num_scalar_prefetch=1,
            grid=(blocks // per_step,),
            in_specs=[
                pl.BlockSpec(attended.shape, lambda c, sel: (0, 0)),
                pl.BlockSpec((devices, per_step * weight_rows, HD), lambda c, sel: (sel[0], c, 0)),
            ]
            + [pl.BlockSpec((rows, per_step * HD), lambda c, sel: (0, c)) for _ in bases],
            out_specs=pl.BlockSpec((rows, per_step * HD), lambda c, sel: (0, c)),
        ),
    )(which, attended, slab, *bases)


def to_slab(x):
    rows, cols = x.shape
    return x.reshape(rows, cols // HD, HD).transpose(1, 0, 2).reshape(-1, HD)


def make_body(heads_count):
    def gather_heads(x):
        if heads_count == 2:
            other = lax.ppermute(x, "heads", [(0, 1), (1, 0)])
            first = lax.axis_index("heads") == 0
            low = jnp.where(first, x, other)
            high = jnp.where(first, other, x)
            return jnp.concatenate([low, high], axis=1)
        return lax.all_gather(x, "heads", axis=1, tiled=True)

    def body(
        residual_in,
        self_queries,
        self_keys_values,
        self_out_weight,
        gain_query,
        gain_keyvalue,
        cross_weight,
    ):
        tok_rows = residual_in.shape[0]
        groups = self_keys_values.shape[1] // (2 * HD)
        seq_place = lax.axis_index("seq")
        first_pos = (seq_place * tok_rows).astype(jnp.int32).reshape(1)

        weight_rows = self_out_weight.shape[0]
        weight_part = to_slab(self_out_weight)
        pad = (-weight_part.shape[0]) % (2 * tok_rows)
        weight_part = jnp.pad(weight_part, ((0, pad), (0, 0)))
        offset = weight_part.shape[0] // (2 * tok_rows)
        packed = jnp.concatenate([weight_part, to_slab(self_keys_values)], axis=0)
        slab = lax.all_gather(packed[None], "seq", axis=0, tiled=True)
        col_layout = cross_weight.reshape(cross_weight.shape[0], groups, QPK + 2, HD)
        weight_kv = col_layout[:, :, QPK:].reshape(cross_weight.shape[0], groups * 2 * HD)
        weight_q = col_layout[:, :, :QPK].reshape(cross_weight.shape[0], groups * QPK * HD)
        slab, weight_kv, weight_q = lax.optimization_barrier((slab, weight_kv, weight_q))
        attended = attend(first_pos, self_queries, slab, WINDOW, False, groups, offset)
        if heads_count == 2:
            place = lax.axis_index("heads")
            other = lax.ppermute(attended, "heads", [(0, 1), (1, 0)])
            width = residual_in.shape[1]
            own_part = project_half(
                place.astype(jnp.int32).reshape(1), attended, slab,
                [], weight_rows, jnp.float32, width,
            )
            hidden = project_half(
                (1 - place).astype(jnp.int32).reshape(1), other, slab,
                [own_part, residual_in], weight_rows, jnp.bfloat16, width,
            )
        else:
            hidden = project(gather_heads(attended), slab, residual_in, weight_rows)
        full_rows = gather_heads(hidden)
        widened = full_rows.astype(jnp.float32)
        inverse = lax.rsqrt(jnp.mean(widened * widened, axis=-1, keepdims=True) + 1e-06)
        normed_q = (widened * inverse * gain_query).astype(jnp.bfloat16)
        normed_kv = (widened * inverse * gain_keyvalue).astype(jnp.bfloat16)
        shared = jnp.dot(normed_kv, weight_kv, preferred_element_type=jnp.float32)
        shared_all = lax.all_gather(shared.astype(jnp.bfloat16), "seq", axis=0, tiled=True)
        cross_q = jnp.dot(normed_q, weight_q, preferred_element_type=jnp.float32)
        cross_attention = attend(first_pos, cross_q, shared_all, None, True)
        return (hidden, cross_attention)

    return body


def solution(mesh):
    return jax.shard_map(
        make_body(mesh.shape["heads"]),
        mesh=mesh,
        in_specs=(
            P("seq", "heads"),
            P("seq", "heads"),
            P("seq", "heads"),
            P("seq", "heads"),
            P(),
            P(),
            P(None, "heads"),
        ),
        out_specs=(P("seq", "heads"), P("seq", "heads")),
        check_vma=False,
    )
```

```python
import functools
import math

import jax
import jax.numpy as jnp
from jax import lax
from jax.experimental import pallas as pl
from jax.experimental.pallas import tpu as pltpu
from jax.sharding import PartitionSpec as P

HD = 128
QPK = 3
WINDOW = 2048


def _split(x):
    high = x.astype(jnp.bfloat16)
    low = (x - high.astype(jnp.float32)).astype(jnp.bfloat16)
    return high, low


def _attend_kernel(pos_ref, q_ref, kv_ref, o_ref, *, window, exact):
    rows = q_ref.shape[0]
    keys = kv_ref.shape[0] * (kv_ref.shape[1] // 2 if len(kv_ref.shape) == 3 else 1)
    first = pos_ref[0]
    query_pos = first + lax.broadcasted_iota(jnp.int32, (rows, keys), 0)
    key_pos = lax.broadcasted_iota(jnp.int32, (rows, keys), 1)
    allowed = key_pos <= query_pos
    if window is not None:
        allowed = allowed & (key_pos > query_pos - window)
    if len(kv_ref.shape) == 3:
        half = kv_ref.shape[1] // 2
        key = kv_ref[:, :half, :].reshape(-1, HD)
        value = kv_ref[:, half:, :].reshape(-1, HD)
    else:
        key = kv_ref[:, :HD]
        value = kv_ref[:, HD:]
    score_scale = 1.0 / math.sqrt(HD)
    contract = (((1,), (1,)), ((), ()))
    for head in range(q_ref.shape[1] // HD):
        query = q_ref[:, head * HD:(head + 1) * HD]
        if exact:
            q_hi, q_lo = _split(query.astype(jnp.float32))
            scores = lax.dot_general(q_hi, key, contract, preferred_element_type=jnp.float32)
            scores = scores + lax.dot_general(q_lo, key, contract, preferred_element_type=jnp.float32)
        else:
            scores = lax.dot_general(query, key, contract, preferred_element_type=jnp.float32)
        scores = scores * score_scale
        masked = jnp.where(allowed, scores, -jnp.inf)
        row_top = jnp.max(masked, axis=-1, keepdims=True)
        weights = jnp.where(allowed, jnp.exp(masked - row_top), 0.0)
        totals = jnp.sum(weights, axis=-1, keepdims=True)
        if exact:
            w_hi, w_lo = _split(weights)
            acc = jnp.dot(w_hi, value, preferred_element_type=jnp.float32)
            acc = acc + jnp.dot(w_lo, value, preferred_element_type=jnp.float32)
        else:
            acc = jnp.dot(weights.astype(jnp.bfloat16), value, preferred_element_type=jnp.float32)
        o_ref[:, head * HD:(head + 1) * HD] = (acc / totals).astype(o_ref.dtype)


def attend(first_pos, queries, pairs, window, exact, groups=None, offset=0):
    rows, qcols = queries.shape
    if groups is None:
        groups = pairs.shape[1] // (2 * HD)
        kv_spec = pl.BlockSpec((pairs.shape[0], 2 * HD), lambda g, pos: (0, g))
    else:
        kv_spec = pl.BlockSpec((pairs.shape[0], 2 * rows, HD), lambda g, pos: (0, offset + g, 0))
    qblock = qcols // groups
    kernel = functools.partial(_attend_kernel, window=window, exact=exact)
    return pl.pallas_call(
        kernel,
        out_shape=jax.ShapeDtypeStruct((rows, qcols), jnp.bfloat16),
        grid_spec=pltpu.PrefetchScalarGridSpec(
            num_scalar_prefetch=1,
            grid=(groups,),
            in_specs=[
                pl.BlockSpec((rows, qblock), lambda g, pos: (0, g)),
                kv_spec,
            ],
            out_specs=pl.BlockSpec((rows, qblock), lambda g, pos: (0, g)),
        ),
    )(first_pos, queries, pairs)


def _project_kernel(att_ref, w_ref, res_ref, o_ref, *, weight_rows):
    for part in range(o_ref.shape[1] // HD):
        weight = w_ref[:, part * weight_rows:(part + 1) * weight_rows, :].reshape(-1, HD)
        acc = jnp.dot(att_ref[...], weight, preferred_element_type=jnp.float32)
        cols = slice(part * HD, (part + 1) * HD)
        o_ref[:, cols] = (res_ref[:, cols].astype(jnp.float32) + acc).astype(o_ref.dtype)


def project(attended, slab, residual, weight_rows):
    rows, width = residual.shape
    blocks = width // HD
    per_step = next(n for n in (4, 3, 2, 1) if blocks % n == 0)
    return pl.pallas_call(
        functools.partial(_project_kernel, weight_rows=weight_rows),
        out_shape=jax.ShapeDtypeStruct((rows, width), jnp.bfloat16),
        grid=(blocks // per_step,),
        in_specs=[
            pl.BlockSpec(attended.shape, lambda c: (0, 0)),
            pl.BlockSpec((slab.shape[0], per_step * weight_rows, HD), lambda c: (0, c, 0)),
            pl.BlockSpec((rows, per_step * HD), lambda c: (0, c)),
        ],
        out_specs=pl.BlockSpec((rows, per_step * HD), lambda c: (0, c)),
    )(attended, slab, residual)


def _half_kernel(sel_ref, att_ref, w_ref, *refs, weight_rows):
    o_ref = refs[-1]
    for part in range(o_ref.shape[1] // HD):
        weight = w_ref[:, part * weight_rows:(part + 1) * weight_rows, :].reshape(-1, HD)
        acc = jnp.dot(att_ref[...], weight, preferred_element_type=jnp.float32)
        cols = slice(part * HD, (part + 1) * HD)
        for base_ref in refs[:-1]:
            acc = acc + base_ref[:, cols].astype(jnp.float32)
        o_ref[:, cols] = acc.astype(o_ref.dtype)


def project_half(which, attended, slab, bases, weight_rows, out_dtype, width):
    rows = attended.shape[0]
    blocks = width // HD
    per_step = next(n for n in (4, 3, 2, 1) if blocks % n == 0)
    devices = attended.shape[1] // weight_rows
    return pl.pallas_call(
        functools.partial(_half_kernel, weight_rows=weight_rows),
        out_shape=jax.ShapeDtypeStruct((rows, width), out_dtype),
        grid_spec=pltpu.PrefetchScalarGridSpec(
            num_scalar_prefetch=1,
            grid=(blocks // per_step,),
            in_specs=[
                pl.BlockSpec(attended.shape, lambda c, sel: (0, 0)),
                pl.BlockSpec((devices, per_step * weight_rows, HD), lambda c, sel: (sel[0], c, 0)),
            ]
            + [pl.BlockSpec((rows, per_step * HD), lambda c, sel: (0, c)) for _ in bases],
            out_specs=pl.BlockSpec((rows, per_step * HD), lambda c, sel: (0, c)),
        ),
    )(which, attended, slab, *bases)


def to_slab(x):
    rows, cols = x.shape
    return x.reshape(rows, cols // HD, HD).transpose(1, 0, 2).reshape(-1, HD)


def swap_heads(x):
    half = x.shape[1] // 2
    pieces = [
        lax.ppermute(x[:, :half], "heads", [(0, 1), (1, 0)]),
        lax.ppermute(x[:, half:], "heads", [(0, 1), (1, 0)]),
    ]
    return jnp.concatenate(pieces, axis=1)


def make_body(heads_count):
    def gather_heads(x):
        if heads_count == 2:
            other = swap_heads(x)
            first = lax.axis_index("heads") == 0
            low = jnp.where(first, x, other)
            high = jnp.where(first, other, x)
            return jnp.concatenate([low, high], axis=1)
        return lax.all_gather(x, "heads", axis=1, tiled=True)

    def body(
        residual_in,
        self_queries,
        self_keys_values,
        self_out_weight,
        gain_query,
        gain_keyvalue,
        cross_weight,
    ):
        tok_rows = residual_in.shape[0]
        groups = self_keys_values.shape[1] // (2 * HD)
        seq_place = lax.axis_index("seq")
        first_pos = (seq_place * tok_rows).astype(jnp.int32).reshape(1)

        weight_rows = self_out_weight.shape[0]
        weight_part = to_slab(self_out_weight)
        pad = (-weight_part.shape[0]) % (2 * tok_rows)
        weight_part = jnp.pad(weight_part, ((0, pad), (0, 0)))
        offset = weight_part.shape[0] // (2 * tok_rows)
        packed = jnp.concatenate([weight_part, to_slab(self_keys_values)], axis=0)
        slab = lax.all_gather(packed[None], "seq", axis=0, tiled=True)
        col_layout = cross_weight.reshape(cross_weight.shape[0], groups, QPK + 2, HD)
        weight_kv = col_layout[:, :, QPK:].reshape(cross_weight.shape[0], groups * 2 * HD)
        weight_q = col_layout[:, :, :QPK].reshape(cross_weight.shape[0], groups * QPK * HD)
        slab, weight_kv, weight_q = lax.optimization_barrier((slab, weight_kv, weight_q))
        attended = attend(first_pos, self_queries, slab, WINDOW, False, groups, offset)
        if heads_count == 2:
            place = lax.axis_index("heads")
            other = swap_heads(attended)
            width = residual_in.shape[1]
            own_part = project_half(
                place.astype(jnp.int32).reshape(1), attended, slab,
                [], weight_rows, jnp.float32, width,
            )
            hidden = project_half(
                (1 - place).astype(jnp.int32).reshape(1), other, slab,
                [own_part, residual_in], weight_rows, jnp.bfloat16, width,
            )
        else:
            hidden = project(gather_heads(attended), slab, residual_in, weight_rows)
        full_rows = gather_heads(hidden)
        widened = full_rows.astype(jnp.float32)
        inverse = lax.rsqrt(jnp.mean(widened * widened, axis=-1, keepdims=True) + 1e-06)
        normed_q = (widened * inverse * gain_query).astype(jnp.bfloat16)
        normed_kv = (widened * inverse * gain_keyvalue).astype(jnp.bfloat16)
        shared = jnp.dot(normed_kv, weight_kv, preferred_element_type=jnp.float32)
        shared_all = lax.all_gather(shared.astype(jnp.bfloat16), "seq", axis=0, tiled=True)
        cross_q = jnp.dot(normed_q, weight_q, preferred_element_type=jnp.float32)
        cross_attention = attend(first_pos, cross_q, shared_all, None, True)
        return (hidden, cross_attention)

    return body


def solution(mesh):
    return jax.shard_map(
        make_body(mesh.shape["heads"]),
        mesh=mesh,
        in_specs=(
            P("seq", "heads"),
            P("seq", "heads"),
            P("seq", "heads"),
            P("seq", "heads"),
            P(),
            P(),
            P(None, "heads"),
        ),
        out_specs=(P("seq", "heads"), P("seq", "heads")),
        check_vma=False,
    )
```

```python
import functools
import math

import jax
import jax.numpy as jnp
from jax import lax
from jax.experimental import pallas as pl
from jax.experimental.pallas import tpu as pltpu
from jax.sharding import PartitionSpec as P

HD = 128
QPK = 3
WINDOW = 2048


def _split(x):
    high = x.astype(jnp.bfloat16)
    low = (x - high.astype(jnp.float32)).astype(jnp.bfloat16)
    return high, low


def _attend_kernel(pos_ref, q_ref, kv_ref, o_ref, bias_ref, *, window, exact):
    rows, keys = bias_ref.shape

    @pl.when(pl.program_id(0) == 0)
    def _():
        query_pos = pos_ref[0] + lax.broadcasted_iota(jnp.int32, (rows, keys), 0)
        key_pos = lax.broadcasted_iota(jnp.int32, (rows, keys), 1)
        allowed = key_pos <= query_pos
        if window is not None:
            allowed = allowed & (key_pos > query_pos - window)
        bias_ref[...] = jnp.where(allowed, 0.0, -jnp.inf)

    if len(kv_ref.shape) == 3:
        half = kv_ref.shape[1] // 2
        key = kv_ref[:, :half, :].reshape(-1, HD)
        value = kv_ref[:, half:, :].reshape(-1, HD)
    else:
        key = kv_ref[:, :HD]
        value = kv_ref[:, HD:]
    score_scale = 1.0 / math.sqrt(HD)
    contract = (((1,), (1,)), ((), ()))
    for head in range(q_ref.shape[1] // HD):
        query = q_ref[:, head * HD:(head + 1) * HD]
        if exact:
            q_hi, q_lo = _split(query.astype(jnp.float32))
            scores = lax.dot_general(q_hi, key, contract, preferred_element_type=jnp.float32)
            scores = scores + lax.dot_general(q_lo, key, contract, preferred_element_type=jnp.float32)
        else:
            scores = lax.dot_general(query, key, contract, preferred_element_type=jnp.float32)
        masked = scores * score_scale + bias_ref[...]
        row_top = jnp.max(masked, axis=-1, keepdims=True)
        weights = jnp.exp(masked - row_top)
        totals = jnp.sum(weights, axis=-1, keepdims=True)
        if exact:
            w_hi, w_lo = _split(weights)
            acc = jnp.dot(w_hi, value, preferred_element_type=jnp.float32)
            acc = acc + jnp.dot(w_lo, value, preferred_element_type=jnp.float32)
        else:
            acc = jnp.dot(weights.astype(jnp.bfloat16), value, preferred_element_type=jnp.float32)
        o_ref[:, head * HD:(head + 1) * HD] = (acc / totals).astype(o_ref.dtype)


def attend(first_pos, queries, pairs, window, exact, groups=None, offset=0):
    rows, qcols = queries.shape
    if groups is None:
        groups = pairs.shape[1] // (2 * HD)
        kv_spec = pl.BlockSpec((pairs.shape[0], 2 * HD), lambda g, pos: (0, g))
    else:
        kv_spec = pl.BlockSpec((pairs.shape[0], 2 * rows, HD), lambda g, pos: (0, offset + g, 0))
    qblock = qcols // groups
    keys = pairs.shape[0] * (rows if pairs.ndim == 3 else 1)
    kernel = functools.partial(_attend_kernel, window=window, exact=exact)
    return pl.pallas_call(
        kernel,
        out_shape=jax.ShapeDtypeStruct((rows, qcols), jnp.bfloat16),
        grid_spec=pltpu.PrefetchScalarGridSpec(
            num_scalar_prefetch=1,
            grid=(groups,),
            in_specs=[
                pl.BlockSpec((rows, qblock), lambda g, pos: (0, g)),
                kv_spec,
            ],
            out_specs=pl.BlockSpec((rows, qblock), lambda g, pos: (0, g)),
            scratch_shapes=[pltpu.VMEM((rows, keys), jnp.float32)],
        ),
    )(first_pos, queries, pairs)


def _project_kernel(att_ref, w_ref, res_ref, o_ref, *, weight_rows):
    for part in range(o_ref.shape[1] // HD):
        weight = w_ref[:, part * weight_rows:(part + 1) * weight_rows, :].reshape(-1, HD)
        acc = jnp.dot(att_ref[...], weight, preferred_element_type=jnp.float32)
        cols = slice(part * HD, (part + 1) * HD)
        o_ref[:, cols] = (res_ref[:, cols].astype(jnp.float32) + acc).astype(o_ref.dtype)


def project(attended, slab, residual, weight_rows):
    rows, width = residual.shape
    blocks = width // HD
    per_step = next(n for n in (4, 3, 2, 1) if blocks % n == 0)
    return pl.pallas_call(
        functools.partial(_project_kernel, weight_rows=weight_rows),
        out_shape=jax.ShapeDtypeStruct((rows, width), jnp.bfloat16),
        grid=(blocks // per_step,),
        in_specs=[
            pl.BlockSpec(attended.shape, lambda c: (0, 0)),
            pl.BlockSpec((slab.shape[0], per_step * weight_rows, HD), lambda c: (0, c, 0)),
            pl.BlockSpec((rows, per_step * HD), lambda c: (0, c)),
        ],
        out_specs=pl.BlockSpec((rows, per_step * HD), lambda c: (0, c)),
    )(attended, slab, residual)


def _half_kernel(sel_ref, att_ref, w_ref, *refs, weight_rows):
    o_ref = refs[-1]
    for part in range(o_ref.shape[1] // HD):
        weight = w_ref[:, part * weight_rows:(part + 1) * weight_rows, :].reshape(-1, HD)
        acc = jnp.dot(att_ref[...], weight, preferred_element_type=jnp.float32)
        cols = slice(part * HD, (part + 1) * HD)
        for base_ref in refs[:-1]:
            acc = acc + base_ref[:, cols].astype(jnp.float32)
        o_ref[:, cols] = acc.astype(o_ref.dtype)


def project_half(which, attended, slab, bases, weight_rows, out_dtype, width):
    rows = attended.shape[0]
    blocks = width // HD
    per_step = next(n for n in (4, 3, 2, 1) if blocks % n == 0)
    devices = attended.shape[1] // weight_rows
    return pl.pallas_call(
        functools.partial(_half_kernel, weight_rows=weight_rows),
        out_shape=jax.ShapeDtypeStruct((rows, width), out_dtype),
        grid_spec=pltpu.PrefetchScalarGridSpec(
            num_scalar_prefetch=1,
            grid=(blocks // per_step,),
            in_specs=[
                pl.BlockSpec(attended.shape, lambda c, sel: (0, 0)),
                pl.BlockSpec((devices, per_step * weight_rows, HD), lambda c, sel: (sel[0], c, 0)),
            ]
            + [pl.BlockSpec((rows, per_step * HD), lambda c, sel: (0, c)) for _ in bases],
            out_specs=pl.BlockSpec((rows, per_step * HD), lambda c, sel: (0, c)),
        ),
    )(which, attended, slab, *bases)


def to_slab(x):
    rows, cols = x.shape
    return x.reshape(rows, cols // HD, HD).transpose(1, 0, 2).reshape(-1, HD)


def make_body(heads_count):
    def gather_heads(x):
        if heads_count == 2:
            other = lax.ppermute(x, "heads", [(0, 1), (1, 0)])
            first = lax.axis_index("heads") == 0
            low = jnp.where(first, x, other)
            high = jnp.where(first, other, x)
            return jnp.concatenate([low, high], axis=1)
        return lax.all_gather(x, "heads", axis=1, tiled=True)

    def body(
        residual_in,
        self_queries,
        self_keys_values,
        self_out_weight,
        gain_query,
        gain_keyvalue,
        cross_weight,
    ):
        tok_rows = residual_in.shape[0]
        groups = self_keys_values.shape[1] // (2 * HD)
        seq_place = lax.axis_index("seq")
        first_pos = (seq_place * tok_rows).astype(jnp.int32).reshape(1)

        weight_rows = self_out_weight.shape[0]
        weight_part = to_slab(self_out_weight)
        pad = (-weight_part.shape[0]) % (2 * tok_rows)
        weight_part = jnp.pad(weight_part, ((0, pad), (0, 0)))
        offset = weight_part.shape[0] // (2 * tok_rows)
        packed = jnp.concatenate([weight_part, to_slab(self_keys_values)], axis=0)
        slab = lax.all_gather(packed[None], "seq", axis=0, tiled=True)
        col_layout = cross_weight.reshape(cross_weight.shape[0], groups, QPK + 2, HD)
        weight_kv = col_layout[:, :, QPK:].reshape(cross_weight.shape[0], groups * 2 * HD)
        weight_q = col_layout[:, :, :QPK].reshape(cross_weight.shape[0], groups * QPK * HD)
        slab, weight_kv, weight_q = lax.optimization_barrier((slab, weight_kv, weight_q))
        attended = attend(first_pos, self_queries, slab, WINDOW, False, groups, offset)
        if heads_count == 2:
            place = lax.axis_index("heads")
            other = lax.ppermute(attended, "heads", [(0, 1), (1, 0)])
            width = residual_in.shape[1]
            own_part = project_half(
                place.astype(jnp.int32).reshape(1), attended, slab,
                [], weight_rows, jnp.float32, width,
            )
            hidden = project_half(
                (1 - place).astype(jnp.int32).reshape(1), other, slab,
                [own_part, residual_in], weight_rows, jnp.bfloat16, width,
            )
        else:
            hidden = project(gather_heads(attended), slab, residual_in, weight_rows)
        full_rows = gather_heads(hidden)
        widened = full_rows.astype(jnp.float32)
        inverse = lax.rsqrt(jnp.mean(widened * widened, axis=-1, keepdims=True) + 1e-06)
        normed_q = (widened * inverse * gain_query).astype(jnp.bfloat16)
        normed_kv = (widened * inverse * gain_keyvalue).astype(jnp.bfloat16)
        shared = jnp.dot(normed_kv, weight_kv, preferred_element_type=jnp.float32)
        shared_all = lax.all_gather(shared.astype(jnp.bfloat16), "seq", axis=0, tiled=True)
        cross_q = jnp.dot(normed_q, weight_q, preferred_element_type=jnp.float32)
        cross_attention = attend(first_pos, cross_q, shared_all, None, True)
        return (hidden, cross_attention)

    return body


def solution(mesh):
    return jax.shard_map(
        make_body(mesh.shape["heads"]),
        mesh=mesh,
        in_specs=(
            P("seq", "heads"),
            P("seq", "heads"),
            P("seq", "heads"),
            P("seq", "heads"),
            P(),
            P(),
            P(None, "heads"),
        ),
        out_specs=(P("seq", "heads"), P("seq", "heads")),
        check_vma=False,
    )
```

```python
import functools
import math

import jax
import jax.numpy as jnp
from jax import lax
from jax.experimental import pallas as pl
from jax.experimental.pallas import tpu as pltpu
from jax.sharding import PartitionSpec as P

HD = 128
QPK = 3
WINDOW = 2048


def _split(x):
    high = x.astype(jnp.bfloat16)
    low = (x - high.astype(jnp.float32)).astype(jnp.bfloat16)
    return high, low


def _attend_kernel(pos_ref, q_ref, kv_ref, o_ref, bias_ref, *, window, exact):
    rows, keys = bias_ref.shape

    @pl.when(pl.program_id(0) == 0)
    def _():
        query_pos = pos_ref[0] + lax.broadcasted_iota(jnp.int32, (rows, keys), 0)
        key_pos = lax.broadcasted_iota(jnp.int32, (rows, keys), 1)
        allowed = key_pos <= query_pos
        if window is not None:
            allowed = allowed & (key_pos > query_pos - window)
        bias_ref[...] = jnp.where(allowed, 0.0, -jnp.inf)

    if len(kv_ref.shape) == 3:
        half = kv_ref.shape[1] // 2
        key = kv_ref[:, :half, :].reshape(-1, HD)
        value = kv_ref[:, half:, :].reshape(-1, HD)
    else:
        key = kv_ref[:, :HD]
        value = kv_ref[:, HD:]
    score_scale = 1.0 / math.sqrt(HD)
    contract = (((1,), (1,)), ((), ()))
    for head in range(q_ref.shape[1] // HD):
        query = q_ref[:, head * HD:(head + 1) * HD]
        if exact:
            q_hi, q_lo = _split(query.astype(jnp.float32))
            scores = lax.dot_general(q_hi, key, contract, preferred_element_type=jnp.float32)
            scores = scores + lax.dot_general(q_lo, key, contract, preferred_element_type=jnp.float32)
        else:
            scores = lax.dot_general(query, key, contract, preferred_element_type=jnp.float32)
        masked = scores * score_scale + bias_ref[...]
        row_top = jnp.max(masked, axis=-1, keepdims=True)
        weights = jnp.exp(masked - row_top)
        totals = jnp.sum(weights, axis=-1, keepdims=True)
        acc = jnp.dot(weights.astype(jnp.bfloat16), value, preferred_element_type=jnp.float32)
        o_ref[:, head * HD:(head + 1) * HD] = (acc / totals).astype(o_ref.dtype)


def attend(first_pos, queries, pairs, window, exact, groups=None, offset=0):
    rows, qcols = queries.shape
    if groups is None:
        groups = pairs.shape[1] // (2 * HD)
        kv_spec = pl.BlockSpec((pairs.shape[0], 2 * HD), lambda g, pos: (0, g))
    else:
        kv_spec = pl.BlockSpec((pairs.shape[0], 2 * rows, HD), lambda g, pos: (0, offset + g, 0))
    qblock = qcols // groups
    keys = pairs.shape[0] * (rows if pairs.ndim == 3 else 1)
    kernel = functools.partial(_attend_kernel, window=window, exact=exact)
    return pl.pallas_call(
        kernel,
        out_shape=jax.ShapeDtypeStruct((rows, qcols), jnp.bfloat16),
        grid_spec=pltpu.PrefetchScalarGridSpec(
            num_scalar_prefetch=1,
            grid=(groups,),
            in_specs=[
                pl.BlockSpec((rows, qblock), lambda g, pos: (0, g)),
                kv_spec,
            ],
            out_specs=pl.BlockSpec((rows, qblock), lambda g, pos: (0, g)),
            scratch_shapes=[pltpu.VMEM((rows, keys), jnp.float32)],
        ),
    )(first_pos, queries, pairs)


def _project_kernel(att_ref, w_ref, res_ref, o_ref, *, weight_rows):
    for part in range(o_ref.shape[1] // HD):
        weight = w_ref[:, part * weight_rows:(part + 1) * weight_rows, :].reshape(-1, HD)
        acc = jnp.dot(att_ref[...], weight, preferred_element_type=jnp.float32)
        cols = slice(part * HD, (part + 1) * HD)
        o_ref[:, cols] = (res_ref[:, cols].astype(jnp.float32) + acc).astype(o_ref.dtype)


def project(attended, slab, residual, weight_rows):
    rows, width = residual.shape
    blocks = width // HD
    per_step = next(n for n in (4, 3, 2, 1) if blocks % n == 0)
    return pl.pallas_call(
        functools.partial(_project_kernel, weight_rows=weight_rows),
        out_shape=jax.ShapeDtypeStruct((rows, width), jnp.bfloat16),
        grid=(blocks // per_step,),
        in_specs=[
            pl.BlockSpec(attended.shape, lambda c: (0, 0)),
            pl.BlockSpec((slab.shape[0], per_step * weight_rows, HD), lambda c: (0, c, 0)),
            pl.BlockSpec((rows, per_step * HD), lambda c: (0, c)),
        ],
        out_specs=pl.BlockSpec((rows, per_step * HD), lambda c: (0, c)),
    )(attended, slab, residual)


def _half_kernel(sel_ref, att_ref, w_ref, *refs, weight_rows):
    o_ref = refs[-1]
    for part in range(o_ref.shape[1] // HD):
        weight = w_ref[:, part * weight_rows:(part + 1) * weight_rows, :].reshape(-1, HD)
        acc = jnp.dot(att_ref[...], weight, preferred_element_type=jnp.float32)
        cols = slice(part * HD, (part + 1) * HD)
        for base_ref in refs[:-1]:
            acc = acc + base_ref[:, cols].astype(jnp.float32)
        o_ref[:, cols] = acc.astype(o_ref.dtype)


def project_half(which, attended, slab, bases, weight_rows, out_dtype, width):
    rows = attended.shape[0]
    blocks = width // HD
    per_step = next(n for n in (4, 3, 2, 1) if blocks % n == 0)
    devices = attended.shape[1] // weight_rows
    return pl.pallas_call(
        functools.partial(_half_kernel, weight_rows=weight_rows),
        out_shape=jax.ShapeDtypeStruct((rows, width), out_dtype),
        grid_spec=pltpu.PrefetchScalarGridSpec(
            num_scalar_prefetch=1,
            grid=(blocks // per_step,),
            in_specs=[
                pl.BlockSpec(attended.shape, lambda c, sel: (0, 0)),
                pl.BlockSpec((devices, per_step * weight_rows, HD), lambda c, sel: (sel[0], c, 0)),
            ]
            + [pl.BlockSpec((rows, per_step * HD), lambda c, sel: (0, c)) for _ in bases],
            out_specs=pl.BlockSpec((rows, per_step * HD), lambda c, sel: (0, c)),
        ),
    )(which, attended, slab, *bases)


def to_slab(x):
    rows, cols = x.shape
    return x.reshape(rows, cols // HD, HD).transpose(1, 0, 2).reshape(-1, HD)


def make_body(heads_count):
    def gather_heads(x):
        if heads_count == 2:
            other = lax.ppermute(x, "heads", [(0, 1), (1, 0)])
            first = lax.axis_index("heads") == 0
            low = jnp.where(first, x, other)
            high = jnp.where(first, other, x)
            return jnp.concatenate([low, high], axis=1)
        return lax.all_gather(x, "heads", axis=1, tiled=True)

    def body(
        residual_in,
        self_queries,
        self_keys_values,
        self_out_weight,
        gain_query,
        gain_keyvalue,
        cross_weight,
    ):
        tok_rows = residual_in.shape[0]
        groups = self_keys_values.shape[1] // (2 * HD)
        seq_place = lax.axis_index("seq")
        first_pos = (seq_place * tok_rows).astype(jnp.int32).reshape(1)

        weight_rows = self_out_weight.shape[0]
        weight_part = to_slab(self_out_weight)
        pad = (-weight_part.shape[0]) % (2 * tok_rows)
        weight_part = jnp.pad(weight_part, ((0, pad), (0, 0)))
        offset = weight_part.shape[0] // (2 * tok_rows)
        packed = jnp.concatenate([weight_part, to_slab(self_keys_values)], axis=0)
        slab = lax.all_gather(packed[None], "seq", axis=0, tiled=True)
        col_layout = cross_weight.reshape(cross_weight.shape[0], groups, QPK + 2, HD)
        weight_kv = col_layout[:, :, QPK:].reshape(cross_weight.shape[0], groups * 2 * HD)
        weight_q = col_layout[:, :, :QPK].reshape(cross_weight.shape[0], groups * QPK * HD)
        slab, weight_kv, weight_q = lax.optimization_barrier((slab, weight_kv, weight_q))
        attended = attend(first_pos, self_queries, slab, WINDOW, False, groups, offset)
        if heads_count == 2:
            place = lax.axis_index("heads")
            other = lax.ppermute(attended, "heads", [(0, 1), (1, 0)])
            width = residual_in.shape[1]
            own_part = project_half(
                place.astype(jnp.int32).reshape(1), attended, slab,
                [], weight_rows, jnp.float32, width,
            )
            hidden = project_half(
                (1 - place).astype(jnp.int32).reshape(1), other, slab,
                [own_part, residual_in], weight_rows, jnp.bfloat16, width,
            )
        else:
            hidden = project(gather_heads(attended), slab, residual_in, weight_rows)
        full_rows = gather_heads(hidden)
        widened = full_rows.astype(jnp.float32)
        inverse = lax.rsqrt(jnp.mean(widened * widened, axis=-1, keepdims=True) + 1e-06)
        normed_q = (widened * inverse * gain_query).astype(jnp.bfloat16)
        normed_kv = (widened * inverse * gain_keyvalue).astype(jnp.bfloat16)
        shared = jnp.dot(normed_kv, weight_kv, preferred_element_type=jnp.float32)
        shared_all = lax.all_gather(shared.astype(jnp.bfloat16), "seq", axis=0, tiled=True)
        cross_q = jnp.dot(normed_q, weight_q, preferred_element_type=jnp.float32)
        cross_attention = attend(first_pos, cross_q, shared_all, None, True)
        return (hidden, cross_attention)

    return body


def solution(mesh):
    return jax.shard_map(
        make_body(mesh.shape["heads"]),
        mesh=mesh,
        in_specs=(
            P("seq", "heads"),
            P("seq", "heads"),
            P("seq", "heads"),
            P("seq", "heads"),
            P(),
            P(),
            P(None, "heads"),
        ),
        out_specs=(P("seq", "heads"), P("seq", "heads")),
        check_vma=False,
    )
```

```python
import functools
import math

import jax
import jax.numpy as jnp
from jax import lax
from jax.experimental import pallas as pl
from jax.experimental.pallas import tpu as pltpu
from jax.sharding import PartitionSpec as P

HD = 128
QPK = 3
WINDOW = 2048


def _split(x):
    high = x.astype(jnp.bfloat16)
    low = (x - high.astype(jnp.float32)).astype(jnp.bfloat16)
    return high, low


def _attend_kernel(pos_ref, q_ref, kv_ref, o_ref, bias_ref, *, window, exact):
    rows, keys = bias_ref.shape

    @pl.when(pl.program_id(0) == 0)
    def _():
        query_pos = pos_ref[0] + lax.broadcasted_iota(jnp.int32, (rows, keys), 0)
        key_pos = lax.broadcasted_iota(jnp.int32, (rows, keys), 1)
        allowed = key_pos <= query_pos
        if window is not None:
            allowed = allowed & (key_pos > query_pos - window)
        bias_ref[...] = jnp.where(allowed, 0.0, -jnp.inf)

    if len(kv_ref.shape) == 3:
        half = kv_ref.shape[1] // 2
        key = kv_ref[:, :half, :].reshape(-1, HD)
        value = kv_ref[:, half:, :].reshape(-1, HD)
    else:
        key = kv_ref[:, :HD]
        value = kv_ref[:, HD:]
    score_scale = 1.0 / math.sqrt(HD)
    contract = (((1,), (1,)), ((), ()))
    for head in range(q_ref.shape[1] // HD):
        query = q_ref[:, head * HD:(head + 1) * HD]
        if exact:
            q_hi, q_lo = _split(query.astype(jnp.float32))
            scores = lax.dot_general(q_hi, key, contract, preferred_element_type=jnp.float32)
            scores = scores + lax.dot_general(q_lo, key, contract, preferred_element_type=jnp.float32)
        else:
            scores = lax.dot_general(query, key, contract, preferred_element_type=jnp.float32)
        masked = scores * score_scale + bias_ref[...]
        row_top = jnp.max(masked, axis=-1, keepdims=True)
        weights = jnp.exp(masked - row_top)
        totals = jnp.sum(weights, axis=-1, keepdims=True)
        acc = jnp.dot(weights.astype(jnp.bfloat16), value, preferred_element_type=jnp.float32)
        o_ref[:, head * HD:(head + 1) * HD] = (acc / totals).astype(o_ref.dtype)


def attend(first_pos, queries, pairs, window, exact, groups=None, offset=0):
    rows, qcols = queries.shape
    if groups is None:
        groups = pairs.shape[1] // (2 * HD)
        kv_spec = pl.BlockSpec((pairs.shape[0], 2 * HD), lambda g, pos: (0, g))
    else:
        kv_spec = pl.BlockSpec((pairs.shape[0], 2 * rows, HD), lambda g, pos: (0, offset + g, 0))
    qblock = qcols // groups
    keys = pairs.shape[0] * (rows if pairs.ndim == 3 else 1)
    kernel = functools.partial(_attend_kernel, window=window, exact=exact)
    return pl.pallas_call(
        kernel,
        out_shape=jax.ShapeDtypeStruct((rows, qcols), jnp.bfloat16),
        grid_spec=pltpu.PrefetchScalarGridSpec(
            num_scalar_prefetch=1,
            grid=(groups,),
            in_specs=[
                pl.BlockSpec((rows, qblock), lambda g, pos: (0, g)),
                kv_spec,
            ],
            out_specs=pl.BlockSpec((rows, qblock), lambda g, pos: (0, g)),
            scratch_shapes=[pltpu.VMEM((rows, keys), jnp.float32)],
        ),
    )(first_pos, queries, pairs)


def _project_kernel(att_ref, w_ref, res_ref, o_ref, *, weight_rows):
    for part in range(o_ref.shape[1] // HD):
        weight = w_ref[:, part * weight_rows:(part + 1) * weight_rows, :].reshape(-1, HD)
        acc = jnp.dot(att_ref[...], weight, preferred_element_type=jnp.float32)
        cols = slice(part * HD, (part + 1) * HD)
        o_ref[:, cols] = (res_ref[:, cols].astype(jnp.float32) + acc).astype(o_ref.dtype)


def project(attended, slab, residual, weight_rows):
    rows, width = residual.shape
    blocks = width // HD
    per_step = next(n for n in (4, 3, 2, 1) if blocks % n == 0)
    return pl.pallas_call(
        functools.partial(_project_kernel, weight_rows=weight_rows),
        out_shape=jax.ShapeDtypeStruct((rows, width), jnp.bfloat16),
        grid=(blocks // per_step,),
        in_specs=[
            pl.BlockSpec(attended.shape, lambda c: (0, 0)),
            pl.BlockSpec((slab.shape[0], per_step * weight_rows, HD), lambda c: (0, c, 0)),
            pl.BlockSpec((rows, per_step * HD), lambda c: (0, c)),
        ],
        out_specs=pl.BlockSpec((rows, per_step * HD), lambda c: (0, c)),
    )(attended, slab, residual)


def _half_kernel(sel_ref, att_ref, w_ref, *refs, weight_rows):
    o_ref = refs[-1]
    for part in range(o_ref.shape[1] // HD):
        weight = w_ref[:, part * weight_rows:(part + 1) * weight_rows, :].reshape(-1, HD)
        acc = jnp.dot(att_ref[...], weight, preferred_element_type=jnp.float32)
        cols = slice(part * HD, (part + 1) * HD)
        for base_ref in refs[:-1]:
            acc = acc + base_ref[:, cols].astype(jnp.float32)
        o_ref[:, cols] = acc.astype(o_ref.dtype)


def project_half(which, attended, slab, bases, weight_rows, out_dtype, width):
    rows = attended.shape[0]
    blocks = width // HD
    per_step = next(n for n in (4, 3, 2, 1) if blocks % n == 0)
    devices = attended.shape[1] // weight_rows
    return pl.pallas_call(
        functools.partial(_half_kernel, weight_rows=weight_rows),
        out_shape=jax.ShapeDtypeStruct((rows, width), out_dtype),
        grid_spec=pltpu.PrefetchScalarGridSpec(
            num_scalar_prefetch=1,
            grid=(blocks // per_step,),
            in_specs=[
                pl.BlockSpec(attended.shape, lambda c, sel: (0, 0)),
                pl.BlockSpec((devices, per_step * weight_rows, HD), lambda c, sel: (sel[0], c, 0)),
            ]
            + [pl.BlockSpec((rows, per_step * HD), lambda c, sel: (0, c)) for _ in bases],
            out_specs=pl.BlockSpec((rows, per_step * HD), lambda c, sel: (0, c)),
        ),
    )(which, attended, slab, *bases)


def to_slab(x):
    rows, cols = x.shape
    return x.reshape(rows, cols // HD, HD).transpose(1, 0, 2).reshape(-1, HD)


def make_body(heads_count):
    def gather_heads(x):
        if heads_count == 2:
            other = lax.ppermute(x, "heads", [(0, 1), (1, 0)])
            first = lax.axis_index("heads") == 0
            low = jnp.where(first, x, other)
            high = jnp.where(first, other, x)
            return jnp.concatenate([low, high], axis=1)
        return lax.all_gather(x, "heads", axis=1, tiled=True)

    def body(
        residual_in,
        self_queries,
        self_keys_values,
        self_out_weight,
        gain_query,
        gain_keyvalue,
        cross_weight,
    ):
        tok_rows = residual_in.shape[0]
        groups = self_keys_values.shape[1] // (2 * HD)
        seq_place = lax.axis_index("seq")
        first_pos = (seq_place * tok_rows).astype(jnp.int32).reshape(1)

        weight_rows = self_out_weight.shape[0]
        weight_part = to_slab(self_out_weight)
        pad = (-weight_part.shape[0]) % (2 * tok_rows)
        weight_part = jnp.pad(weight_part, ((0, pad), (0, 0)))
        offset = weight_part.shape[0] // (2 * tok_rows)
        packed = jnp.concatenate([weight_part, to_slab(self_keys_values)], axis=0)
        slab = lax.all_gather(packed[None], "seq", axis=0, tiled=True)
        col_layout = cross_weight.reshape(cross_weight.shape[0], groups, QPK + 2, HD)
        weight_kv = col_layout[:, :, QPK:].reshape(cross_weight.shape[0], groups * 2 * HD)
        weight_q = col_layout[:, :, :QPK].reshape(cross_weight.shape[0], groups * QPK * HD)
        if heads_count == 2:
            place = lax.axis_index("heads")
            feats = residual_in.shape[1]
            halves = [place * feats, (1 - place) * feats]
            weight_kv = [lax.dynamic_slice_in_dim(weight_kv, at, feats, 0) for at in halves]
            weight_q = [lax.dynamic_slice_in_dim(weight_q, at, feats, 0) for at in halves]
            gains_kv = [lax.dynamic_slice_in_dim(gain_keyvalue, at, feats, 0) for at in halves]
            gains_q = [lax.dynamic_slice_in_dim(gain_query, at, feats, 0) for at in halves]
        slab, weight_kv, weight_q = lax.optimization_barrier((slab, weight_kv, weight_q))
        attended = attend(first_pos, self_queries, slab, WINDOW, False, groups, offset)
        if heads_count == 2:
            place = lax.axis_index("heads")
            other = lax.ppermute(attended, "heads", [(0, 1), (1, 0)])
            width = residual_in.shape[1]
            own_part = project_half(
                place.astype(jnp.int32).reshape(1), attended, slab,
                [], weight_rows, jnp.float32, width,
            )
            hidden = project_half(
                (1 - place).astype(jnp.int32).reshape(1), other, slab,
                [own_part, residual_in], weight_rows, jnp.bfloat16, width,
            )
        else:
            hidden = project(gather_heads(attended), slab, residual_in, weight_rows)
        if heads_count == 2:
            own = hidden.astype(jnp.float32)
            own_squares = jnp.sum(own * own, axis=-1, keepdims=True)
            other_squares = lax.ppermute(own_squares, "heads", [(0, 1), (1, 0)])
            other = lax.ppermute(hidden, "heads", [(0, 1), (1, 0)]).astype(jnp.float32)
            mean = (own_squares + other_squares) / (2 * own.shape[1])
            inverse = lax.rsqrt(mean + 1e-06)
            shared = jnp.dot(
                (own * inverse * gains_kv[0]).astype(jnp.bfloat16), weight_kv[0],
                preferred_element_type=jnp.float32,
            ) + jnp.dot(
                (other * inverse * gains_kv[1]).astype(jnp.bfloat16), weight_kv[1],
                preferred_element_type=jnp.float32,
            )
            shared_all = lax.all_gather(shared.astype(jnp.bfloat16), "seq", axis=0, tiled=True)
            cross_q = jnp.dot(
                (own * inverse * gains_q[0]).astype(jnp.bfloat16), weight_q[0],
                preferred_element_type=jnp.float32,
            ) + jnp.dot(
                (other * inverse * gains_q[1]).astype(jnp.bfloat16), weight_q[1],
                preferred_element_type=jnp.float32,
            )
        else:
            full_rows = gather_heads(hidden)
            widened = full_rows.astype(jnp.float32)
            inverse = lax.rsqrt(jnp.mean(widened * widened, axis=-1, keepdims=True) + 1e-06)
            normed_q = (widened * inverse * gain_query).astype(jnp.bfloat16)
            normed_kv = (widened * inverse * gain_keyvalue).astype(jnp.bfloat16)
            shared = jnp.dot(normed_kv, weight_kv, preferred_element_type=jnp.float32)
            shared_all = lax.all_gather(shared.astype(jnp.bfloat16), "seq", axis=0, tiled=True)
            cross_q = jnp.dot(normed_q, weight_q, preferred_element_type=jnp.float32)
        cross_attention = attend(first_pos, cross_q, shared_all, None, True)
        return (hidden, cross_attention)

    return body


def solution(mesh):
    return jax.shard_map(
        make_body(mesh.shape["heads"]),
        mesh=mesh,
        in_specs=(
            P("seq", "heads"),
            P("seq", "heads"),
            P("seq", "heads"),
            P("seq", "heads"),
            P(),
            P(),
            P(None, "heads"),
        ),
        out_specs=(P("seq", "heads"), P("seq", "heads")),
        check_vma=False,
    )
```

```python
import functools
import math

import jax
import jax.numpy as jnp
from jax import lax
from jax.experimental import pallas as pl
from jax.experimental.pallas import tpu as pltpu
from jax.sharding import PartitionSpec as P

HD = 128
QPK = 3
WINDOW = 2048


def _split(x):
    high = x.astype(jnp.bfloat16)
    low = (x - high.astype(jnp.float32)).astype(jnp.bfloat16)
    return high, low


def _attend_kernel(pos_ref, q_ref, kv_ref, o_ref, bias_ref, *, window, exact):
    rows, keys = bias_ref.shape

    @pl.when(pl.program_id(0) == 0)
    def _():
        query_pos = pos_ref[0] + lax.broadcasted_iota(jnp.int32, (rows, keys), 0)
        key_pos = lax.broadcasted_iota(jnp.int32, (rows, keys), 1)
        allowed = key_pos <= query_pos
        if window is not None:
            allowed = allowed & (key_pos > query_pos - window)
        bias_ref[...] = jnp.where(allowed, 0.0, -jnp.inf)

    if len(kv_ref.shape) == 3:
        half = kv_ref.shape[1] // 2
        key = kv_ref[:, :half, :].reshape(-1, HD)
        value = kv_ref[:, half:, :].reshape(-1, HD)
    else:
        key = kv_ref[:, :HD]
        value = kv_ref[:, HD:]
    score_scale = 1.0 / math.sqrt(HD)
    contract = (((1,), (1,)), ((), ()))
    for head in range(q_ref.shape[1] // HD):
        query = q_ref[:, head * HD:(head + 1) * HD]
        if exact:
            q_hi, q_lo = _split(query.astype(jnp.float32))
            scores = lax.dot_general(q_hi, key, contract, preferred_element_type=jnp.float32)
            scores = scores + lax.dot_general(q_lo, key, contract, preferred_element_type=jnp.float32)
        else:
            scores = lax.dot_general(query, key, contract, preferred_element_type=jnp.float32)
        masked = scores * score_scale + bias_ref[...]
        row_top = jnp.max(masked, axis=-1, keepdims=True)
        weights = jnp.exp(masked - row_top)
        totals = jnp.sum(weights, axis=-1, keepdims=True)
        acc = jnp.dot(weights.astype(jnp.bfloat16), value, preferred_element_type=jnp.float32)
        o_ref[:, head * HD:(head + 1) * HD] = (acc / totals).astype(o_ref.dtype)


def attend(first_pos, queries, pairs, window, exact, groups=None, offset=0, first=0, count=None):
    rows, qcols = queries.shape
    if groups is None:
        groups = pairs.shape[1] // (2 * HD)
        kv_spec = pl.BlockSpec((pairs.shape[0], 2 * HD), lambda g, pos: (0, first + g))
    else:
        kv_spec = pl.BlockSpec(
            (pairs.shape[0], 2 * rows, HD), lambda g, pos: (0, offset + first + g, 0)
        )
    qblock = qcols // groups
    count = groups - first if count is None else count
    keys = pairs.shape[0] * (rows if pairs.ndim == 3 else 1)
    kernel = functools.partial(_attend_kernel, window=window, exact=exact)
    return pl.pallas_call(
        kernel,
        out_shape=jax.ShapeDtypeStruct((rows, count * qblock), jnp.bfloat16),
        grid_spec=pltpu.PrefetchScalarGridSpec(
            num_scalar_prefetch=1,
            grid=(count,),
            in_specs=[
                pl.BlockSpec((rows, qblock), lambda g, pos: (0, first + g)),
                kv_spec,
            ],
            out_specs=pl.BlockSpec((rows, qblock), lambda g, pos: (0, g)),
            scratch_shapes=[pltpu.VMEM((rows, keys), jnp.float32)],
        ),
    )(first_pos, queries, pairs)


def _project_kernel(att_ref, w_ref, res_ref, o_ref, *, weight_rows):
    for part in range(o_ref.shape[1] // HD):
        weight = w_ref[:, part * weight_rows:(part + 1) * weight_rows, :].reshape(-1, HD)
        acc = jnp.dot(att_ref[...], weight, preferred_element_type=jnp.float32)
        cols = slice(part * HD, (part + 1) * HD)
        o_ref[:, cols] = (res_ref[:, cols].astype(jnp.float32) + acc).astype(o_ref.dtype)


def project(attended, slab, residual, weight_rows):
    rows, width = residual.shape
    blocks = width // HD
    per_step = next(n for n in (4, 3, 2, 1) if blocks % n == 0)
    return pl.pallas_call(
        functools.partial(_project_kernel, weight_rows=weight_rows),
        out_shape=jax.ShapeDtypeStruct((rows, width), jnp.bfloat16),
        grid=(blocks // per_step,),
        in_specs=[
            pl.BlockSpec(attended.shape, lambda c: (0, 0)),
            pl.BlockSpec((slab.shape[0], per_step * weight_rows, HD), lambda c: (0, c, 0)),
            pl.BlockSpec((rows, per_step * HD), lambda c: (0, c)),
        ],
        out_specs=pl.BlockSpec((rows, per_step * HD), lambda c: (0, c)),
    )(attended, slab, residual)


def _half_kernel(sel_ref, att_ref, w_ref, *refs, weight_rows):
    o_ref = refs[-1]
    for part in range(o_ref.shape[1] // HD):
        weight = w_ref[:, part * weight_rows:(part + 1) * weight_rows, :].reshape(-1, HD)
        acc = jnp.dot(att_ref[...], weight, preferred_element_type=jnp.float32)
        cols = slice(part * HD, (part + 1) * HD)
        for base_ref in refs[:-1]:
            acc = acc + base_ref[:, cols].astype(jnp.float32)
        o_ref[:, cols] = acc.astype(o_ref.dtype)


def project_half(which, attended, slab, bases, weight_rows, out_dtype, width):
    rows = attended.shape[0]
    blocks = width // HD
    per_step = next(n for n in (4, 3, 2, 1) if blocks % n == 0)
    devices = attended.shape[1] // weight_rows
    return pl.pallas_call(
        functools.partial(_half_kernel, weight_rows=weight_rows),
        out_shape=jax.ShapeDtypeStruct((rows, width), out_dtype),
        grid_spec=pltpu.PrefetchScalarGridSpec(
            num_scalar_prefetch=1,
            grid=(blocks // per_step,),
            in_specs=[
                pl.BlockSpec(attended.shape, lambda c, sel: (0, 0)),
                pl.BlockSpec((devices, per_step * weight_rows, HD), lambda c, sel: (sel[0], c, 0)),
            ]
            + [pl.BlockSpec((rows, per_step * HD), lambda c, sel: (0, c)) for _ in bases],
            out_specs=pl.BlockSpec((rows, per_step * HD), lambda c, sel: (0, c)),
        ),
    )(which, attended, slab, *bases)


def to_slab(x):
    rows, cols = x.shape
    return x.reshape(rows, cols // HD, HD).transpose(1, 0, 2).reshape(-1, HD)


def make_body(heads_count):
    def gather_heads(x):
        if heads_count == 2:
            other = lax.ppermute(x, "heads", [(0, 1), (1, 0)])
            first = lax.axis_index("heads") == 0
            low = jnp.where(first, x, other)
            high = jnp.where(first, other, x)
            return jnp.concatenate([low, high], axis=1)
        return lax.all_gather(x, "heads", axis=1, tiled=True)

    def body(
        residual_in,
        self_queries,
        self_keys_values,
        self_out_weight,
        gain_query,
        gain_keyvalue,
        cross_weight,
    ):
        tok_rows = residual_in.shape[0]
        groups = self_keys_values.shape[1] // (2 * HD)
        seq_place = lax.axis_index("seq")
        first_pos = (seq_place * tok_rows).astype(jnp.int32).reshape(1)

        weight_rows = self_out_weight.shape[0]
        weight_part = to_slab(self_out_weight)
        pad = (-weight_part.shape[0]) % (2 * tok_rows)
        weight_part = jnp.pad(weight_part, ((0, pad), (0, 0)))
        offset = weight_part.shape[0] // (2 * tok_rows)
        packed = jnp.concatenate([weight_part, to_slab(self_keys_values)], axis=0)
        slab = lax.all_gather(packed[None], "seq", axis=0, tiled=True)
        col_layout = cross_weight.reshape(cross_weight.shape[0], groups, QPK + 2, HD)
        weight_kv = col_layout[:, :, QPK:].reshape(cross_weight.shape[0], groups * 2 * HD)
        weight_q = col_layout[:, :, :QPK].reshape(cross_weight.shape[0], groups * QPK * HD)
        if heads_count == 2:
            place = lax.axis_index("heads")
            feats = residual_in.shape[1]
            halves = [place * feats, (1 - place) * feats]
            weight_kv = [lax.dynamic_slice_in_dim(weight_kv, at, feats, 0) for at in halves]
            weight_q = [lax.dynamic_slice_in_dim(weight_q, at, feats, 0) for at in halves]
            gains_kv = [lax.dynamic_slice_in_dim(gain_keyvalue, at, feats, 0) for at in halves]
            gains_q = [lax.dynamic_slice_in_dim(gain_query, at, feats, 0) for at in halves]
        slab, weight_kv, weight_q = lax.optimization_barrier((slab, weight_kv, weight_q))
        if heads_count == 2 and groups % 2 == 0:
            pieces = [
                attend(first_pos, self_queries, slab, WINDOW, False, groups, offset, at, groups // 2)
                for at in (0, groups // 2)
            ]
            first_other = lax.ppermute(pieces[0], "heads", [(0, 1), (1, 0)])
            second, first_other = lax.optimization_barrier((pieces[1], first_other))
            others = [first_other, lax.ppermute(second, "heads", [(0, 1), (1, 0)])]
            attended = jnp.concatenate(pieces, axis=1)
        else:
            attended = attend(first_pos, self_queries, slab, WINDOW, False, groups, offset)
        if heads_count == 2:
            place = lax.axis_index("heads")
            if groups % 2 == 0:
                other = jnp.concatenate(others, axis=1)
            else:
                other = lax.ppermute(attended, "heads", [(0, 1), (1, 0)])
            width = residual_in.shape[1]
            own_part = project_half(
                place.astype(jnp.int32).reshape(1), attended, slab,
                [], weight_rows, jnp.float32, width,
            )
            hidden = project_half(
                (1 - place).astype(jnp.int32).reshape(1), other, slab,
                [own_part, residual_in], weight_rows, jnp.bfloat16, width,
            )
        else:
            hidden = project(gather_heads(attended), slab, residual_in, weight_rows)
        if heads_count == 2:
            own = hidden.astype(jnp.float32)
            own_squares = jnp.sum(own * own, axis=-1, keepdims=True)
            other_squares = lax.ppermute(own_squares, "heads", [(0, 1), (1, 0)])
            other = lax.ppermute(hidden, "heads", [(0, 1), (1, 0)]).astype(jnp.float32)
            mean = (own_squares + other_squares) / (2 * own.shape[1])
            inverse = lax.rsqrt(mean + 1e-06)
            shared = jnp.dot(
                (own * inverse * gains_kv[0]).astype(jnp.bfloat16), weight_kv[0],
                preferred_element_type=jnp.float32,
            ) + jnp.dot(
                (other * inverse * gains_kv[1]).astype(jnp.bfloat16), weight_kv[1],
                preferred_element_type=jnp.float32,
            )
            shared_all = lax.all_gather(shared.astype(jnp.bfloat16), "seq", axis=0, tiled=True)
            cross_q = jnp.dot(
                (own * inverse * gains_q[0]).astype(jnp.bfloat16), weight_q[0],
                preferred_element_type=jnp.float32,
            ) + jnp.dot(
                (other * inverse * gains_q[1]).astype(jnp.bfloat16), weight_q[1],
                preferred_element_type=jnp.float32,
            )
        else:
            full_rows = gather_heads(hidden)
            widened = full_rows.astype(jnp.float32)
            inverse = lax.rsqrt(jnp.mean(widened * widened, axis=-1, keepdims=True) + 1e-06)
            normed_q = (widened * inverse * gain_query).astype(jnp.bfloat16)
            normed_kv = (widened * inverse * gain_keyvalue).astype(jnp.bfloat16)
            shared = jnp.dot(normed_kv, weight_kv, preferred_element_type=jnp.float32)
            shared_all = lax.all_gather(shared.astype(jnp.bfloat16), "seq", axis=0, tiled=True)
            cross_q = jnp.dot(normed_q, weight_q, preferred_element_type=jnp.float32)
        cross_attention = attend(first_pos, cross_q, shared_all, None, True)
        return (hidden, cross_attention)

    return body


def solution(mesh):
    return jax.shard_map(
        make_body(mesh.shape["heads"]),
        mesh=mesh,
        in_specs=(
            P("seq", "heads"),
            P("seq", "heads"),
            P("seq", "heads"),
            P("seq", "heads"),
            P(),
            P(),
            P(None, "heads"),
        ),
        out_specs=(P("seq", "heads"), P("seq", "heads")),
        check_vma=False,
    )
```

```python
import functools
import math

import jax
import jax.numpy as jnp
from jax import lax
from jax.experimental import pallas as pl
from jax.experimental.pallas import tpu as pltpu
from jax.sharding import PartitionSpec as P

HD = 128
QPK = 3
WINDOW = 2048


def _split(x):
    high = x.astype(jnp.bfloat16)
    low = (x - high.astype(jnp.float32)).astype(jnp.bfloat16)
    return high, low


def _attend_kernel(pos_ref, q_ref, kv_ref, o_ref, bias_ref, *, window, exact):
    rows, keys = bias_ref.shape

    @pl.when(pl.program_id(0) == 0)
    def _():
        query_pos = pos_ref[0] + lax.broadcasted_iota(jnp.int32, (rows, keys), 0)
        key_pos = lax.broadcasted_iota(jnp.int32, (rows, keys), 1)
        allowed = key_pos <= query_pos
        if window is not None:
            allowed = allowed & (key_pos > query_pos - window)
        bias_ref[...] = jnp.where(allowed, 0.0, -jnp.inf)

    if len(kv_ref.shape) == 3:
        half = kv_ref.shape[1] // 2
        key = kv_ref[:, :half, :].reshape(-1, HD)
        value = kv_ref[:, half:, :].reshape(-1, HD)
    else:
        key = kv_ref[:, :HD]
        value = kv_ref[:, HD:]
    score_scale = 1.0 / math.sqrt(HD)
    contract = (((1,), (1,)), ((), ()))
    for head in range(q_ref.shape[1] // HD):
        query = q_ref[:, head * HD:(head + 1) * HD]
        if exact:
            q_hi, q_lo = _split(query.astype(jnp.float32))
            scores = lax.dot_general(q_hi, key, contract, preferred_element_type=jnp.float32)
            scores = scores + lax.dot_general(q_lo, key, contract, preferred_element_type=jnp.float32)
        else:
            scores = lax.dot_general(query, key, contract, preferred_element_type=jnp.float32)
        masked = scores * score_scale + bias_ref[...]
        row_top = jnp.max(masked, axis=-1, keepdims=True)
        weights = jnp.exp(masked - row_top)
        totals = jnp.sum(weights, axis=-1, keepdims=True)
        acc = jnp.dot(weights.astype(jnp.bfloat16), value, preferred_element_type=jnp.float32)
        o_ref[:, head * HD:(head + 1) * HD] = (acc / totals).astype(o_ref.dtype)


def attend(first_pos, queries, pairs, window, exact, groups=None, offset=0, first=0, count=None):
    rows, qcols = queries.shape
    if groups is None:
        groups = pairs.shape[1] // (2 * HD)
        kv_spec = pl.BlockSpec((pairs.shape[0], 2 * HD), lambda g, pos: (0, first + g))
    else:
        kv_spec = pl.BlockSpec(
            (pairs.shape[0], 2 * rows, HD), lambda g, pos: (0, offset + first + g, 0)
        )
    qblock = qcols // groups
    count = groups - first if count is None else count
    keys = pairs.shape[0] * (rows if pairs.ndim == 3 else 1)
    kernel = functools.partial(_attend_kernel, window=window, exact=exact)
    return pl.pallas_call(
        kernel,
        out_shape=jax.ShapeDtypeStruct((rows, count * qblock), jnp.bfloat16),
        grid_spec=pltpu.PrefetchScalarGridSpec(
            num_scalar_prefetch=1,
            grid=(count,),
            in_specs=[
                pl.BlockSpec((rows, qblock), lambda g, pos: (0, first + g)),
                kv_spec,
            ],
            out_specs=pl.BlockSpec((rows, qblock), lambda g, pos: (0, g)),
            scratch_shapes=[pltpu.VMEM((rows, keys), jnp.float32)],
        ),
    )(first_pos, queries, pairs)


def _project_kernel(att_ref, w_ref, res_ref, o_ref, *, weight_rows):
    for part in range(o_ref.shape[1] // HD):
        weight = w_ref[:, part * weight_rows:(part + 1) * weight_rows, :].reshape(-1, HD)
        acc = jnp.dot(att_ref[...], weight, preferred_element_type=jnp.float32)
        cols = slice(part * HD, (part + 1) * HD)
        o_ref[:, cols] = (res_ref[:, cols].astype(jnp.float32) + acc).astype(o_ref.dtype)


def project(attended, slab, residual, weight_rows):
    rows, width = residual.shape
    blocks = width // HD
    per_step = next(n for n in (4, 3, 2, 1) if blocks % n == 0)
    return pl.pallas_call(
        functools.partial(_project_kernel, weight_rows=weight_rows),
        out_shape=jax.ShapeDtypeStruct((rows, width), jnp.bfloat16),
        grid=(blocks // per_step,),
        in_specs=[
            pl.BlockSpec(attended.shape, lambda c: (0, 0)),
            pl.BlockSpec((slab.shape[0], per_step * weight_rows, HD), lambda c: (0, c, 0)),
            pl.BlockSpec((rows, per_step * HD), lambda c: (0, c)),
        ],
        out_specs=pl.BlockSpec((rows, per_step * HD), lambda c: (0, c)),
    )(attended, slab, residual)


def _half_kernel(sel_ref, *refs, weight_rows, pieces):
    att_refs = refs[:pieces]
    w_refs = refs[pieces:2 * pieces]
    base_refs = refs[2 * pieces:-1]
    o_ref = refs[-1]
    for part in range(o_ref.shape[1] // HD):
        span = slice(part * weight_rows, (part + 1) * weight_rows)
        acc = 0.0
        for att_ref, w_ref in zip(att_refs, w_refs):
            weight = w_ref[:, span, :].reshape(-1, HD)
            acc = acc + jnp.dot(att_ref[...], weight, preferred_element_type=jnp.float32)
        cols = slice(part * HD, (part + 1) * HD)
        for base_ref in base_refs:
            acc = acc + base_ref[:, cols].astype(jnp.float32)
        o_ref[:, cols] = acc.astype(o_ref.dtype)


def project_half(which, attended, slab, bases, weight_rows, out_dtype, width):
    rows = attended[0].shape[0]
    blocks = width // HD
    per_step = next(n for n in (4, 3, 2, 1) if blocks % n == 0)
    devices = attended[0].shape[1] // weight_rows
    count = len(attended)

    def weight_map(i):
        return lambda c, sel: (sel[0] * count + i, c, 0)

    return pl.pallas_call(
        functools.partial(_half_kernel, weight_rows=weight_rows, pieces=count),
        out_shape=jax.ShapeDtypeStruct((rows, width), out_dtype),
        grid_spec=pltpu.PrefetchScalarGridSpec(
            num_scalar_prefetch=1,
            grid=(blocks // per_step,),
            in_specs=[pl.BlockSpec(p.shape, lambda c, sel: (0, 0)) for p in attended]
            + [
                pl.BlockSpec((devices, per_step * weight_rows, HD), weight_map(i))
                for i in range(count)
            ]
            + [pl.BlockSpec((rows, per_step * HD), lambda c, sel: (0, c)) for _ in bases],
            out_specs=pl.BlockSpec((rows, per_step * HD), lambda c, sel: (0, c)),
        ),
    )(which, *attended, *([slab] * count), *bases)


def to_slab(x):
    rows, cols = x.shape
    return x.reshape(rows, cols // HD, HD).transpose(1, 0, 2).reshape(-1, HD)


def make_body(heads_count):
    def gather_heads(x):
        if heads_count == 2:
            other = lax.ppermute(x, "heads", [(0, 1), (1, 0)])
            first = lax.axis_index("heads") == 0
            low = jnp.where(first, x, other)
            high = jnp.where(first, other, x)
            return jnp.concatenate([low, high], axis=1)
        return lax.all_gather(x, "heads", axis=1, tiled=True)

    def body(
        residual_in,
        self_queries,
        self_keys_values,
        self_out_weight,
        gain_query,
        gain_keyvalue,
        cross_weight,
    ):
        tok_rows = residual_in.shape[0]
        groups = self_keys_values.shape[1] // (2 * HD)
        seq_place = lax.axis_index("seq")
        first_pos = (seq_place * tok_rows).astype(jnp.int32).reshape(1)

        weight_rows = self_out_weight.shape[0]
        weight_part = to_slab(self_out_weight)
        pad = (-weight_part.shape[0]) % (2 * tok_rows)
        weight_part = jnp.pad(weight_part, ((0, pad), (0, 0)))
        offset = weight_part.shape[0] // (2 * tok_rows)
        packed = jnp.concatenate([weight_part, to_slab(self_keys_values)], axis=0)
        slab = lax.all_gather(packed[None], "seq", axis=0, tiled=True)
        col_layout = cross_weight.reshape(cross_weight.shape[0], groups, QPK + 2, HD)
        weight_kv = col_layout[:, :, QPK:].reshape(cross_weight.shape[0], groups * 2 * HD)
        weight_q = col_layout[:, :, :QPK].reshape(cross_weight.shape[0], groups * QPK * HD)
        if heads_count == 2:
            place = lax.axis_index("heads")
            feats = residual_in.shape[1]
            halves = [place * feats, (1 - place) * feats]
            weight_kv = [lax.dynamic_slice_in_dim(weight_kv, at, feats, 0) for at in halves]
            weight_q = [lax.dynamic_slice_in_dim(weight_q, at, feats, 0) for at in halves]
            gains_kv = [lax.dynamic_slice_in_dim(gain_keyvalue, at, feats, 0) for at in halves]
            gains_q = [lax.dynamic_slice_in_dim(gain_query, at, feats, 0) for at in halves]
        slab, weight_kv, weight_q = lax.optimization_barrier((slab, weight_kv, weight_q))
        if heads_count == 2 and groups % 2 == 0:
            pieces = [
                attend(first_pos, self_queries, slab, WINDOW, False, groups, offset, at, groups // 2)
                for at in (0, groups // 2)
            ]
            first_other = lax.ppermute(pieces[0], "heads", [(0, 1), (1, 0)])
            second, first_other = lax.optimization_barrier((pieces[1], first_other))
            others = [first_other, lax.ppermute(second, "heads", [(0, 1), (1, 0)])]
        else:
            attended = attend(first_pos, self_queries, slab, WINDOW, False, groups, offset)
            pieces = [attended]
        if heads_count == 2:
            place = lax.axis_index("heads")
            if groups % 2 != 0:
                others = [lax.ppermute(attended, "heads", [(0, 1), (1, 0)])]
            width = residual_in.shape[1]
            own_part = project_half(
                place.astype(jnp.int32).reshape(1), pieces, slab,
                [], weight_rows, jnp.float32, width,
            )
            hidden = project_half(
                (1 - place).astype(jnp.int32).reshape(1), others, slab,
                [own_part, residual_in], weight_rows, jnp.bfloat16, width,
            )
        else:
            hidden = project(gather_heads(attended), slab, residual_in, weight_rows)
        if heads_count == 2:
            own = hidden.astype(jnp.float32)
            own_squares = jnp.sum(own * own, axis=-1, keepdims=True)
            other_squares = lax.ppermute(own_squares, "heads", [(0, 1), (1, 0)])
            other = lax.ppermute(hidden, "heads", [(0, 1), (1, 0)]).astype(jnp.float32)
            mean = (own_squares + other_squares) / (2 * own.shape[1])
            inverse = lax.rsqrt(mean + 1e-06)
            shared = jnp.dot(
                (own * inverse * gains_kv[0]).astype(jnp.bfloat16), weight_kv[0],
                preferred_element_type=jnp.float32,
            ) + jnp.dot(
                (other * inverse * gains_kv[1]).astype(jnp.bfloat16), weight_kv[1],
                preferred_element_type=jnp.float32,
            )
            shared_all = lax.all_gather(shared.astype(jnp.bfloat16), "seq", axis=0, tiled=True)
            cross_q = jnp.dot(
                (own * inverse * gains_q[0]).astype(jnp.bfloat16), weight_q[0],
                preferred_element_type=jnp.float32,
            ) + jnp.dot(
                (other * inverse * gains_q[1]).astype(jnp.bfloat16), weight_q[1],
                preferred_element_type=jnp.float32,
            )
        else:
            full_rows = gather_heads(hidden)
            widened = full_rows.astype(jnp.float32)
            inverse = lax.rsqrt(jnp.mean(widened * widened, axis=-1, keepdims=True) + 1e-06)
            normed_q = (widened * inverse * gain_query).astype(jnp.bfloat16)
            normed_kv = (widened * inverse * gain_keyvalue).astype(jnp.bfloat16)
            shared = jnp.dot(normed_kv, weight_kv, preferred_element_type=jnp.float32)
            shared_all = lax.all_gather(shared.astype(jnp.bfloat16), "seq", axis=0, tiled=True)
            cross_q = jnp.dot(normed_q, weight_q, preferred_element_type=jnp.float32)
        cross_attention = attend(first_pos, cross_q, shared_all, None, True)
        return (hidden, cross_attention)

    return body


def solution(mesh):
    return jax.shard_map(
        make_body(mesh.shape["heads"]),
        mesh=mesh,
        in_specs=(
            P("seq", "heads"),
            P("seq", "heads"),
            P("seq", "heads"),
            P("seq", "heads"),
            P(),
            P(),
            P(None, "heads"),
        ),
        out_specs=(P("seq", "heads"), P("seq", "heads")),
        check_vma=False,
    )
```

```python
import functools
import math

import jax
import jax.numpy as jnp
from jax import lax
from jax.experimental import pallas as pl
from jax.experimental.pallas import tpu as pltpu
from jax.sharding import PartitionSpec as P

HD = 128
QPK = 3
WINDOW = 2048


def _split(x):
    high = x.astype(jnp.bfloat16)
    low = (x - high.astype(jnp.float32)).astype(jnp.bfloat16)
    return high, low


def mask_bias(first_pos, rows, keys, window):
    query_pos = first_pos[0] + lax.broadcasted_iota(jnp.int32, (rows, keys), 0)
    key_pos = lax.broadcasted_iota(jnp.int32, (rows, keys), 1)
    allowed = key_pos <= query_pos
    if window is not None:
        allowed = allowed & (key_pos > query_pos - window)
    return jnp.where(allowed, 0.0, -jnp.inf).astype(jnp.float32)


def _attend_kernel(pos_ref, q_ref, kv_ref, bias_ref, o_ref, *, window, exact):
    if len(kv_ref.shape) == 3:
        half = kv_ref.shape[1] // 2
        key = kv_ref[:, :half, :].reshape(-1, HD)
        value = kv_ref[:, half:, :].reshape(-1, HD)
    else:
        key = kv_ref[:, :HD]
        value = kv_ref[:, HD:]
    score_scale = 1.0 / math.sqrt(HD)
    contract = (((1,), (1,)), ((), ()))
    for head in range(q_ref.shape[1] // HD):
        query = q_ref[:, head * HD:(head + 1) * HD]
        if exact:
            q_hi, q_lo = _split(query.astype(jnp.float32))
            scores = lax.dot_general(q_hi, key, contract, preferred_element_type=jnp.float32)
            scores = scores + lax.dot_general(q_lo, key, contract, preferred_element_type=jnp.float32)
        else:
            scores = lax.dot_general(query, key, contract, preferred_element_type=jnp.float32)
        masked = scores * score_scale + bias_ref[...]
        row_top = jnp.max(masked, axis=-1, keepdims=True)
        weights = jnp.exp(masked - row_top)
        totals = jnp.sum(weights, axis=-1, keepdims=True)
        acc = jnp.dot(weights.astype(jnp.bfloat16), value, preferred_element_type=jnp.float32)
        o_ref[:, head * HD:(head + 1) * HD] = (acc / totals).astype(o_ref.dtype)


def attend(first_pos, queries, pairs, bias, exact, groups=None, offset=0, first=0, count=None):
    window = None
    rows, qcols = queries.shape
    if groups is None:
        groups = pairs.shape[1] // (2 * HD)
        kv_spec = pl.BlockSpec((pairs.shape[0], 2 * HD), lambda g, pos: (0, first + g))
    else:
        kv_spec = pl.BlockSpec(
            (pairs.shape[0], 2 * rows, HD), lambda g, pos: (0, offset + first + g, 0)
        )
    qblock = qcols // groups
    count = groups - first if count is None else count
    keys = pairs.shape[0] * (rows if pairs.ndim == 3 else 1)
    kernel = functools.partial(_attend_kernel, window=window, exact=exact)
    return pl.pallas_call(
        kernel,
        out_shape=jax.ShapeDtypeStruct((rows, count * qblock), jnp.bfloat16),
        grid_spec=pltpu.PrefetchScalarGridSpec(
            num_scalar_prefetch=1,
            grid=(count,),
            in_specs=[
                pl.BlockSpec((rows, qblock), lambda g, pos: (0, first + g)),
                kv_spec,
                pl.BlockSpec((rows, keys), lambda g, pos: (0, 0)),
            ],
            out_specs=pl.BlockSpec((rows, qblock), lambda g, pos: (0, g)),
        ),
    )(first_pos, queries, pairs, bias)


def _project_kernel(att_ref, w_ref, res_ref, o_ref, *, weight_rows):
    for part in range(o_ref.shape[1] // HD):
        weight = w_ref[:, part * weight_rows:(part + 1) * weight_rows, :].reshape(-1, HD)
        acc = jnp.dot(att_ref[...], weight, preferred_element_type=jnp.float32)
        cols = slice(part * HD, (part + 1) * HD)
        o_ref[:, cols] = (res_ref[:, cols].astype(jnp.float32) + acc).astype(o_ref.dtype)


def project(attended, slab, residual, weight_rows):
    rows, width = residual.shape
    blocks = width // HD
    per_step = next(n for n in (4, 3, 2, 1) if blocks % n == 0)
    return pl.pallas_call(
        functools.partial(_project_kernel, weight_rows=weight_rows),
        out_shape=jax.ShapeDtypeStruct((rows, width), jnp.bfloat16),
        grid=(blocks // per_step,),
        in_specs=[
            pl.BlockSpec(attended.shape, lambda c: (0, 0)),
            pl.BlockSpec((slab.shape[0], per_step * weight_rows, HD), lambda c: (0, c, 0)),
            pl.BlockSpec((rows, per_step * HD), lambda c: (0, c)),
        ],
        out_specs=pl.BlockSpec((rows, per_step * HD), lambda c: (0, c)),
    )(attended, slab, residual)


def _half_kernel(sel_ref, *refs, weight_rows, pieces):
    att_refs = refs[:pieces]
    w_refs = refs[pieces:2 * pieces]
    base_refs = refs[2 * pieces:-1]
    o_ref = refs[-1]
    for part in range(o_ref.shape[1] // HD):
        span = slice(part * weight_rows, (part + 1) * weight_rows)
        acc = 0.0
        for att_ref, w_ref in zip(att_refs, w_refs):
            weight = w_ref[:, span, :].reshape(-1, HD)
            acc = acc + jnp.dot(att_ref[...], weight, preferred_element_type=jnp.float32)
        cols = slice(part * HD, (part + 1) * HD)
        for base_ref in base_refs:
            acc = acc + base_ref[:, cols].astype(jnp.float32)
        o_ref[:, cols] = acc.astype(o_ref.dtype)


def project_half(which, attended, slab, bases, weight_rows, out_dtype, width):
    rows = attended[0].shape[0]
    blocks = width // HD
    per_step = next(n for n in (4, 3, 2, 1) if blocks % n == 0)
    devices = attended[0].shape[1] // weight_rows
    count = len(attended)

    def weight_map(i):
        return lambda c, sel: (sel[0] * count + i, c, 0)

    return pl.pallas_call(
        functools.partial(_half_kernel, weight_rows=weight_rows, pieces=count),
        out_shape=jax.ShapeDtypeStruct((rows, width), out_dtype),
        grid_spec=pltpu.PrefetchScalarGridSpec(
            num_scalar_prefetch=1,
            grid=(blocks // per_step,),
            in_specs=[pl.BlockSpec(p.shape, lambda c, sel: (0, 0)) for p in attended]
            + [
                pl.BlockSpec((devices, per_step * weight_rows, HD), weight_map(i))
                for i in range(count)
            ]
            + [pl.BlockSpec((rows, per_step * HD), lambda c, sel: (0, c)) for _ in bases],
            out_specs=pl.BlockSpec((rows, per_step * HD), lambda c, sel: (0, c)),
        ),
    )(which, *attended, *([slab] * count), *bases)


def to_slab(x):
    rows, cols = x.shape
    return x.reshape(rows, cols // HD, HD).transpose(1, 0, 2).reshape(-1, HD)


def make_body(heads_count):
    def gather_heads(x):
        if heads_count == 2:
            other = lax.ppermute(x, "heads", [(0, 1), (1, 0)])
            first = lax.axis_index("heads") == 0
            low = jnp.where(first, x, other)
            high = jnp.where(first, other, x)
            return jnp.concatenate([low, high], axis=1)
        return lax.all_gather(x, "heads", axis=1, tiled=True)

    def body(
        residual_in,
        self_queries,
        self_keys_values,
        self_out_weight,
        gain_query,
        gain_keyvalue,
        cross_weight,
    ):
        tok_rows = residual_in.shape[0]
        groups = self_keys_values.shape[1] // (2 * HD)
        seq_place = lax.axis_index("seq")
        first_pos = (seq_place * tok_rows).astype(jnp.int32).reshape(1)

        weight_rows = self_out_weight.shape[0]
        weight_part = to_slab(self_out_weight)
        pad = (-weight_part.shape[0]) % (2 * tok_rows)
        weight_part = jnp.pad(weight_part, ((0, pad), (0, 0)))
        offset = weight_part.shape[0] // (2 * tok_rows)
        packed = jnp.concatenate([weight_part, to_slab(self_keys_values)], axis=0)
        slab = lax.all_gather(packed[None], "seq", axis=0, tiled=True)
        keys = slab.shape[0] * tok_rows
        self_bias = mask_bias(first_pos, tok_rows, keys, WINDOW)
        cross_bias = mask_bias(first_pos, tok_rows, keys, None)
        col_layout = cross_weight.reshape(cross_weight.shape[0], groups, QPK + 2, HD)
        weight_kv = col_layout[:, :, QPK:].reshape(cross_weight.shape[0], groups * 2 * HD)
        weight_q = col_layout[:, :, :QPK].reshape(cross_weight.shape[0], groups * QPK * HD)
        if heads_count == 2:
            place = lax.axis_index("heads")
            feats = residual_in.shape[1]
            halves = [place * feats, (1 - place) * feats]
            weight_kv = [lax.dynamic_slice_in_dim(weight_kv, at, feats, 0) for at in halves]
            weight_q = [lax.dynamic_slice_in_dim(weight_q, at, feats, 0) for at in halves]
            gains_kv = [lax.dynamic_slice_in_dim(gain_keyvalue, at, feats, 0) for at in halves]
            gains_q = [lax.dynamic_slice_in_dim(gain_query, at, feats, 0) for at in halves]
        slab, weight_kv, weight_q, self_bias, cross_bias = lax.optimization_barrier(
            (slab, weight_kv, weight_q, self_bias, cross_bias)
        )
        if heads_count == 2 and groups % 2 == 0:
            pieces = [
                attend(first_pos, self_queries, slab, self_bias, False, groups, offset, at, groups // 2)
                for at in (0, groups // 2)
            ]
            first_other = lax.ppermute(pieces[0], "heads", [(0, 1), (1, 0)])
            second, first_other = lax.optimization_barrier((pieces[1], first_other))
            others = [first_other, lax.ppermute(second, "heads", [(0, 1), (1, 0)])]
        else:
            attended = attend(first_pos, self_queries, slab, self_bias, False, groups, offset)
            pieces = [attended]
        if heads_count == 2:
            place = lax.axis_index("heads")
            if groups % 2 != 0:
                others = [lax.ppermute(attended, "heads", [(0, 1), (1, 0)])]
            width = residual_in.shape[1]
            own_part = project_half(
                place.astype(jnp.int32).reshape(1), pieces, slab,
                [], weight_rows, jnp.float32, width,
            )
            hidden = project_half(
                (1 - place).astype(jnp.int32).reshape(1), others, slab,
                [own_part, residual_in], weight_rows, jnp.bfloat16, width,
            )
        else:
            hidden = project(gather_heads(attended), slab, residual_in, weight_rows)
        if heads_count == 2:
            own = hidden.astype(jnp.float32)
            own_squares = jnp.sum(own * own, axis=-1, keepdims=True)
            other_squares = lax.ppermute(own_squares, "heads", [(0, 1), (1, 0)])
            other = lax.ppermute(hidden, "heads", [(0, 1), (1, 0)]).astype(jnp.float32)
            mean = (own_squares + other_squares) / (2 * own.shape[1])
            inverse = lax.rsqrt(mean + 1e-06)
            shared = jnp.dot(
                (own * inverse * gains_kv[0]).astype(jnp.bfloat16), weight_kv[0],
                preferred_element_type=jnp.float32,
            ) + jnp.dot(
                (other * inverse * gains_kv[1]).astype(jnp.bfloat16), weight_kv[1],
                preferred_element_type=jnp.float32,
            )
            shared_all = lax.all_gather(shared.astype(jnp.bfloat16), "seq", axis=0, tiled=True)
            cross_q = jnp.dot(
                (own * inverse * gains_q[0]).astype(jnp.bfloat16), weight_q[0],
                preferred_element_type=jnp.float32,
            ) + jnp.dot(
                (other * inverse * gains_q[1]).astype(jnp.bfloat16), weight_q[1],
                preferred_element_type=jnp.float32,
            )
        else:
            full_rows = gather_heads(hidden)
            widened = full_rows.astype(jnp.float32)
            inverse = lax.rsqrt(jnp.mean(widened * widened, axis=-1, keepdims=True) + 1e-06)
            normed_q = (widened * inverse * gain_query).astype(jnp.bfloat16)
            normed_kv = (widened * inverse * gain_keyvalue).astype(jnp.bfloat16)
            shared = jnp.dot(normed_kv, weight_kv, preferred_element_type=jnp.float32)
            shared_all = lax.all_gather(shared.astype(jnp.bfloat16), "seq", axis=0, tiled=True)
            cross_q = jnp.dot(normed_q, weight_q, preferred_element_type=jnp.float32)
        cross_attention = attend(first_pos, cross_q, shared_all, cross_bias, True)
        return (hidden, cross_attention)

    return body


def solution(mesh):
    return jax.shard_map(
        make_body(mesh.shape["heads"]),
        mesh=mesh,
        in_specs=(
            P("seq", "heads"),
            P("seq", "heads"),
            P("seq", "heads"),
            P("seq", "heads"),
            P(),
            P(),
            P(None, "heads"),
        ),
        out_specs=(P("seq", "heads"), P("seq", "heads")),
        check_vma=False,
    )
```

```python
import functools
import math

import jax
import jax.numpy as jnp
from jax import lax
from jax.experimental import pallas as pl
from jax.experimental.pallas import tpu as pltpu
from jax.sharding import PartitionSpec as P

HD = 128
QPK = 3
WINDOW = 2048


def _split(x):
    high = x.astype(jnp.bfloat16)
    low = (x - high.astype(jnp.float32)).astype(jnp.bfloat16)
    return high, low


def _attend_kernel(pos_ref, q_ref, kv_ref, o_ref, bias_ref, *, window, exact):
    rows, keys = bias_ref.shape

    @pl.when(pl.program_id(0) == 0)
    def _():
        query_pos = pos_ref[0] + lax.broadcasted_iota(jnp.int32, (rows, keys), 0)
        key_pos = lax.broadcasted_iota(jnp.int32, (rows, keys), 1)
        allowed = key_pos <= query_pos
        if window is not None:
            allowed = allowed & (key_pos > query_pos - window)
        bias_ref[...] = jnp.where(allowed, 0.0, -jnp.inf)

    if len(kv_ref.shape) == 3:
        half = kv_ref.shape[1] // 2
        key = kv_ref[:, :half, :].reshape(-1, HD)
        value = kv_ref[:, half:, :].reshape(-1, HD)
    else:
        key = kv_ref[:, :HD]
        value = kv_ref[:, HD:]
    score_scale = 1.0 / math.sqrt(HD)
    contract = (((1,), (1,)), ((), ()))
    heads = q_ref.shape[1] // HD
    query = jnp.concatenate([q_ref[:, h * HD:(h + 1) * HD] for h in range(heads)], axis=0)
    if exact:
        q_hi, q_lo = _split(query.astype(jnp.float32))
        scores = lax.dot_general(q_hi, key, contract, preferred_element_type=jnp.float32)
        scores = scores + lax.dot_general(q_lo, key, contract, preferred_element_type=jnp.float32)
    else:
        scores = lax.dot_general(query, key, contract, preferred_element_type=jnp.float32)
    masked = (scores * score_scale).reshape(heads, rows, keys) + bias_ref[...][None]
    masked = masked.reshape(heads * rows, keys)
    row_top = jnp.max(masked, axis=-1, keepdims=True)
    weights = jnp.exp(masked - row_top)
    totals = jnp.sum(weights, axis=-1, keepdims=True)
    acc = jnp.dot(weights.astype(jnp.bfloat16), value, preferred_element_type=jnp.float32)
    result = acc / totals
    for head in range(heads):
        o_ref[:, head * HD:(head + 1) * HD] = result[head * rows:(head + 1) * rows].astype(o_ref.dtype)


def attend(first_pos, queries, pairs, window, exact, groups=None, offset=0, first=0, count=None):
    rows, qcols = queries.shape
    if groups is None:
        groups = pairs.shape[1] // (2 * HD)
        kv_spec = pl.BlockSpec((pairs.shape[0], 2 * HD), lambda g, pos: (0, first + g))
    else:
        kv_spec = pl.BlockSpec(
            (pairs.shape[0], 2 * rows, HD), lambda g, pos: (0, offset + first + g, 0)
        )
    qblock = qcols // groups
    count = groups - first if count is None else count
    keys = pairs.shape[0] * (rows if pairs.ndim == 3 else 1)
    kernel = functools.partial(_attend_kernel, window=window, exact=exact)
    return pl.pallas_call(
        kernel,
        out_shape=jax.ShapeDtypeStruct((rows, count * qblock), jnp.bfloat16),
        grid_spec=pltpu.PrefetchScalarGridSpec(
            num_scalar_prefetch=1,
            grid=(count,),
            in_specs=[
                pl.BlockSpec((rows, qblock), lambda g, pos: (0, first + g)),
                kv_spec,
            ],
            out_specs=pl.BlockSpec((rows, qblock), lambda g, pos: (0, g)),
            scratch_shapes=[pltpu.VMEM((rows, keys), jnp.float32)],
        ),
    )(first_pos, queries, pairs)


def _project_kernel(att_ref, w_ref, res_ref, o_ref, *, weight_rows):
    for part in range(o_ref.shape[1] // HD):
        weight = w_ref[:, part * weight_rows:(part + 1) * weight_rows, :].reshape(-1, HD)
        acc = jnp.dot(att_ref[...], weight, preferred_element_type=jnp.float32)
        cols = slice(part * HD, (part + 1) * HD)
        o_ref[:, cols] = (res_ref[:, cols].astype(jnp.float32) + acc).astype(o_ref.dtype)


def project(attended, slab, residual, weight_rows):
    rows, width = residual.shape
    blocks = width // HD
    per_step = next(n for n in (4, 3, 2, 1) if blocks % n == 0)
    return pl.pallas_call(
        functools.partial(_project_kernel, weight_rows=weight_rows),
        out_shape=jax.ShapeDtypeStruct((rows, width), jnp.bfloat16),
        grid=(blocks // per_step,),
        in_specs=[
            pl.BlockSpec(attended.shape, lambda c: (0, 0)),
            pl.BlockSpec((slab.shape[0], per_step * weight_rows, HD), lambda c: (0, c, 0)),
            pl.BlockSpec((rows, per_step * HD), lambda c: (0, c)),
        ],
        out_specs=pl.BlockSpec((rows, per_step * HD), lambda c: (0, c)),
    )(attended, slab, residual)


def _half_kernel(sel_ref, *refs, weight_rows, pieces):
    att_refs = refs[:pieces]
    w_refs = refs[pieces:2 * pieces]
    base_refs = refs[2 * pieces:-1]
    o_ref = refs[-1]
    for part in range(o_ref.shape[1] // HD):
        span = slice(part * weight_rows, (part + 1) * weight_rows)
        acc = 0.0
        for att_ref, w_ref in zip(att_refs, w_refs):
            weight = w_ref[:, span, :].reshape(-1, HD)
            acc = acc + jnp.dot(att_ref[...], weight, preferred_element_type=jnp.float32)
        cols = slice(part * HD, (part + 1) * HD)
        for base_ref in base_refs:
            acc = acc + base_ref[:, cols].astype(jnp.float32)
        o_ref[:, cols] = acc.astype(o_ref.dtype)


def project_half(which, attended, slab, bases, weight_rows, out_dtype, width):
    rows = attended[0].shape[0]
    blocks = width // HD
    per_step = next(n for n in (4, 3, 2, 1) if blocks % n == 0)
    devices = attended[0].shape[1] // weight_rows
    count = len(attended)

    def weight_map(i):
        return lambda c, sel: (sel[0] * count + i, c, 0)

    return pl.pallas_call(
        functools.partial(_half_kernel, weight_rows=weight_rows, pieces=count),
        out_shape=jax.ShapeDtypeStruct((rows, width), out_dtype),
        grid_spec=pltpu.PrefetchScalarGridSpec(
            num_scalar_prefetch=1,
            grid=(blocks // per_step,),
            in_specs=[pl.BlockSpec(p.shape, lambda c, sel: (0, 0)) for p in attended]
            + [
                pl.BlockSpec((devices, per_step * weight_rows, HD), weight_map(i))
                for i in range(count)
            ]
            + [pl.BlockSpec((rows, per_step * HD), lambda c, sel: (0, c)) for _ in bases],
            out_specs=pl.BlockSpec((rows, per_step * HD), lambda c, sel: (0, c)),
        ),
    )(which, *attended, *([slab] * count), *bases)


def to_slab(x):
    rows, cols = x.shape
    return x.reshape(rows, cols // HD, HD).transpose(1, 0, 2).reshape(-1, HD)


def make_body(heads_count):
    def gather_heads(x):
        if heads_count == 2:
            other = lax.ppermute(x, "heads", [(0, 1), (1, 0)])
            first = lax.axis_index("heads") == 0
            low = jnp.where(first, x, other)
            high = jnp.where(first, other, x)
            return jnp.concatenate([low, high], axis=1)
        return lax.all_gather(x, "heads", axis=1, tiled=True)

    def body(
        residual_in,
        self_queries,
        self_keys_values,
        self_out_weight,
        gain_query,
        gain_keyvalue,
        cross_weight,
    ):
        tok_rows = residual_in.shape[0]
        groups = self_keys_values.shape[1] // (2 * HD)
        seq_place = lax.axis_index("seq")
        first_pos = (seq_place * tok_rows).astype(jnp.int32).reshape(1)

        weight_rows = self_out_weight.shape[0]
        weight_part = to_slab(self_out_weight)
        pad = (-weight_part.shape[0]) % (2 * tok_rows)
        weight_part = jnp.pad(weight_part, ((0, pad), (0, 0)))
        offset = weight_part.shape[0] // (2 * tok_rows)
        packed = jnp.concatenate([weight_part, to_slab(self_keys_values)], axis=0)
        slab = lax.all_gather(packed[None], "seq", axis=0, tiled=True)
        col_layout = cross_weight.reshape(cross_weight.shape[0], groups, QPK + 2, HD)
        weight_kv = col_layout[:, :, QPK:].reshape(cross_weight.shape[0], groups * 2 * HD)
        weight_q = col_layout[:, :, :QPK].reshape(cross_weight.shape[0], groups * QPK * HD)
        if heads_count == 2:
            place = lax.axis_index("heads")
            feats = residual_in.shape[1]
            halves = [place * feats, (1 - place) * feats]
            weight_kv = [lax.dynamic_slice_in_dim(weight_kv, at, feats, 0) for at in halves]
            weight_q = [lax.dynamic_slice_in_dim(weight_q, at, feats, 0) for at in halves]
            gains_kv = [lax.dynamic_slice_in_dim(gain_keyvalue, at, feats, 0) for at in halves]
            gains_q = [lax.dynamic_slice_in_dim(gain_query, at, feats, 0) for at in halves]
        slab, weight_kv, weight_q = lax.optimization_barrier((slab, weight_kv, weight_q))
        if heads_count == 2 and groups % 2 == 0:
            pieces = [
                attend(first_pos, self_queries, slab, WINDOW, False, groups, offset, at, groups // 2)
                for at in (0, groups // 2)
            ]
            first_other = lax.ppermute(pieces[0], "heads", [(0, 1), (1, 0)])
            second, first_other = lax.optimization_barrier((pieces[1], first_other))
            others = [first_other, lax.ppermute(second, "heads", [(0, 1), (1, 0)])]
        else:
            attended = attend(first_pos, self_queries, slab, WINDOW, False, groups, offset)
            pieces = [attended]
        if heads_count == 2:
            place = lax.axis_index("heads")
            if groups % 2 != 0:
                others = [lax.ppermute(attended, "heads", [(0, 1), (1, 0)])]
            width = residual_in.shape[1]
            own_part = project_half(
                place.astype(jnp.int32).reshape(1), pieces, slab,
                [], weight_rows, jnp.float32, width,
            )
            hidden = project_half(
                (1 - place).astype(jnp.int32).reshape(1), others, slab,
                [own_part, residual_in], weight_rows, jnp.bfloat16, width,
            )
        else:
            hidden = project(gather_heads(attended), slab, residual_in, weight_rows)
        if heads_count == 2:
            own = hidden.astype(jnp.float32)
            own_squares = jnp.sum(own * own, axis=-1, keepdims=True)
            other_squares = lax.ppermute(own_squares, "heads", [(0, 1), (1, 0)])
            other = lax.ppermute(hidden, "heads", [(0, 1), (1, 0)]).astype(jnp.float32)
            mean = (own_squares + other_squares) / (2 * own.shape[1])
            inverse = lax.rsqrt(mean + 1e-06)
            shared = jnp.dot(
                (own * inverse * gains_kv[0]).astype(jnp.bfloat16), weight_kv[0],
                preferred_element_type=jnp.float32,
            ) + jnp.dot(
                (other * inverse * gains_kv[1]).astype(jnp.bfloat16), weight_kv[1],
                preferred_element_type=jnp.float32,
            )
            shared_all = lax.all_gather(shared.astype(jnp.bfloat16), "seq", axis=0, tiled=True)
            cross_q = jnp.dot(
                (own * inverse * gains_q[0]).astype(jnp.bfloat16), weight_q[0],
                preferred_element_type=jnp.float32,
            ) + jnp.dot(
                (other * inverse * gains_q[1]).astype(jnp.bfloat16), weight_q[1],
                preferred_element_type=jnp.float32,
            )
        else:
            full_rows = gather_heads(hidden)
            widened = full_rows.astype(jnp.float32)
            inverse = lax.rsqrt(jnp.mean(widened * widened, axis=-1, keepdims=True) + 1e-06)
            normed_q = (widened * inverse * gain_query).astype(jnp.bfloat16)
            normed_kv = (widened * inverse * gain_keyvalue).astype(jnp.bfloat16)
            shared = jnp.dot(normed_kv, weight_kv, preferred_element_type=jnp.float32)
            shared_all = lax.all_gather(shared.astype(jnp.bfloat16), "seq", axis=0, tiled=True)
            cross_q = jnp.dot(normed_q, weight_q, preferred_element_type=jnp.float32)
        cross_attention = attend(first_pos, cross_q, shared_all, None, True)
        return (hidden, cross_attention)

    return body


def solution(mesh):
    return jax.shard_map(
        make_body(mesh.shape["heads"]),
        mesh=mesh,
        in_specs=(
            P("seq", "heads"),
            P("seq", "heads"),
            P("seq", "heads"),
            P("seq", "heads"),
            P(),
            P(),
            P(None, "heads"),
        ),
        out_specs=(P("seq", "heads"), P("seq", "heads")),
        check_vma=False,
    )
```

```python
import functools
import math

import jax
import jax.numpy as jnp
from jax import lax
from jax.experimental import pallas as pl
from jax.experimental.pallas import tpu as pltpu
from jax.sharding import PartitionSpec as P

HD = 128
QPK = 3
WINDOW = 2048


def _split(x):
    high = x.astype(jnp.bfloat16)
    low = (x - high.astype(jnp.float32)).astype(jnp.bfloat16)
    return high, low


def _attend_kernel(pos_ref, q_ref, kv_ref, o_ref, bias_ref, *, window, exact):
    rows, keys = bias_ref.shape

    @pl.when(pl.program_id(0) == 0)
    def _():
        query_pos = pos_ref[0] + lax.broadcasted_iota(jnp.int32, (rows, keys), 0)
        key_pos = lax.broadcasted_iota(jnp.int32, (rows, keys), 1)
        allowed = key_pos <= query_pos
        if window is not None:
            allowed = allowed & (key_pos > query_pos - window)
        bias_ref[...] = jnp.where(allowed, 0.0, -jnp.inf)

    if len(kv_ref.shape) == 3:
        half = kv_ref.shape[1] // 2
        key = kv_ref[:, :half, :].reshape(-1, HD)
        value = kv_ref[:, half:, :].reshape(-1, HD)
    else:
        key = kv_ref[:, :HD]
        value = kv_ref[:, HD:]
    score_scale = 1.0 / math.sqrt(HD)
    contract = (((1,), (1,)), ((), ()))
    if exact:
        doubled = jnp.concatenate([key, key], axis=1)
    for head in range(q_ref.shape[1] // HD):
        query = q_ref[:, head * HD:(head + 1) * HD]
        if exact:
            q_hi, q_lo = _split(query.astype(jnp.float32))
            both = jnp.concatenate([q_hi, q_lo], axis=1)
            scores = lax.dot_general(both, doubled, contract, preferred_element_type=jnp.float32)
        else:
            scores = lax.dot_general(query, key, contract, preferred_element_type=jnp.float32)
        masked = scores * score_scale + bias_ref[...]
        row_top = jnp.max(masked, axis=-1, keepdims=True)
        weights = jnp.exp(masked - row_top)
        totals = jnp.sum(weights, axis=-1, keepdims=True)
        acc = jnp.dot(weights.astype(jnp.bfloat16), value, preferred_element_type=jnp.float32)
        o_ref[:, head * HD:(head + 1) * HD] = (acc / totals).astype(o_ref.dtype)


def attend(first_pos, queries, pairs, window, exact, groups=None, offset=0, first=0, count=None):
    rows, qcols = queries.shape
    if groups is None:
        groups = pairs.shape[1] // (2 * HD)
        kv_spec = pl.BlockSpec((pairs.shape[0], 2 * HD), lambda g, pos: (0, first + g))
    else:
        kv_spec = pl.BlockSpec(
            (pairs.shape[0], 2 * rows, HD), lambda g, pos: (0, offset + first + g, 0)
        )
    qblock = qcols // groups
    count = groups - first if count is None else count
    keys = pairs.shape[0] * (rows if pairs.ndim == 3 else 1)
    kernel = functools.partial(_attend_kernel, window=window, exact=exact)
    return pl.pallas_call(
        kernel,
        out_shape=jax.ShapeDtypeStruct((rows, count * qblock), jnp.bfloat16),
        grid_spec=pltpu.PrefetchScalarGridSpec(
            num_scalar_prefetch=1,
            grid=(count,),
            in_specs=[
                pl.BlockSpec((rows, qblock), lambda g, pos: (0, first + g)),
                kv_spec,
            ],
            out_specs=pl.BlockSpec((rows, qblock), lambda g, pos: (0, g)),
            scratch_shapes=[pltpu.VMEM((rows, keys), jnp.float32)],
        ),
    )(first_pos, queries, pairs)


def _project_kernel(att_ref, w_ref, res_ref, o_ref, *, weight_rows):
    for part in range(o_ref.shape[1] // HD):
        weight = w_ref[:, part * weight_rows:(part + 1) * weight_rows, :].reshape(-1, HD)
        acc = jnp.dot(att_ref[...], weight, preferred_element_type=jnp.float32)
        cols = slice(part * HD, (part + 1) * HD)
        o_ref[:, cols] = (res_ref[:, cols].astype(jnp.float32) + acc).astype(o_ref.dtype)


def project(attended, slab, residual, weight_rows):
    rows, width = residual.shape
    blocks = width // HD
    per_step = next(n for n in (4, 3, 2, 1) if blocks % n == 0)
    return pl.pallas_call(
        functools.partial(_project_kernel, weight_rows=weight_rows),
        out_shape=jax.ShapeDtypeStruct((rows, width), jnp.bfloat16),
        grid=(blocks // per_step,),
        in_specs=[
            pl.BlockSpec(attended.shape, lambda c: (0, 0)),
            pl.BlockSpec((slab.shape[0], per_step * weight_rows, HD), lambda c: (0, c, 0)),
            pl.BlockSpec((rows, per_step * HD), lambda c: (0, c)),
        ],
        out_specs=pl.BlockSpec((rows, per_step * HD), lambda c: (0, c)),
    )(attended, slab, residual)


def _half_kernel(sel_ref, *refs, weight_rows, pieces):
    att_refs = refs[:pieces]
    w_refs = refs[pieces:2 * pieces]
    base_refs = refs[2 * pieces:-1]
    o_ref = refs[-1]
    for part in range(o_ref.shape[1] // HD):
        span = slice(part * weight_rows, (part + 1) * weight_rows)
        acc = 0.0
        for att_ref, w_ref in zip(att_refs, w_refs):
            weight = w_ref[:, span, :].reshape(-1, HD)
            acc = acc + jnp.dot(att_ref[...], weight, preferred_element_type=jnp.float32)
        cols = slice(part * HD, (part + 1) * HD)
        for base_ref in base_refs:
            acc = acc + base_ref[:, cols].astype(jnp.float32)
        o_ref[:, cols] = acc.astype(o_ref.dtype)


def project_half(which, attended, slab, bases, weight_rows, out_dtype, width):
    rows = attended[0].shape[0]
    blocks = width // HD
    per_step = next(n for n in (4, 3, 2, 1) if blocks % n == 0)
    devices = attended[0].shape[1] // weight_rows
    count = len(attended)

    def weight_map(i):
        return lambda c, sel: (sel[0] * count + i, c, 0)

    return pl.pallas_call(
        functools.partial(_half_kernel, weight_rows=weight_rows, pieces=count),
        out_shape=jax.ShapeDtypeStruct((rows, width), out_dtype),
        grid_spec=pltpu.PrefetchScalarGridSpec(
            num_scalar_prefetch=1,
            grid=(blocks // per_step,),
            in_specs=[pl.BlockSpec(p.shape, lambda c, sel: (0, 0)) for p in attended]
            + [
                pl.BlockSpec((devices, per_step * weight_rows, HD), weight_map(i))
                for i in range(count)
            ]
            + [pl.BlockSpec((rows, per_step * HD), lambda c, sel: (0, c)) for _ in bases],
            out_specs=pl.BlockSpec((rows, per_step * HD), lambda c, sel: (0, c)),
        ),
    )(which, *attended, *([slab] * count), *bases)


def to_slab(x):
    rows, cols = x.shape
    return x.reshape(rows, cols // HD, HD).transpose(1, 0, 2).reshape(-1, HD)


def make_body(heads_count):
    def gather_heads(x):
        if heads_count == 2:
            other = lax.ppermute(x, "heads", [(0, 1), (1, 0)])
            first = lax.axis_index("heads") == 0
            low = jnp.where(first, x, other)
            high = jnp.where(first, other, x)
            return jnp.concatenate([low, high], axis=1)
        return lax.all_gather(x, "heads", axis=1, tiled=True)

    def body(
        residual_in,
        self_queries,
        self_keys_values,
        self_out_weight,
        gain_query,
        gain_keyvalue,
        cross_weight,
    ):
        tok_rows = residual_in.shape[0]
        groups = self_keys_values.shape[1] // (2 * HD)
        seq_place = lax.axis_index("seq")
        first_pos = (seq_place * tok_rows).astype(jnp.int32).reshape(1)

        weight_rows = self_out_weight.shape[0]
        weight_part = to_slab(self_out_weight)
        pad = (-weight_part.shape[0]) % (2 * tok_rows)
        weight_part = jnp.pad(weight_part, ((0, pad), (0, 0)))
        offset = weight_part.shape[0] // (2 * tok_rows)
        packed = jnp.concatenate([weight_part, to_slab(self_keys_values)], axis=0)
        slab = lax.all_gather(packed[None], "seq", axis=0, tiled=True)
        col_layout = cross_weight.reshape(cross_weight.shape[0], groups, QPK + 2, HD)
        weight_kv = col_layout[:, :, QPK:].reshape(cross_weight.shape[0], groups * 2 * HD)
        weight_q = col_layout[:, :, :QPK].reshape(cross_weight.shape[0], groups * QPK * HD)
        if heads_count == 2:
            place = lax.axis_index("heads")
            feats = residual_in.shape[1]
            halves = [place * feats, (1 - place) * feats]
            weight_kv = [lax.dynamic_slice_in_dim(weight_kv, at, feats, 0) for at in halves]
            weight_q = [lax.dynamic_slice_in_dim(weight_q, at, feats, 0) for at in halves]
            gains_kv = [lax.dynamic_slice_in_dim(gain_keyvalue, at, feats, 0) for at in halves]
            gains_q = [lax.dynamic_slice_in_dim(gain_query, at, feats, 0) for at in halves]
        slab, weight_kv, weight_q = lax.optimization_barrier((slab, weight_kv, weight_q))
        if heads_count == 2 and groups % 2 == 0:
            pieces = [
                attend(first_pos, self_queries, slab, WINDOW, False, groups, offset, at, groups // 2)
                for at in (0, groups // 2)
            ]
            first_other = lax.ppermute(pieces[0], "heads", [(0, 1), (1, 0)])
            second, first_other = lax.optimization_barrier((pieces[1], first_other))
            others = [first_other, lax.ppermute(second, "heads", [(0, 1), (1, 0)])]
        else:
            attended = attend(first_pos, self_queries, slab, WINDOW, False, groups, offset)
            pieces = [attended]
        if heads_count == 2:
            place = lax.axis_index("heads")
            if groups % 2 != 0:
                others = [lax.ppermute(attended, "heads", [(0, 1), (1, 0)])]
            width = residual_in.shape[1]
            own_part = project_half(
                place.astype(jnp.int32).reshape(1), pieces, slab,
                [], weight_rows, jnp.float32, width,
            )
            hidden = project_half(
                (1 - place).astype(jnp.int32).reshape(1), others, slab,
                [own_part, residual_in], weight_rows, jnp.bfloat16, width,
            )
        else:
            hidden = project(gather_heads(attended), slab, residual_in, weight_rows)
        if heads_count == 2:
            own = hidden.astype(jnp.float32)
            own_squares = jnp.sum(own * own, axis=-1, keepdims=True)
            other_squares = lax.ppermute(own_squares, "heads", [(0, 1), (1, 0)])
            other = lax.ppermute(hidden, "heads", [(0, 1), (1, 0)]).astype(jnp.float32)
            mean = (own_squares + other_squares) / (2 * own.shape[1])
            inverse = lax.rsqrt(mean + 1e-06)
            shared = jnp.dot(
                (own * inverse * gains_kv[0]).astype(jnp.bfloat16), weight_kv[0],
                preferred_element_type=jnp.float32,
            ) + jnp.dot(
                (other * inverse * gains_kv[1]).astype(jnp.bfloat16), weight_kv[1],
                preferred_element_type=jnp.float32,
            )
            shared_all = lax.all_gather(shared.astype(jnp.bfloat16), "seq", axis=0, tiled=True)
            cross_q = jnp.dot(
                (own * inverse * gains_q[0]).astype(jnp.bfloat16), weight_q[0],
                preferred_element_type=jnp.float32,
            ) + jnp.dot(
                (other * inverse * gains_q[1]).astype(jnp.bfloat16), weight_q[1],
                preferred_element_type=jnp.float32,
            )
        else:
            full_rows = gather_heads(hidden)
            widened = full_rows.astype(jnp.float32)
            inverse = lax.rsqrt(jnp.mean(widened * widened, axis=-1, keepdims=True) + 1e-06)
            normed_q = (widened * inverse * gain_query).astype(jnp.bfloat16)
            normed_kv = (widened * inverse * gain_keyvalue).astype(jnp.bfloat16)
            shared = jnp.dot(normed_kv, weight_kv, preferred_element_type=jnp.float32)
            shared_all = lax.all_gather(shared.astype(jnp.bfloat16), "seq", axis=0, tiled=True)
            cross_q = jnp.dot(normed_q, weight_q, preferred_element_type=jnp.float32)
        cross_attention = attend(first_pos, cross_q, shared_all, None, True)
        return (hidden, cross_attention)

    return body


def solution(mesh):
    return jax.shard_map(
        make_body(mesh.shape["heads"]),
        mesh=mesh,
        in_specs=(
            P("seq", "heads"),
            P("seq", "heads"),
            P("seq", "heads"),
            P("seq", "heads"),
            P(),
            P(),
            P(None, "heads"),
        ),
        out_specs=(P("seq", "heads"), P("seq", "heads")),
        check_vma=False,
    )
```

```python
import functools
import math

import jax
import jax.numpy as jnp
from jax import lax
from jax.experimental import pallas as pl
from jax.experimental.pallas import tpu as pltpu
from jax.sharding import PartitionSpec as P

HD = 128
QPK = 3
WINDOW = 2048


def _split(x):
    high = x.astype(jnp.bfloat16)
    low = (x - high.astype(jnp.float32)).astype(jnp.bfloat16)
    return high, low


def _attend_kernel(pos_ref, q_ref, kv_ref, o_ref, bias_ref, *, window, exact):
    rows, keys = bias_ref.shape

    @pl.when(pl.program_id(0) == 0)
    def _():
        query_pos = pos_ref[0] + lax.broadcasted_iota(jnp.int32, (rows, keys), 0)
        key_pos = lax.broadcasted_iota(jnp.int32, (rows, keys), 1)
        allowed = key_pos <= query_pos
        if window is not None:
            allowed = allowed & (key_pos > query_pos - window)
        bias_ref[...] = jnp.where(allowed, 0.0, -jnp.inf)

    if len(kv_ref.shape) == 3:
        half = kv_ref.shape[1] // 2
        key = kv_ref[:, :half, :].reshape(-1, HD)
        value = kv_ref[:, half:, :].reshape(-1, HD)
    else:
        key = kv_ref[:, :HD]
        value = kv_ref[:, HD:]
    score_scale = 1.0 / math.sqrt(HD)
    contract = (((1,), (1,)), ((), ()))
    for head in range(q_ref.shape[1] // HD):
        query = q_ref[:, head * HD:(head + 1) * HD]
        if exact:
            q_hi, q_lo = _split(query.astype(jnp.float32))
            scores = lax.dot_general(q_hi, key, contract, preferred_element_type=jnp.float32)
            scores = scores + lax.dot_general(q_lo, key, contract, preferred_element_type=jnp.float32)
        else:
            scores = lax.dot_general(query, key, contract, preferred_element_type=jnp.float32)
        masked = scores * score_scale + bias_ref[...]
        row_top = jnp.max(masked, axis=-1, keepdims=True)
        weights = jnp.exp(masked - row_top)
        totals = jnp.sum(weights, axis=-1, keepdims=True)
        acc = jnp.dot(weights.astype(jnp.bfloat16), value, preferred_element_type=jnp.float32)
        o_ref[:, head * HD:(head + 1) * HD] = (acc / totals).astype(o_ref.dtype)


def attend(first_pos, queries, pairs, window, exact, groups=None, offset=0, first=0, count=None):
    rows, qcols = queries.shape
    if groups is None:
        groups = pairs.shape[1] // (2 * HD)
        kv_spec = pl.BlockSpec((pairs.shape[0], 2 * HD), lambda g, pos: (0, first + g))
    else:
        kv_spec = pl.BlockSpec(
            (pairs.shape[0], 2 * rows, HD), lambda g, pos: (0, offset + first + g, 0)
        )
    qblock = qcols // groups
    count = groups - first if count is None else count
    keys = pairs.shape[0] * (rows if pairs.ndim == 3 else 1)
    kernel = functools.partial(_attend_kernel, window=window, exact=exact)
    return pl.pallas_call(
        kernel,
        out_shape=jax.ShapeDtypeStruct((rows, count * qblock), jnp.bfloat16),
        grid_spec=pltpu.PrefetchScalarGridSpec(
            num_scalar_prefetch=1,
            grid=(count,),
            in_specs=[
                pl.BlockSpec((rows, qblock), lambda g, pos: (0, first + g)),
                kv_spec,
            ],
            out_specs=pl.BlockSpec((rows, qblock), lambda g, pos: (0, g)),
            scratch_shapes=[pltpu.VMEM((rows, keys), jnp.float32)],
        ),
    )(first_pos, queries, pairs)


def _project_kernel(att_ref, w_ref, res_ref, o_ref, *, weight_rows):
    for part in range(o_ref.shape[1] // HD):
        weight = w_ref[:, part * weight_rows:(part + 1) * weight_rows, :].reshape(-1, HD)
        acc = jnp.dot(att_ref[...], weight, preferred_element_type=jnp.float32)
        cols = slice(part * HD, (part + 1) * HD)
        o_ref[:, cols] = (res_ref[:, cols].astype(jnp.float32) + acc).astype(o_ref.dtype)


def project(attended, slab, residual, weight_rows):
    rows, width = residual.shape
    blocks = width // HD
    per_step = next(n for n in (4, 3, 2, 1) if blocks % n == 0)
    return pl.pallas_call(
        functools.partial(_project_kernel, weight_rows=weight_rows),
        out_shape=jax.ShapeDtypeStruct((rows, width), jnp.bfloat16),
        grid=(blocks // per_step,),
        in_specs=[
            pl.BlockSpec(attended.shape, lambda c: (0, 0)),
            pl.BlockSpec((slab.shape[0], per_step * weight_rows, HD), lambda c: (0, c, 0)),
            pl.BlockSpec((rows, per_step * HD), lambda c: (0, c)),
        ],
        out_specs=pl.BlockSpec((rows, per_step * HD), lambda c: (0, c)),
    )(attended, slab, residual)


def _half_kernel(sel_ref, *refs, weight_rows, pieces):
    att_refs = refs[:pieces]
    w_refs = refs[pieces:2 * pieces]
    base_refs = refs[2 * pieces:-1]
    o_ref = refs[-1]
    for part in range(o_ref.shape[1] // HD):
        span = slice(part * weight_rows, (part + 1) * weight_rows)
        acc = 0.0
        for att_ref, w_ref in zip(att_refs, w_refs):
            weight = w_ref[:, span, :].reshape(-1, HD)
            acc = acc + jnp.dot(att_ref[...], weight, preferred_element_type=jnp.float32)
        cols = slice(part * HD, (part + 1) * HD)
        for base_ref in base_refs:
            acc = acc + base_ref[:, cols].astype(jnp.float32)
        o_ref[:, cols] = acc.astype(o_ref.dtype)


def project_half(which, attended, slab, bases, weight_rows, out_dtype, width):
    rows = attended[0].shape[0]
    blocks = width // HD
    per_step = next(n for n in (4, 3, 2, 1) if blocks % n == 0)
    devices = attended[0].shape[1] // weight_rows
    count = len(attended)

    def weight_map(i):
        return lambda c, sel: (sel[0] * count + i, c, 0)

    return pl.pallas_call(
        functools.partial(_half_kernel, weight_rows=weight_rows, pieces=count),
        out_shape=jax.ShapeDtypeStruct((rows, width), out_dtype),
        grid_spec=pltpu.PrefetchScalarGridSpec(
            num_scalar_prefetch=1,
            grid=(blocks // per_step,),
            in_specs=[pl.BlockSpec(p.shape, lambda c, sel: (0, 0)) for p in attended]
            + [
                pl.BlockSpec((devices, per_step * weight_rows, HD), weight_map(i))
                for i in range(count)
            ]
            + [pl.BlockSpec((rows, per_step * HD), lambda c, sel: (0, c)) for _ in bases],
            out_specs=pl.BlockSpec((rows, per_step * HD), lambda c, sel: (0, c)),
        ),
    )(which, *attended, *([slab] * count), *bases)


def _pack_kernel(w_ref, kv_ref, o_ref):
    w_rows = w_ref.shape[0]
    kv_rows = kv_ref.shape[0]
    w_blocks = w_ref.shape[1] // HD
    for c in range(w_blocks):
        o_ref[c * w_rows:(c + 1) * w_rows, :] = w_ref[:, c * HD:(c + 1) * HD]
    start = w_blocks * w_rows
    kv_start = o_ref.shape[0] - (kv_ref.shape[1] // HD) * kv_rows
    if kv_start > start:
        o_ref[start:kv_start, :] = jnp.zeros((kv_start - start, HD), o_ref.dtype)
    for c in range(kv_ref.shape[1] // HD):
        o_ref[kv_start + c * kv_rows:kv_start + (c + 1) * kv_rows, :] = kv_ref[:, c * HD:(c + 1) * HD]


def pack(weight, pairs, total_rows):
    return pl.pallas_call(
        _pack_kernel,
        out_shape=jax.ShapeDtypeStruct((total_rows, HD), weight.dtype),
    )(weight, pairs)


def to_slab(x):
    rows, cols = x.shape
    return x.reshape(rows, cols // HD, HD).transpose(1, 0, 2).reshape(-1, HD)


def make_body(heads_count):
    def gather_heads(x):
        if heads_count == 2:
            other = lax.ppermute(x, "heads", [(0, 1), (1, 0)])
            first = lax.axis_index("heads") == 0
            low = jnp.where(first, x, other)
            high = jnp.where(first, other, x)
            return jnp.concatenate([low, high], axis=1)
        return lax.all_gather(x, "heads", axis=1, tiled=True)

    def body(
        residual_in,
        self_queries,
        self_keys_values,
        self_out_weight,
        gain_query,
        gain_keyvalue,
        cross_weight,
    ):
        tok_rows = residual_in.shape[0]
        groups = self_keys_values.shape[1] // (2 * HD)
        seq_place = lax.axis_index("seq")
        first_pos = (seq_place * tok_rows).astype(jnp.int32).reshape(1)

        weight_rows = self_out_weight.shape[0]
        weight_part = to_slab(self_out_weight)
        pad = (-weight_part.shape[0]) % (2 * tok_rows)
        weight_part = jnp.pad(weight_part, ((0, pad), (0, 0)))
        offset = weight_part.shape[0] // (2 * tok_rows)
        packed = pack(
            self_out_weight, self_keys_values, weight_part.shape[0] + self_keys_values.size // HD
        )
        slab = lax.all_gather(packed[None], "seq", axis=0, tiled=True)
        col_layout = cross_weight.reshape(cross_weight.shape[0], groups, QPK + 2, HD)
        weight_kv = col_layout[:, :, QPK:].reshape(cross_weight.shape[0], groups * 2 * HD)
        weight_q = col_layout[:, :, :QPK].reshape(cross_weight.shape[0], groups * QPK * HD)
        if heads_count == 2:
            place = lax.axis_index("heads")
            feats = residual_in.shape[1]
            halves = [place * feats, (1 - place) * feats]
            weight_kv = [lax.dynamic_slice_in_dim(weight_kv, at, feats, 0) for at in halves]
            weight_q = [lax.dynamic_slice_in_dim(weight_q, at, feats, 0) for at in halves]
            gains_kv = [lax.dynamic_slice_in_dim(gain_keyvalue, at, feats, 0) for at in halves]
            gains_q = [lax.dynamic_slice_in_dim(gain_query, at, feats, 0) for at in halves]
        slab, weight_kv, weight_q = lax.optimization_barrier((slab, weight_kv, weight_q))
        if heads_count == 2 and groups % 2 == 0:
            pieces = [
                attend(first_pos, self_queries, slab, WINDOW, False, groups, offset, at, groups // 2)
                for at in (0, groups // 2)
            ]
            first_other = lax.ppermute(pieces[0], "heads", [(0, 1), (1, 0)])
            second, first_other = lax.optimization_barrier((pieces[1], first_other))
            others = [first_other, lax.ppermute(second, "heads", [(0, 1), (1, 0)])]
        else:
            attended = attend(first_pos, self_queries, slab, WINDOW, False, groups, offset)
            pieces = [attended]
        if heads_count == 2:
            place = lax.axis_index("heads")
            if groups % 2 != 0:
                others = [lax.ppermute(attended, "heads", [(0, 1), (1, 0)])]
            width = residual_in.shape[1]
            own_part = project_half(
                place.astype(jnp.int32).reshape(1), pieces, slab,
                [], weight_rows, jnp.float32, width,
            )
            hidden = project_half(
                (1 - place).astype(jnp.int32).reshape(1), others, slab,
                [own_part, residual_in], weight_rows, jnp.bfloat16, width,
            )
        else:
            hidden = project(gather_heads(attended), slab, residual_in, weight_rows)
        if heads_count == 2:
            own = hidden.astype(jnp.float32)
            own_squares = jnp.sum(own * own, axis=-1, keepdims=True)
            other_squares = lax.ppermute(own_squares, "heads", [(0, 1), (1, 0)])
            other = lax.ppermute(hidden, "heads", [(0, 1), (1, 0)]).astype(jnp.float32)
            mean = (own_squares + other_squares) / (2 * own.shape[1])
            inverse = lax.rsqrt(mean + 1e-06)
            shared = jnp.dot(
                (own * inverse * gains_kv[0]).astype(jnp.bfloat16), weight_kv[0],
                preferred_element_type=jnp.float32,
            ) + jnp.dot(
                (other * inverse * gains_kv[1]).astype(jnp.bfloat16), weight_kv[1],
                preferred_element_type=jnp.float32,
            )
            shared_all = lax.all_gather(shared.astype(jnp.bfloat16), "seq", axis=0, tiled=True)
            cross_q = jnp.dot(
                (own * inverse * gains_q[0]).astype(jnp.bfloat16), weight_q[0],
                preferred_element_type=jnp.float32,
            ) + jnp.dot(
                (other * inverse * gains_q[1]).astype(jnp.bfloat16), weight_q[1],
                preferred_element_type=jnp.float32,
            )
        else:
            full_rows = gather_heads(hidden)
            widened = full_rows.astype(jnp.float32)
            inverse = lax.rsqrt(jnp.mean(widened * widened, axis=-1, keepdims=True) + 1e-06)
            normed_q = (widened * inverse * gain_query).astype(jnp.bfloat16)
            normed_kv = (widened * inverse * gain_keyvalue).astype(jnp.bfloat16)
            shared = jnp.dot(normed_kv, weight_kv, preferred_element_type=jnp.float32)
            shared_all = lax.all_gather(shared.astype(jnp.bfloat16), "seq", axis=0, tiled=True)
            cross_q = jnp.dot(normed_q, weight_q, preferred_element_type=jnp.float32)
        cross_attention = attend(first_pos, cross_q, shared_all, None, True)
        return (hidden, cross_attention)

    return body


def solution(mesh):
    return jax.shard_map(
        make_body(mesh.shape["heads"]),
        mesh=mesh,
        in_specs=(
            P("seq", "heads"),
            P("seq", "heads"),
            P("seq", "heads"),
            P("seq", "heads"),
            P(),
            P(),
            P(None, "heads"),
        ),
        out_specs=(P("seq", "heads"), P("seq", "heads")),
        check_vma=False,
    )
```

```python
import functools
import math

import jax
import jax.numpy as jnp
from jax import lax
from jax.experimental import pallas as pl
from jax.experimental.pallas import tpu as pltpu
from jax.sharding import PartitionSpec as P

HD = 128
QPK = 3
WINDOW = 2048


def _split(x):
    high = x.astype(jnp.bfloat16)
    low = (x - high.astype(jnp.float32)).astype(jnp.bfloat16)
    return high, low


def _attend_kernel(pos_ref, q_ref, kv_ref, o_ref, bias_ref, *, window, exact):
    rows, keys = bias_ref.shape

    @pl.when(pl.program_id(0) == 0)
    def _():
        query_pos = pos_ref[0] + lax.broadcasted_iota(jnp.int32, (rows, keys), 0)
        key_pos = lax.broadcasted_iota(jnp.int32, (rows, keys), 1)
        allowed = key_pos <= query_pos
        if window is not None:
            allowed = allowed & (key_pos > query_pos - window)
        bias_ref[...] = jnp.where(allowed, 0.0, -jnp.inf)

    if len(kv_ref.shape) == 3:
        half = kv_ref.shape[1] // 2
        key = kv_ref[:, :half, :].reshape(-1, HD)
        value = kv_ref[:, half:, :].reshape(-1, HD)
    else:
        key = kv_ref[:, :HD]
        value = kv_ref[:, HD:]
    score_scale = 1.0 / math.sqrt(HD)
    contract = (((1,), (1,)), ((), ()))
    for head in range(q_ref.shape[1] // HD):
        query = q_ref[:, head * HD:(head + 1) * HD]
        if exact:
            q_hi, q_lo = _split(query.astype(jnp.float32))
            scores = lax.dot_general(q_hi, key, contract, preferred_element_type=jnp.float32)
            scores = scores + lax.dot_general(q_lo, key, contract, preferred_element_type=jnp.float32)
        else:
            scores = lax.dot_general(query, key, contract, preferred_element_type=jnp.float32)
        masked = scores * score_scale + bias_ref[...]
        row_top = jnp.max(masked, axis=-1, keepdims=True)
        weights = jnp.exp(masked - row_top)
        totals = jnp.sum(weights, axis=-1, keepdims=True)
        acc = jnp.dot(weights.astype(jnp.bfloat16), value, preferred_element_type=jnp.float32)
        o_ref[:, head * HD:(head + 1) * HD] = (acc / totals).astype(o_ref.dtype)


def attend(first_pos, queries, pairs, window, exact, groups=None, offset=0, first=0, count=None):
    rows, qcols = queries.shape
    if groups is None:
        groups = pairs.shape[1] // (2 * HD)
        kv_spec = pl.BlockSpec((pairs.shape[0], 2 * HD), lambda g, pos: (0, first + g))
    else:
        kv_spec = pl.BlockSpec(
            (pairs.shape[0], 2 * rows, HD), lambda g, pos: (0, offset + first + g, 0)
        )
    qblock = qcols // groups
    count = groups - first if count is None else count
    keys = pairs.shape[0] * (rows if pairs.ndim == 3 else 1)
    kernel = functools.partial(_attend_kernel, window=window, exact=exact)
    return pl.pallas_call(
        kernel,
        out_shape=jax.ShapeDtypeStruct((rows, count * qblock), jnp.bfloat16),
        grid_spec=pltpu.PrefetchScalarGridSpec(
            num_scalar_prefetch=1,
            grid=(count,),
            in_specs=[
                pl.BlockSpec((rows, qblock), lambda g, pos: (0, first + g)),
                kv_spec,
            ],
            out_specs=pl.BlockSpec((rows, qblock), lambda g, pos: (0, g)),
            scratch_shapes=[pltpu.VMEM((rows, keys), jnp.float32)],
        ),
    )(first_pos, queries, pairs)


def _project_kernel(att_ref, w_ref, res_ref, o_ref, *, weight_rows):
    for part in range(o_ref.shape[1] // HD):
        weight = w_ref[:, part * weight_rows:(part + 1) * weight_rows, :].reshape(-1, HD)
        acc = jnp.dot(att_ref[...], weight, preferred_element_type=jnp.float32)
        cols = slice(part * HD, (part + 1) * HD)
        o_ref[:, cols] = (res_ref[:, cols].astype(jnp.float32) + acc).astype(o_ref.dtype)


def project(attended, slab, residual, weight_rows):
    rows, width = residual.shape
    blocks = width // HD
    per_step = next(n for n in (6, 4, 3, 2, 1) if blocks % n == 0)
    return pl.pallas_call(
        functools.partial(_project_kernel, weight_rows=weight_rows),
        out_shape=jax.ShapeDtypeStruct((rows, width), jnp.bfloat16),
        grid=(blocks // per_step,),
        in_specs=[
            pl.BlockSpec(attended.shape, lambda c: (0, 0)),
            pl.BlockSpec((slab.shape[0], per_step * weight_rows, HD), lambda c: (0, c, 0)),
            pl.BlockSpec((rows, per_step * HD), lambda c: (0, c)),
        ],
        out_specs=pl.BlockSpec((rows, per_step * HD), lambda c: (0, c)),
    )(attended, slab, residual)


def _half_kernel(sel_ref, *refs, weight_rows, pieces):
    att_refs = refs[:pieces]
    w_refs = refs[pieces:2 * pieces]
    base_refs = refs[2 * pieces:-1]
    o_ref = refs[-1]
    for part in range(o_ref.shape[1] // HD):
        span = slice(part * weight_rows, (part + 1) * weight_rows)
        acc = 0.0
        for att_ref, w_ref in zip(att_refs, w_refs):
            weight = w_ref[:, span, :].reshape(-1, HD)
            acc = acc + jnp.dot(att_ref[...], weight, preferred_element_type=jnp.float32)
        cols = slice(part * HD, (part + 1) * HD)
        for base_ref in base_refs:
            acc = acc + base_ref[:, cols].astype(jnp.float32)
        o_ref[:, cols] = acc.astype(o_ref.dtype)


def project_half(which, attended, slab, bases, weight_rows, out_dtype, width):
    rows = attended[0].shape[0]
    blocks = width // HD
    per_step = next(n for n in (6, 4, 3, 2, 1) if blocks % n == 0)
    devices = attended[0].shape[1] // weight_rows
    count = len(attended)

    def weight_map(i):
        return lambda c, sel: (sel[0] * count + i, c, 0)

    return pl.pallas_call(
        functools.partial(_half_kernel, weight_rows=weight_rows, pieces=count),
        out_shape=jax.ShapeDtypeStruct((rows, width), out_dtype),
        grid_spec=pltpu.PrefetchScalarGridSpec(
            num_scalar_prefetch=1,
            grid=(blocks // per_step,),
            in_specs=[pl.BlockSpec(p.shape, lambda c, sel: (0, 0)) for p in attended]
            + [
                pl.BlockSpec((devices, per_step * weight_rows, HD), weight_map(i))
                for i in range(count)
            ]
            + [pl.BlockSpec((rows, per_step * HD), lambda c, sel: (0, c)) for _ in bases],
            out_specs=pl.BlockSpec((rows, per_step * HD), lambda c, sel: (0, c)),
        ),
    )(which, *attended, *([slab] * count), *bases)


def to_slab(x):
    rows, cols = x.shape
    return x.reshape(rows, cols // HD, HD).transpose(1, 0, 2).reshape(-1, HD)


def make_body(heads_count):
    def gather_heads(x):
        if heads_count == 2:
            other = lax.ppermute(x, "heads", [(0, 1), (1, 0)])
            first = lax.axis_index("heads") == 0
            low = jnp.where(first, x, other)
            high = jnp.where(first, other, x)
            return jnp.concatenate([low, high], axis=1)
        return lax.all_gather(x, "heads", axis=1, tiled=True)

    def body(
        residual_in,
        self_queries,
        self_keys_values,
        self_out_weight,
        gain_query,
        gain_keyvalue,
        cross_weight,
    ):
        tok_rows = residual_in.shape[0]
        groups = self_keys_values.shape[1] // (2 * HD)
        seq_place = lax.axis_index("seq")
        first_pos = (seq_place * tok_rows).astype(jnp.int32).reshape(1)

        weight_rows = self_out_weight.shape[0]
        weight_part = to_slab(self_out_weight)
        pad = (-weight_part.shape[0]) % (2 * tok_rows)
        weight_part = jnp.pad(weight_part, ((0, pad), (0, 0)))
        offset = weight_part.shape[0] // (2 * tok_rows)
        packed = jnp.concatenate([weight_part, to_slab(self_keys_values)], axis=0)
        slab = lax.all_gather(packed[None], "seq", axis=0, tiled=True)
        col_layout = cross_weight.reshape(cross_weight.shape[0], groups, QPK + 2, HD)
        weight_kv = col_layout[:, :, QPK:].reshape(cross_weight.shape[0], groups * 2 * HD)
        weight_q = col_layout[:, :, :QPK].reshape(cross_weight.shape[0], groups * QPK * HD)
        if heads_count == 2:
            place = lax.axis_index("heads")
            feats = residual_in.shape[1]
            halves = [place * feats, (1 - place) * feats]
            weight_kv = [lax.dynamic_slice_in_dim(weight_kv, at, feats, 0) for at in halves]
            weight_q = [lax.dynamic_slice_in_dim(weight_q, at, feats, 0) for at in halves]
            gains_kv = [lax.dynamic_slice_in_dim(gain_keyvalue, at, feats, 0) for at in halves]
            gains_q = [lax.dynamic_slice_in_dim(gain_query, at, feats, 0) for at in halves]
        slab, weight_kv, weight_q = lax.optimization_barrier((slab, weight_kv, weight_q))
        if heads_count == 2 and groups % 2 == 0:
            pieces = [
                attend(first_pos, self_queries, slab, WINDOW, False, groups, offset, at, groups // 2)
                for at in (0, groups // 2)
            ]
            first_other = lax.ppermute(pieces[0], "heads", [(0, 1), (1, 0)])
            second, first_other = lax.optimization_barrier((pieces[1], first_other))
            others = [first_other, lax.ppermute(second, "heads", [(0, 1), (1, 0)])]
        else:
            attended = attend(first_pos, self_queries, slab, WINDOW, False, groups, offset)
            pieces = [attended]
        if heads_count == 2:
            place = lax.axis_index("heads")
            if groups % 2 != 0:
                others = [lax.ppermute(attended, "heads", [(0, 1), (1, 0)])]
            width = residual_in.shape[1]
            own_part = project_half(
                place.astype(jnp.int32).reshape(1), pieces, slab,
                [], weight_rows, jnp.float32, width,
            )
            hidden = project_half(
                (1 - place).astype(jnp.int32).reshape(1), others, slab,
                [own_part, residual_in], weight_rows, jnp.bfloat16, width,
            )
        else:
            hidden = project(gather_heads(attended), slab, residual_in, weight_rows)
        if heads_count == 2:
            own = hidden.astype(jnp.float32)
            own_squares = jnp.sum(own * own, axis=-1, keepdims=True)
            other_squares = lax.ppermute(own_squares, "heads", [(0, 1), (1, 0)])
            other = lax.ppermute(hidden, "heads", [(0, 1), (1, 0)]).astype(jnp.float32)
            mean = (own_squares + other_squares) / (2 * own.shape[1])
            inverse = lax.rsqrt(mean + 1e-06)
            shared = jnp.dot(
                (own * inverse * gains_kv[0]).astype(jnp.bfloat16), weight_kv[0],
                preferred_element_type=jnp.float32,
            ) + jnp.dot(
                (other * inverse * gains_kv[1]).astype(jnp.bfloat16), weight_kv[1],
                preferred_element_type=jnp.float32,
            )
            shared_all = lax.all_gather(shared.astype(jnp.bfloat16), "seq", axis=0, tiled=True)
            cross_q = jnp.dot(
                (own * inverse * gains_q[0]).astype(jnp.bfloat16), weight_q[0],
                preferred_element_type=jnp.float32,
            ) + jnp.dot(
                (other * inverse * gains_q[1]).astype(jnp.bfloat16), weight_q[1],
                preferred_element_type=jnp.float32,
            )
        else:
            full_rows = gather_heads(hidden)
            widened = full_rows.astype(jnp.float32)
            inverse = lax.rsqrt(jnp.mean(widened * widened, axis=-1, keepdims=True) + 1e-06)
            normed_q = (widened * inverse * gain_query).astype(jnp.bfloat16)
            normed_kv = (widened * inverse * gain_keyvalue).astype(jnp.bfloat16)
            shared = jnp.dot(normed_kv, weight_kv, preferred_element_type=jnp.float32)
            shared_all = lax.all_gather(shared.astype(jnp.bfloat16), "seq", axis=0, tiled=True)
            cross_q = jnp.dot(normed_q, weight_q, preferred_element_type=jnp.float32)
        cross_attention = attend(first_pos, cross_q, shared_all, None, True)
        return (hidden, cross_attention)

    return body


def solution(mesh):
    return jax.shard_map(
        make_body(mesh.shape["heads"]),
        mesh=mesh,
        in_specs=(
            P("seq", "heads"),
            P("seq", "heads"),
            P("seq", "heads"),
            P("seq", "heads"),
            P(),
            P(),
            P(None, "heads"),
        ),
        out_specs=(P("seq", "heads"), P("seq", "heads")),
        check_vma=False,
    )
```

```python
import functools
import math

import jax
import jax.numpy as jnp
from jax import lax
from jax.experimental import pallas as pl
from jax.experimental.pallas import tpu as pltpu
from jax.sharding import PartitionSpec as P

HD = 128
QPK = 3
WINDOW = 2048


def _split(x):
    high = x.astype(jnp.bfloat16)
    low = (x - high.astype(jnp.float32)).astype(jnp.bfloat16)
    return high, low


def _attend_kernel(pos_ref, q_ref, kv_ref, o_ref, bias_ref, *, window, exact):
    rows, keys = bias_ref.shape

    @pl.when(pl.program_id(0) == 0)
    def _():
        query_pos = pos_ref[0] + lax.broadcasted_iota(jnp.int32, (rows, keys), 0)
        key_pos = lax.broadcasted_iota(jnp.int32, (rows, keys), 1)
        allowed = key_pos <= query_pos
        if window is not None:
            allowed = allowed & (key_pos > query_pos - window)
        bias_ref[...] = jnp.where(allowed, 0.0, -jnp.inf)

    if len(kv_ref.shape) == 3:
        half = kv_ref.shape[1] // 2
        key = kv_ref[:, :half, :].reshape(-1, HD)
        value = kv_ref[:, half:, :].reshape(-1, HD)
    else:
        key = kv_ref[:, :HD]
        value = kv_ref[:, HD:]
    score_scale = 1.0 / math.sqrt(HD)
    contract = (((1,), (1,)), ((), ()))
    for head in range(q_ref.shape[1] // HD):
        query = q_ref[:, head * HD:(head + 1) * HD]
        if exact:
            q_hi, q_lo = _split(query.astype(jnp.float32))
            scores = lax.dot_general(q_hi, key, contract, preferred_element_type=jnp.float32)
            scores = scores + lax.dot_general(q_lo, key, contract, preferred_element_type=jnp.float32)
        else:
            scores = lax.dot_general(query, key, contract, preferred_element_type=jnp.float32)
        masked = scores * score_scale + bias_ref[...]
        row_top = jnp.max(masked, axis=-1, keepdims=True)
        weights = jnp.exp(masked - row_top)
        totals = jnp.sum(weights, axis=-1, keepdims=True)
        acc = jnp.dot(weights.astype(jnp.bfloat16), value, preferred_element_type=jnp.float32)
        o_ref[:, head * HD:(head + 1) * HD] = (acc / totals).astype(o_ref.dtype)


def attend(first_pos, queries, pairs, window, exact, groups=None, offset=0, first=0, count=None):
    rows, qcols = queries.shape
    if groups is None:
        groups = pairs.shape[1] // (2 * HD)
        kv_spec = pl.BlockSpec((pairs.shape[0], 2 * HD), lambda g, pos: (0, first + g))
    else:
        kv_spec = pl.BlockSpec(
            (pairs.shape[0], 2 * rows, HD), lambda g, pos: (0, offset + first + g, 0)
        )
    qblock = qcols // groups
    count = groups - first if count is None else count
    keys = pairs.shape[0] * (rows if pairs.ndim == 3 else 1)
    kernel = functools.partial(_attend_kernel, window=window, exact=exact)
    return pl.pallas_call(
        kernel,
        out_shape=jax.ShapeDtypeStruct((rows, count * qblock), jnp.bfloat16),
        grid_spec=pltpu.PrefetchScalarGridSpec(
            num_scalar_prefetch=1,
            grid=(count,),
            in_specs=[
                pl.BlockSpec((rows, qblock), lambda g, pos: (0, first + g)),
                kv_spec,
            ],
            out_specs=pl.BlockSpec((rows, qblock), lambda g, pos: (0, g)),
            scratch_shapes=[pltpu.VMEM((rows, keys), jnp.float32)],
        ),
    )(first_pos, queries, pairs)


def _project_kernel(att_ref, w_ref, res_ref, o_ref, *, weight_rows):
    for part in range(o_ref.shape[1] // HD):
        weight = w_ref[:, part * weight_rows:(part + 1) * weight_rows, :].reshape(-1, HD)
        acc = jnp.dot(att_ref[...], weight, preferred_element_type=jnp.float32)
        cols = slice(part * HD, (part + 1) * HD)
        o_ref[:, cols] = (res_ref[:, cols].astype(jnp.float32) + acc).astype(o_ref.dtype)


def project(attended, slab, residual, weight_rows):
    rows, width = residual.shape
    blocks = width // HD
    per_step = next(n for n in (12, 6, 4, 3, 2, 1) if blocks % n == 0)
    return pl.pallas_call(
        functools.partial(_project_kernel, weight_rows=weight_rows),
        out_shape=jax.ShapeDtypeStruct((rows, width), jnp.bfloat16),
        grid=(blocks // per_step,),
        in_specs=[
            pl.BlockSpec(attended.shape, lambda c: (0, 0)),
            pl.BlockSpec((slab.shape[0], per_step * weight_rows, HD), lambda c: (0, c, 0)),
            pl.BlockSpec((rows, per_step * HD), lambda c: (0, c)),
        ],
        out_specs=pl.BlockSpec((rows, per_step * HD), lambda c: (0, c)),
    )(attended, slab, residual)


def _half_kernel(sel_ref, *refs, weight_rows, pieces):
    att_refs = refs[:pieces]
    w_refs = refs[pieces:2 * pieces]
    base_refs = refs[2 * pieces:-1]
    o_ref = refs[-1]
    for part in range(o_ref.shape[1] // HD):
        span = slice(part * weight_rows, (part + 1) * weight_rows)
        acc = 0.0
        for att_ref, w_ref in zip(att_refs, w_refs):
            weight = w_ref[:, span, :].reshape(-1, HD)
            acc = acc + jnp.dot(att_ref[...], weight, preferred_element_type=jnp.float32)
        cols = slice(part * HD, (part + 1) * HD)
        for base_ref in base_refs:
            acc = acc + base_ref[:, cols].astype(jnp.float32)
        o_ref[:, cols] = acc.astype(o_ref.dtype)


def project_half(which, attended, slab, bases, weight_rows, out_dtype, width):
    rows = attended[0].shape[0]
    blocks = width // HD
    per_step = next(n for n in (12, 6, 4, 3, 2, 1) if blocks % n == 0)
    devices = attended[0].shape[1] // weight_rows
    count = len(attended)

    def weight_map(i):
        return lambda c, sel: (sel[0] * count + i, c, 0)

    return pl.pallas_call(
        functools.partial(_half_kernel, weight_rows=weight_rows, pieces=count),
        out_shape=jax.ShapeDtypeStruct((rows, width), out_dtype),
        grid_spec=pltpu.PrefetchScalarGridSpec(
            num_scalar_prefetch=1,
            grid=(blocks // per_step,),
            in_specs=[pl.BlockSpec(p.shape, lambda c, sel: (0, 0)) for p in attended]
            + [
                pl.BlockSpec((devices, per_step * weight_rows, HD), weight_map(i))
                for i in range(count)
            ]
            + [pl.BlockSpec((rows, per_step * HD), lambda c, sel: (0, c)) for _ in bases],
            out_specs=pl.BlockSpec((rows, per_step * HD), lambda c, sel: (0, c)),
        ),
    )(which, *attended, *([slab] * count), *bases)


def to_slab(x):
    rows, cols = x.shape
    return x.reshape(rows, cols // HD, HD).transpose(1, 0, 2).reshape(-1, HD)


def make_body(heads_count):
    def gather_heads(x):
        if heads_count == 2:
            other = lax.ppermute(x, "heads", [(0, 1), (1, 0)])
            first = lax.axis_index("heads") == 0
            low = jnp.where(first, x, other)
            high = jnp.where(first, other, x)
            return jnp.concatenate([low, high], axis=1)
        return lax.all_gather(x, "heads", axis=1, tiled=True)

    def body(
        residual_in,
        self_queries,
        self_keys_values,
        self_out_weight,
        gain_query,
        gain_keyvalue,
        cross_weight,
    ):
        tok_rows = residual_in.shape[0]
        groups = self_keys_values.shape[1] // (2 * HD)
        seq_place = lax.axis_index("seq")
        first_pos = (seq_place * tok_rows).astype(jnp.int32).reshape(1)

        weight_rows = self_out_weight.shape[0]
        weight_part = to_slab(self_out_weight)
        pad = (-weight_part.shape[0]) % (2 * tok_rows)
        weight_part = jnp.pad(weight_part, ((0, pad), (0, 0)))
        offset = weight_part.shape[0] // (2 * tok_rows)
        packed = jnp.concatenate([weight_part, to_slab(self_keys_values)], axis=0)
        slab = lax.all_gather(packed[None], "seq", axis=0, tiled=True)
        col_layout = cross_weight.reshape(cross_weight.shape[0], groups, QPK + 2, HD)
        weight_kv = col_layout[:, :, QPK:].reshape(cross_weight.shape[0], groups * 2 * HD)
        weight_q = col_layout[:, :, :QPK].reshape(cross_weight.shape[0], groups * QPK * HD)
        if heads_count == 2:
            place = lax.axis_index("heads")
            feats = residual_in.shape[1]
            halves = [place * feats, (1 - place) * feats]
            weight_kv = [lax.dynamic_slice_in_dim(weight_kv, at, feats, 0) for at in halves]
            weight_q = [lax.dynamic_slice_in_dim(weight_q, at, feats, 0) for at in halves]
            gains_kv = [lax.dynamic_slice_in_dim(gain_keyvalue, at, feats, 0) for at in halves]
            gains_q = [lax.dynamic_slice_in_dim(gain_query, at, feats, 0) for at in halves]
        slab, weight_kv, weight_q = lax.optimization_barrier((slab, weight_kv, weight_q))
        if heads_count == 2 and groups % 2 == 0:
            pieces = [
                attend(first_pos, self_queries, slab, WINDOW, False, groups, offset, at, groups // 2)
                for at in (0, groups // 2)
            ]
            first_other = lax.ppermute(pieces[0], "heads", [(0, 1), (1, 0)])
            second, first_other = lax.optimization_barrier((pieces[1], first_other))
            others = [first_other, lax.ppermute(second, "heads", [(0, 1), (1, 0)])]
        else:
            attended = attend(first_pos, self_queries, slab, WINDOW, False, groups, offset)
            pieces = [attended]
        if heads_count == 2:
            place = lax.axis_index("heads")
            if groups % 2 != 0:
                others = [lax.ppermute(attended, "heads", [(0, 1), (1, 0)])]
            width = residual_in.shape[1]
            own_part = project_half(
                place.astype(jnp.int32).reshape(1), pieces, slab,
                [], weight_rows, jnp.float32, width,
            )
            hidden = project_half(
                (1 - place).astype(jnp.int32).reshape(1), others, slab,
                [own_part, residual_in], weight_rows, jnp.bfloat16, width,
            )
        else:
            hidden = project(gather_heads(attended), slab, residual_in, weight_rows)
        if heads_count == 2:
            own = hidden.astype(jnp.float32)
            own_squares = jnp.sum(own * own, axis=-1, keepdims=True)
            other_squares = lax.ppermute(own_squares, "heads", [(0, 1), (1, 0)])
            other = lax.ppermute(hidden, "heads", [(0, 1), (1, 0)]).astype(jnp.float32)
            mean = (own_squares + other_squares) / (2 * own.shape[1])
            inverse = lax.rsqrt(mean + 1e-06)
            shared = jnp.dot(
                (own * inverse * gains_kv[0]).astype(jnp.bfloat16), weight_kv[0],
                preferred_element_type=jnp.float32,
            ) + jnp.dot(
                (other * inverse * gains_kv[1]).astype(jnp.bfloat16), weight_kv[1],
                preferred_element_type=jnp.float32,
            )
            shared_all = lax.all_gather(shared.astype(jnp.bfloat16), "seq", axis=0, tiled=True)
            cross_q = jnp.dot(
                (own * inverse * gains_q[0]).astype(jnp.bfloat16), weight_q[0],
                preferred_element_type=jnp.float32,
            ) + jnp.dot(
                (other * inverse * gains_q[1]).astype(jnp.bfloat16), weight_q[1],
                preferred_element_type=jnp.float32,
            )
        else:
            full_rows = gather_heads(hidden)
            widened = full_rows.astype(jnp.float32)
            inverse = lax.rsqrt(jnp.mean(widened * widened, axis=-1, keepdims=True) + 1e-06)
            normed_q = (widened * inverse * gain_query).astype(jnp.bfloat16)
            normed_kv = (widened * inverse * gain_keyvalue).astype(jnp.bfloat16)
            shared = jnp.dot(normed_kv, weight_kv, preferred_element_type=jnp.float32)
            shared_all = lax.all_gather(shared.astype(jnp.bfloat16), "seq", axis=0, tiled=True)
            cross_q = jnp.dot(normed_q, weight_q, preferred_element_type=jnp.float32)
        cross_attention = attend(first_pos, cross_q, shared_all, None, True)
        return (hidden, cross_attention)

    return body


def solution(mesh):
    return jax.shard_map(
        make_body(mesh.shape["heads"]),
        mesh=mesh,
        in_specs=(
            P("seq", "heads"),
            P("seq", "heads"),
            P("seq", "heads"),
            P("seq", "heads"),
            P(),
            P(),
            P(None, "heads"),
        ),
        out_specs=(P("seq", "heads"), P("seq", "heads")),
        check_vma=False,
    )
```
